32 devices in a mesh: dp: 8 (over y, x, core), mp: 4 (over z).
Axes of the slice: x: 2, y: 2, z: 4, core: 2. Of those that a mesh axis runs over, the one named last changes fastest.
Arguments:
- tokens: bfloat16 [16384, 2048], P(('dp', 'mp')), may hold values from -6 to 6
- norm1_gain: float32 [2048], replicated, may hold values from 0.5 to 1.5
- w_query: bfloat16 [2048, 2048], P(None, 'mp'), may hold values from -0.125 to 0.125
- w_key: bfloat16 [2048, 2048], P(None, 'mp'), may hold values from -0.125 to 0.125
- w_value: bfloat16 [2048, 2048], P(None, 'mp'), may hold values from -0.125 to 0.125
- w_out: bfloat16 [2048, 2048], P('mp'), may hold values from -1 to 1
- gate_logit: float32 [16], P('mp'), may hold values from -1.5 to 1.5
- norm2_gain: float32 [2048], replicated, may hold values from 0.5 to 1.5
- w_gate: bfloat16 [2048, 8192], P(None, 'mp'), may hold values from -0.125 to 0.125
- w_up: bfloat16 [2048, 8192], P(None, 'mp'), may hold values from -0.125 to 0.125
- w_down: bfloat16 [8192, 2048], P('mp'), may hold values from -0.0625 to 0.0625
- doc_lengths: int32 [32], replicated, may hold values from 1 to 8192, 15872 in all
- out_grad: bfloat16 [16384, 2048], P(('dp', 'mp')), may hold values from -6 to 6
Outputs:
- output: bfloat16 [16384, 2048], P(('dp', 'mp'))
- input_grad: float32 [16384, 2048], P(('dp', 'mp'))
- grad_norm1_gain: float32 [2048], replicated
- grad_w_query: float32 [2048, 2048], P('dp', 'mp')
- grad_w_key: float32 [2048, 2048], P('dp', 'mp')
- grad_w_value: float32 [2048, 2048], P('dp', 'mp')
- grad_w_out: float32 [2048, 2048], P('mp', 'dp')
- grad_gate_logit: float32 [16], replicated
- grad_norm2_gain: float32 [2048], replicated
- grad_w_gate: float32 [2048, 8192], P('dp', 'mp')
- grad_w_up: float32 [2048, 8192], P('dp', 'mp')
- grad_w_down: float32 [8192, 2048], P('mp', 'dp')
The draws below stay inside these ranges and needn't reach their ends.
Inputs may be any that keep to these rules, and one draw needn't show every extreme that they name: `doc_lengths`: the documents lie one after another from position 0; their lengths sum to 15872, the last 512 positions are padding, and the longest document has exactly 8192 positions.
All inputs are finite; a program needn't handle non-finite values.
Results may differ from the reference program's by a relative error of at most 0.02.
Values may be sent and summed in bfloat16 or wider, within the bound.
No kernel may reach another device: no remote copies, remote signals or barrier semaphores. Data moves between devices by JAX's collectives and lax.ppermute only.
A program may use at most 320 MiB of HBM per device.

```python
import math
import jax
import jax.numpy as jnp
import numpy as np
from jax import lax

D = 2048
HEADS = 16
HEAD_DIM = 128
FF = 8192
SEG = 2048
TOKENS = 16384
NDOCS = 32
PAD = 512
MOST = 8192


def steps_of(rng, dims, split, low, top_value):
    factor_of = 1.0
    for dim, parts in split:
        heights = jax.random.uniform(jax.random.fold_in(jax.random.fold_in(rng, 6), dim), (parts,), jnp.float32, low / len(split), top_value / len(split))
        factor_of = factor_of * jnp.repeat(jnp.exp(heights), dims[dim] // parts).reshape((-1,) + (1,) * (len(dims) - 1 - dim))
    return factor_of


def split_up(count, total, reach, lean):
    portions = [(1 << 20) // math.isqrt(standing ** lean) + 1 for standing in range(2, count + 1)]
    spare, counts = total - reach - (count - 1), [1] * (count - 1)
    while spare > 0:
        free = [i for i in range(count - 1) if counts[i] < reach]
        pool, remaining = sum([portions[i] for i in free]), spare
        for i in free:
            more = min(reach - counts[i], max(1, remaining * portions[i] // pool), spare)
            counts[i] = counts[i] + more
            spare = spare - more
    return np.array([reach] + counts)


def uneven_parts(key, amount, total, most, skew):
    if amount == 2:
        one = jax.random.randint(key, (), max(1, total - most), min(most, total - 1) + 1)
        return jnp.stack([one, total - one])
    sizes = jnp.asarray(split_up(amount, total, most, skew), jnp.int32)
    twos = (amount - 1) // 2
    source_of, taker = sizes[1:1 + 2 * twos:2], sizes[2:2 + 2 * twos:2]
    slack = jnp.minimum(source_of - 1, most - taker)
    shifted = jax.random.randint(jax.random.fold_in(key, 1), (twos,), 0, 1 << 20) % (slack + 1)
    sizes = sizes.at[1:1 + 2 * twos:2].set(source_of - shifted).at[2:2 + 2 * twos:2].set(taker + shifted)
    return sizes[jax.random.permutation(jax.random.fold_in(key, 2), amount)]


def gaussian(rng, dims, scale, most, shards=(), kind=jnp.bfloat16):
    entries = jax.random.normal(rng, dims, jnp.float32) * scale
    if len(shards) > 0:
        entries = steps_of(rng, dims, shards, -0.22, 0.18) * entries
    return jnp.clip(entries, min=-most, max=most).astype(kind)


def setup_inputs(seed: int = 0) -> dict:
    key_list = jax.random.split(jax.random.key(seed), 14)
    return {
        "tokens": gaussian(key_list[0], (TOKENS, D), 1.0, 6.0, ((0, 32),)),
        "norm1_gain": jnp.clip(1.0 + 0.1 * jax.random.normal(key_list[1], (D,), jnp.float32), 0.5, 1.5),
        "w_query": gaussian(key_list[2], (D, HEADS * HEAD_DIM), D ** -0.5, 0.125, ((1, 4),)),
        "w_key": gaussian(key_list[3], (D, HEADS * HEAD_DIM), D ** -0.5, 0.125, ((1, 4),)),
        "w_value": gaussian(key_list[4], (D, HEADS * HEAD_DIM), D ** -0.5, 0.125, ((1, 4),)),
        "w_out": gaussian(key_list[5], (HEADS * HEAD_DIM, D), (max(HEADS * HEAD_DIM // 64, 1)) ** -0.5, 1.0, ((0, 4),)),
        "gate_logit": jnp.clip(jax.random.uniform(key_list[6], (HEADS,), jnp.float32, -1.5, 1.5) * steps_of(key_list[6], (HEADS,), ((0, 4),), -0.4, 0.0), -1.5, 1.5),
        "norm2_gain": jnp.clip(1.0 + 0.1 * jax.random.normal(key_list[7], (D,), jnp.float32), 0.5, 1.5),
        "w_gate": gaussian(key_list[8], (D, FF), D ** -0.5, 0.125, ((1, 4),)),
        "w_up": gaussian(key_list[9], (D, FF), D ** -0.5, 0.125, ((1, 4),)),
        "w_down": gaussian(key_list[10], (FF, D), FF ** -0.5, 0.0625, ((0, 4),)),
        "doc_lengths": uneven_parts(key_list[11], NDOCS, TOKENS - PAD, MOST, 2).astype(jnp.int32),
        "out_grad": gaussian(key_list[12], (TOKENS, D), 1.0, 6.0, ((0, 32),)),
    }


eps_norm = 1e-05
neg_fill = -1e+30
highest = lax.Precision.HIGHEST

@jax.custom_vjp
def low(v):
    return lax.optimization_barrier(v.astype(jnp.bfloat16)).astype(jnp.float32)

@jax.custom_vjp
def low_back(v):
    return v

def low_keep(v):
    return (low(v), None)

def low_pass(kept, grad):
    return (grad,)

def back_keep(v):
    return (v, None)

def back_low(kept, grad):
    return (low(grad),)
low.defvjp(low_keep, low_pass)
low_back.defvjp(back_keep, back_low)

def both_round(values):
    return low(low_back(values))

def inverse_rms(values):
    return lax.rsqrt(lax.optimization_barrier(jnp.mean(values * values, axis=-1, keepdims=True)) + eps_norm)

def feature(values):
    return jnp.where(values > 0, values + 1.0, jnp.exp(jnp.minimum(values, 0.0)))

def document_ids(doc_lengths, first, count):
    bounds = jnp.cumsum(doc_lengths)
    position = first + jnp.arange(count, dtype=jnp.int32)
    before = lax.optimization_barrier(jnp.sum((bounds[None, :] <= position[:, None]).astype(jnp.int32), axis=1))
    return jnp.where(position < bounds[-1], before, doc_lengths.shape[0] + position).astype(jnp.int32)

def layer(tokens_f, gain_one, query_w, key_w, value_w, out_w, gate_logits, gain_two, gate_w, up_w, down_w, doc_index):
    seg_docs = doc_index.reshape(TOKENS // SEG, SEG)
    prev_docs = jnp.concatenate([jnp.full((1,), -1, jnp.int32), seg_docs[:-1, -1]])
    x_segs = tokens_f.reshape(TOKENS // SEG, SEG, D)
    score_scale = 1.0 / math.sqrt(HEAD_DIM)
    positions = jnp.arange(SEG, dtype=jnp.int32)
    causal = positions[None, :] <= positions[:, None]

    def seg_step(state, item):
        memory, norm_sum = state
        x_seg, seg_doc, prev_doc = item
        normed1 = low(x_seg * inverse_rms(x_seg) * gain_one)
        query_rows = both_round(jnp.dot(normed1, query_w, precision=highest)).reshape(SEG, HEADS, HEAD_DIM)
        key_rows = both_round(jnp.dot(normed1, key_w, precision=highest)).reshape(SEG, HEADS, HEAD_DIM)
        value_rows = both_round(jnp.dot(normed1, value_w, precision=highest)).reshape(SEG, HEADS, HEAD_DIM)
        allowed = causal & (seg_doc[None, :] == seg_doc[:, None])
        raw_scores = low_back(jnp.einsum('qhd,khd->hqk', query_rows, key_rows, precision=highest))
        scores = jnp.where(allowed[None], raw_scores * score_scale, neg_fill)
        prob_low = low(jax.nn.softmax(scores, axis=-1))
        dot_out = low_back(jnp.einsum('hqk,khd->qhd', prob_low, value_rows, precision=highest))
        sig_q = feature(query_rows)
        sig_k = feature(key_rows)
        cont_flag = jnp.where(seg_doc[0] == prev_doc, 1.0, 0.0).astype(jnp.float32)
        keep_flag = jnp.where(seg_doc[-1] == prev_doc, 1.0, 0.0).astype(jnp.float32)
        read_mask = jnp.where(seg_doc == seg_doc[0], 1.0, 0.0).astype(jnp.float32)
        write_mask = jnp.where(seg_doc == seg_doc[-1], 1.0, 0.0).astype(jnp.float32)
        read_mem = cont_flag * memory
        read_norm = cont_flag * norm_sum
        numer = jnp.einsum('thd,hde->the', sig_q, read_mem, precision=highest)
        denom = jnp.maximum(jnp.einsum('thd,hd->th', sig_q, read_norm, precision=highest), 1.0)
        mem_out = read_mask[:, None, None] * numer / denom[:, :, None]
        gate = jax.nn.sigmoid(gate_logits)[None, :, None]
        mixed = low((gate * mem_out + (1.0 - gate) * dot_out).reshape(SEG, HEADS * HEAD_DIM))
        attn_sum = low_back(jnp.dot(mixed, out_w, precision=highest))
        resid = x_seg + attn_sum
        normed2 = low(resid * inverse_rms(resid) * gain_two)
        gate_pre = both_round(jnp.dot(normed2, gate_w, precision=highest))
        up_pre = both_round(jnp.dot(normed2, up_w, precision=highest))
        act = low(jax.nn.silu(gate_pre) * up_pre)
        result = resid + jnp.dot(act, down_w, precision=highest)
        new_memory = keep_flag * memory + jnp.einsum('t,thd,the->hde', write_mask, sig_k, value_rows, precision=highest)
        new_norm = keep_flag * norm_sum + jnp.einsum('t,thd->hd', write_mask, sig_k, precision=highest)
        return ((new_memory, new_norm), result)
    start_state = (jnp.zeros((HEADS, HEAD_DIM, HEAD_DIM), jnp.float32), jnp.zeros((HEADS, HEAD_DIM), jnp.float32))
    _, outputs = lax.scan(jax.checkpoint(seg_step), start_state, (x_segs, seg_docs, prev_docs))
    return outputs.reshape(TOKENS, D)

def reference(tokens, norm1_gain, w_query, w_key, w_value, w_out, gate_logit, norm2_gain, w_gate, w_up, w_down, doc_lengths, out_grad):
    doc_index = document_ids(doc_lengths, jnp.int32(0), TOKENS)
    floats = tuple((array.astype(jnp.float32) for array in (tokens, norm1_gain, w_query, w_key, w_value, w_out, gate_logit, norm2_gain, w_gate, w_up, w_down)))

    def forward(*arrays):
        return layer(*arrays, doc_index)
    output, pull_back = jax.vjp(forward, *floats)
    grads = pull_back(out_grad.astype(jnp.float32))
    return (output.astype(jnp.bfloat16), grads[0], grads[1], grads[2], grads[3], grads[4], grads[5], grads[6], grads[7], grads[8], grads[9], grads[10])
```

```python
import functools
import math

import jax
import jax.numpy as jnp
from jax import lax
from jax.experimental import pallas as pl
from jax.experimental.pallas import tpu as pltpu
from jax.sharding import PartitionSpec as P

SEG = 2048


eps_norm = 1e-05
neg_fill = -1e30
highest = lax.Precision.HIGHEST


def carried_in(value, axis, combine, identity):
    size, place = (lax.axis_size(axis), lax.axis_index(axis))
    everything = jax.tree.map(lambda part: lax.all_gather(part, axis), value)
    start = jax.tree.map(
        lambda part, zero: jnp.broadcast_to(jnp.asarray(zero, part.dtype), part.shape),
        value,
        identity,
    )

    def carried_hop(k, before):
        reached = k < place
        new = combine(before, jax.tree.map(lambda part: part[k], everything))
        return jax.tree.map(lambda a, b: jnp.where(reached, a, b), new, before)

    return lax.fori_loop(0, size, carried_hop, start)


def prefix(value, axis, combine, identity):
    size, place = (lax.axis_size(axis), lax.axis_index(axis))
    everything = jax.tree.map(
        lambda part, kind: lax.all_gather(part.astype(kind), axis),
        value,
        jax.tree.map(lambda a: jnp.bfloat16 if a.dtype == jnp.float32 else a.dtype, value),
    )
    start = jax.tree.map(
        lambda part, zero: jnp.broadcast_to(jnp.asarray(zero, part.dtype), part.shape),
        value,
        identity,
    )

    def prefix_hop(k, before):
        at = size - 1 - k
        reached = at > place
        new = combine(
            before, jax.tree.map(lambda part, own: part[at].astype(own.dtype), everything, value)
        )
        return jax.tree.map(lambda a, b: jnp.where(reached, a, b), new, before)

    return lax.fori_loop(0, size, prefix_hop, start)


def inverse_rms(values):
    return lax.rsqrt(jnp.mean(values * values, axis=-1, keepdims=True) + eps_norm)


def norm_backward(values, inverse, gain, upstream):
    scaled = upstream * gain
    inner = jnp.mean(values * scaled, axis=-1, keepdims=True)
    return inverse * scaled - values * inverse * inverse * inverse * inner


def feature(values):
    return jnp.where(values > 0, values + 1.0, jnp.exp(jnp.minimum(values, 0.0)))


def feature_slope(values):
    return jnp.where(values > 0, 1.0, jnp.exp(jnp.minimum(values, 0.0)))


def link_states(earlier, later):
    return (
        earlier[0] * later[0],
        later[0] * earlier[1] + later[1],
        later[0] * earlier[2] + later[2],
    )


def fold_states(state, item):
    return (link_states(state, item), None)


def document_ids(doc_lengths, first, count):
    bounds = jnp.cumsum(doc_lengths)
    position = first + jnp.arange(count, dtype=jnp.int32)
    before = jnp.sum((bounds[None, :] <= position[:, None]).astype(jnp.int32), axis=1)
    return jnp.where(position < bounds[-1], before, doc_lengths.shape[0] + position)


def block_allowed(doc_index, row_start, seg_start, block_rows):
    query_docs = lax.dynamic_slice_in_dim(doc_index, row_start, block_rows, 0)
    query_pos = row_start + jnp.arange(block_rows, dtype=jnp.int32)
    key_pos = seg_start + jnp.arange(SEG, dtype=jnp.int32)
    return (key_pos[None, :] <= query_pos[:, None]) & (doc_index[None, :] == query_docs[:, None])


NEG = -1e30
BQ = 256


def _mask(qi, docq, dock, seg):
    row = (qi * BQ) % seg + lax.broadcasted_iota(jnp.int32, (BQ, seg), 0)
    col = lax.broadcasted_iota(jnp.int32, (BQ, seg), 1)
    return (col <= row) & (docq == dock)


def _fwd_kernel(scale, seg, q_ref, k_ref, v_ref, docq_ref, dock_ref, o_ref, lse_ref):
    qi = pl.program_id(1)
    q = q_ref[0]
    k = k_ref[0]
    v = v_ref[0]
    s = lax.dot_general(q, k, (((1,), (1,)), ((), ())), preferred_element_type=jnp.float32)
    allowed = _mask(qi, docq_ref[...], dock_ref[...], seg)
    s = jnp.where(allowed, s * scale, NEG)
    m = jnp.max(s, axis=1, keepdims=True)
    e = jnp.exp(s - m)
    l = jnp.sum(e, axis=1, keepdims=True)
    p = (e / l).astype(jnp.bfloat16)
    o_ref[0] = jnp.dot(p, v, preferred_element_type=jnp.float32)
    lse_ref[0] = m + jnp.log(l)


def _bwd_kernel(scale, seg, q_ref, k_ref, v_ref, do_ref, lse_ref, docq_ref, dock_ref,
                dq_ref, dk_ref, dv_ref):
    qi = pl.program_id(1)

    @pl.when((qi * BQ) % seg == 0)
    def _():
        dk_ref[...] = jnp.zeros_like(dk_ref)
        dv_ref[...] = jnp.zeros_like(dv_ref)

    q = q_ref[0]
    k = k_ref[0]
    v = v_ref[0]
    do = do_ref[0]
    s = lax.dot_general(q, k, (((1,), (1,)), ((), ())), preferred_element_type=jnp.float32)
    allowed = _mask(qi, docq_ref[...], dock_ref[...], seg)
    s = jnp.where(allowed, s * scale, NEG)
    p = jnp.exp(s - lse_ref[0])
    dp = lax.dot_general(do, v, (((1,), (1,)), ((), ())), preferred_element_type=jnp.float32)
    delta = jnp.sum(p * dp, axis=1, keepdims=True)
    ds = (p * (dp - delta) * scale).astype(jnp.bfloat16)
    dq_ref[0] = jnp.dot(ds, k, preferred_element_type=jnp.float32)
    dk_ref[0] += lax.dot_general(ds, q, (((0,), (0,)), ((), ())), preferred_element_type=jnp.float32)
    dv_ref[0] += lax.dot_general(p.astype(jnp.bfloat16), do, (((0,), (0,)), ((), ())),
                                 preferred_element_type=jnp.float32)


def attention_fwd(q, k, v, doc, scale):
    H, T, d = q.shape
    seg = min(SEG, T)
    nq = T // BQ
    docq = doc.reshape(T, 1)
    dock = doc.reshape(1, T)
    qspec = pl.BlockSpec((1, BQ, d), lambda h, i: (h, i, 0))
    kspec = pl.BlockSpec((1, seg, d), lambda h, i: (h, i * BQ // seg, 0))
    flops = 4 * H * T * seg * d
    return pl.pallas_call(
        functools.partial(_fwd_kernel, scale, seg),
        grid=(H, nq),
        in_specs=[qspec, kspec, kspec,
                  pl.BlockSpec((BQ, 1), lambda h, i: (i, 0)),
                  pl.BlockSpec((1, seg), lambda h, i: (0, i * BQ // seg))],
        out_specs=[pl.BlockSpec((1, BQ, d), lambda h, i: (h, i, 0)),
                   pl.BlockSpec((1, BQ, 1), lambda h, i: (h, i, 0))],
        out_shape=[jax.ShapeDtypeStruct((H, T, d), jnp.float32),
                   jax.ShapeDtypeStruct((H, T, 1), jnp.float32)],
        compiler_params=pltpu.CompilerParams(dimension_semantics=("arbitrary", "arbitrary")),
        cost_estimate=pl.CostEstimate(flops=flops, transcendentals=H * T * seg,
                                      bytes_accessed=H * T * d * 10),
    )(q, k, v, docq, dock)


def attention_bwd(q, k, v, do, lse, doc, scale):
    H, T, d = q.shape
    seg = min(SEG, T)
    nq = T // BQ
    docq = doc.reshape(T, 1)
    dock = doc.reshape(1, T)
    qspec = pl.BlockSpec((1, BQ, d), lambda h, i: (h, i, 0))
    kspec = pl.BlockSpec((1, seg, d), lambda h, i: (h, i * BQ // seg, 0))
    flops = 10 * H * T * seg * d
    return pl.pallas_call(
        functools.partial(_bwd_kernel, scale, seg),
        grid=(H, nq),
        in_specs=[qspec, kspec, kspec, qspec,
                  pl.BlockSpec((1, BQ, 1), lambda h, i: (h, i, 0)),
                  pl.BlockSpec((BQ, 1), lambda h, i: (i, 0)),
                  pl.BlockSpec((1, seg), lambda h, i: (0, i * BQ // seg))],
        out_specs=[qspec, kspec, kspec],
        out_shape=[jax.ShapeDtypeStruct((H, T, d), jnp.float32)] * 3,
        compiler_params=pltpu.CompilerParams(dimension_semantics=("arbitrary", "arbitrary")),
        cost_estimate=pl.CostEstimate(flops=flops, transcendentals=H * T * seg,
                                      bytes_accessed=H * T * d * 24),
    )(q, k, v, do, lse, docq, dock)


def local(
    tokens,
    norm1_gain,
    w_query,
    w_key,
    w_value,
    w_out,
    gate_logit,
    norm2_gain,
    w_gate,
    w_up,
    w_down,
    doc_lengths,
    out_grad,
):
    heads_here = gate_logit.shape[0]
    head_size = w_query.shape[1] // heads_here
    local_rows = tokens.shape[0]
    mp_size = lax.axis_size("mp")
    dp_size = lax.axis_size("dp")
    group_rows = local_rows * mp_size
    seg_count = group_rows // SEG
    score_scale = 1.0 / math.sqrt(head_size)
    group_first = lax.axis_index("dp") * group_rows
    shifted_ids = document_ids(doc_lengths, group_first - 1, group_rows + 1)
    doc_index = shifted_ids[1:]
    before_doc = jnp.where(group_first > 0, shifted_ids[0], -1)
    seg_docs = doc_index.reshape(seg_count, SEG)
    seg_first = seg_docs[:, 0]
    seg_last = seg_docs[:, -1]
    prev_last = jnp.concatenate([before_doc[None], seg_last[:-1]])
    cont_flag = jnp.where(seg_first == prev_last, 1.0, 0.0).astype(jnp.float32)
    keep_flag = jnp.where(seg_last == prev_last, 1.0, 0.0).astype(jnp.float32)
    read_mask = jnp.where(seg_docs == seg_first[:, None], 1.0, 0.0).astype(jnp.float32)
    write_mask = jnp.where(seg_docs == seg_last[:, None], 1.0, 0.0).astype(jnp.float32)
    width = w_out.shape[1]

    def to_heads(rows):
        return rows.reshape(group_rows, heads_here, head_size).transpose(1, 0, 2)

    def from_heads(heads):
        return heads.transpose(1, 0, 2).reshape(group_rows, heads_here * head_size)

    seg_shape = (heads_here, seg_count, SEG, head_size)
    piece = width // dp_size
    w_out_piece = lax.dynamic_slice_in_dim(w_out, lax.axis_index("dp") * piece, piece, axis=1)
    w_out_full = lax.all_gather(
        lax.all_gather(w_out_piece, "mp", axis=0, tiled=True), "dp", axis=1, tiled=True
    )
    x_rows = tokens.astype(jnp.float32)
    inverse1 = inverse_rms(x_rows)
    normed1 = (x_rows * inverse1 * norm1_gain).astype(jnp.bfloat16)
    normed1_all = lax.all_gather(normed1, "mp", axis=0, tiled=True)
    query_h = to_heads(
        jnp.dot(normed1_all, w_query, preferred_element_type=jnp.float32).astype(jnp.bfloat16)
    )
    key_h = to_heads(
        jnp.dot(normed1_all, w_key, preferred_element_type=jnp.float32).astype(jnp.bfloat16)
    )
    value_h = to_heads(
        jnp.dot(normed1_all, w_value, preferred_element_type=jnp.float32).astype(jnp.bfloat16)
    )
    dot_out, log_sums = attention_fwd(query_h, key_h, value_h, doc_index, score_scale)
    query_f = query_h.astype(jnp.float32).reshape(seg_shape)
    key_f = key_h.astype(jnp.float32).reshape(seg_shape)
    value_f = value_h.astype(jnp.float32).reshape(seg_shape)
    sig_q = feature(query_f)
    sig_k = feature(key_f)
    updates = jnp.einsum("st,hstd,hste->shde", write_mask, sig_k, value_f, precision=highest)
    norm_updates = jnp.einsum("st,hstd->shd", write_mask, sig_k, precision=highest)
    start_state = (
        jnp.ones((1,), jnp.float32),
        jnp.zeros(updates.shape[1:], jnp.float32),
        jnp.zeros(norm_updates.shape[1:], jnp.float32),
    )
    summary, _ = lax.scan(fold_states, start_state, (keep_flag[:, None], updates, norm_updates))
    _, memory_in, norm_in = carried_in(summary, "dp", link_states, start_state)

    def carry_forward(state, item):
        flag, read_flag, update, norm_update = item
        memory, norm_sum = state
        return (
            (flag * memory + update, flag * norm_sum + norm_update),
            (read_flag * memory, read_flag * norm_sum),
        )

    _, (read_mem, read_norm) = lax.scan(
        carry_forward, (memory_in, norm_in), (keep_flag, cont_flag, updates, norm_updates)
    )
    numer = jnp.einsum("hstd,shde->hste", sig_q, read_mem, precision=highest)
    denom_raw = jnp.einsum("hstd,shd->hst", sig_q, read_norm, precision=highest)
    denom = jnp.maximum(denom_raw, 1.0)
    mem_out = (read_mask[None, :, :, None] * numer / denom[..., None]).reshape(dot_out.shape)
    gate_vec = jax.nn.sigmoid(gate_logit)
    gate = gate_vec[:, None, None]
    mixed_cols = from_heads(gate * mem_out + (1.0 - gate) * dot_out).astype(jnp.bfloat16)
    mixed = lax.all_to_all(mixed_cols, "mp", 0, 1, tiled=True)
    attn_sum = jnp.dot(mixed, w_out_full, preferred_element_type=jnp.float32)
    resid = x_rows + attn_sum
    inverse2 = inverse_rms(resid)
    normed2 = (resid * inverse2 * norm2_gain).astype(jnp.bfloat16)
    normed2_all = lax.all_gather(normed2, "mp", axis=0, tiled=True)
    gate_pre = jnp.dot(normed2_all, w_gate, preferred_element_type=jnp.float32).astype(jnp.bfloat16)
    up_pre = jnp.dot(normed2_all, w_up, preferred_element_type=jnp.float32).astype(jnp.bfloat16)
    gate_f = gate_pre.astype(jnp.float32)
    up_f = up_pre.astype(jnp.float32)
    sig_gate = jax.nn.sigmoid(gate_f)
    act = (gate_f * sig_gate * up_f).astype(jnp.bfloat16)
    mlp_sum = lax.psum_scatter(
        jnp.dot(act, w_down, preferred_element_type=jnp.float32).astype(jnp.bfloat16),
        "mp",
        scatter_dimension=0,
        tiled=True,
    ).astype(jnp.float32)
    output = (resid + mlp_sum).astype(jnp.bfloat16)
    grad_rows_all = lax.all_gather(out_grad, "mp", axis=0, tiled=True)
    d_act = jnp.dot(grad_rows_all, w_down.T, preferred_element_type=jnp.float32)
    grad_down = jnp.dot(act.T, grad_rows_all, preferred_element_type=jnp.float32)
    d_gate = (d_act * up_f * sig_gate * (1.0 + gate_f * (1.0 - sig_gate))).astype(jnp.bfloat16)
    d_up = (d_act * gate_f * sig_gate).astype(jnp.bfloat16)
    grad_gate = jnp.dot(normed2_all.T, d_gate, preferred_element_type=jnp.float32)
    grad_up = jnp.dot(normed2_all.T, d_up, preferred_element_type=jnp.float32)
    d_norm2 = lax.psum_scatter(
        (
            jnp.dot(d_gate, w_gate.T, preferred_element_type=jnp.float32)
            + jnp.dot(d_up, w_up.T, preferred_element_type=jnp.float32)
        ).astype(jnp.bfloat16),
        "mp",
        scatter_dimension=0,
        tiled=True,
    ).astype(jnp.float32)
    gain2_part = jnp.sum(d_norm2 * resid * inverse2, axis=0)
    d_resid = out_grad.astype(jnp.float32) + norm_backward(resid, inverse2, norm2_gain, d_norm2)
    d_resid_low = d_resid.astype(jnp.bfloat16)
    grad_out = jnp.dot(mixed.T, d_resid_low, preferred_element_type=jnp.float32)
    d_mixed_rows = jnp.dot(d_resid_low, w_out_full.T, preferred_element_type=jnp.float32)
    d_mixed = to_heads(
        lax.all_to_all(d_mixed_rows.astype(jnp.bfloat16), "mp", 1, 0, tiled=True)
    ).astype(jnp.float32)
    gate_part = jnp.sum(d_mixed * (mem_out - dot_out), axis=(1, 2)) * gate_vec * (1.0 - gate_vec)
    d_dot = ((1.0 - gate) * d_mixed).astype(jnp.bfloat16)
    d_mem = (gate * d_mixed).reshape(seg_shape)
    dq_dot, dk_dot, dv_dot = attention_bwd(
        query_h, key_h, value_h, d_dot, log_sums, doc_index, score_scale
    )
    d_numer = read_mask[None, :, :, None] * d_mem / denom[..., None]
    d_denom = -jnp.sum(d_numer * numer, axis=-1) / denom * jnp.where(denom_raw > 1.0, 1.0, 0.0)
    d_sig_q = (
        jnp.einsum("hste,shde->hstd", d_numer, read_mem, precision=highest)
        + d_denom[..., None] * read_norm.transpose(1, 0, 2)[:, :, None]
    )
    d_read_mem = jnp.einsum("hstd,hste->shde", sig_q, d_numer, precision=highest)
    d_read_norm = jnp.einsum("hst,hstd->shd", d_denom, sig_q, precision=highest)
    back_mem = cont_flag[:, None, None, None] * d_read_mem
    back_norm = cont_flag[:, None, None] * d_read_norm
    back_summary, _ = lax.scan(
        fold_states, start_state, (keep_flag[:, None], back_mem, back_norm), reverse=True
    )
    _, grad_in, grad_norm_in = prefix(back_summary, "dp", link_states, start_state)

    def carry_back(state, item):
        flag, mem_read, norm_read = item
        grad_memory, grad_norm = state
        return (
            (flag * grad_memory + mem_read, flag * grad_norm + norm_read),
            (grad_memory, grad_norm),
        )

    _, (d_carried, d_carried_norm) = lax.scan(
        carry_back, (grad_in, grad_norm_in), (keep_flag, back_mem, back_norm), reverse=True
    )
    write4 = write_mask[None, :, :, None]
    d_sig_k = write4 * (
        jnp.einsum("hste,shde->hstd", value_f, d_carried, precision=highest)
        + d_carried_norm.transpose(1, 0, 2)[:, :, None]
    )
    d_val_mem = write4 * jnp.einsum("hstd,shde->hste", sig_k, d_carried, precision=highest)
    d_query = from_heads(
        dq_dot + (d_sig_q * feature_slope(query_f)).reshape(dq_dot.shape)
    ).astype(jnp.bfloat16)
    d_key = from_heads(
        dk_dot + (d_sig_k * feature_slope(key_f)).reshape(dk_dot.shape)
    ).astype(jnp.bfloat16)
    d_value = from_heads(dv_dot + d_val_mem.reshape(dv_dot.shape)).astype(jnp.bfloat16)
    grad_query = jnp.dot(normed1_all.T, d_query, preferred_element_type=jnp.float32)
    grad_key = jnp.dot(normed1_all.T, d_key, preferred_element_type=jnp.float32)
    grad_value = jnp.dot(normed1_all.T, d_value, preferred_element_type=jnp.float32)
    total_term = jnp.dot(d_query, w_query.T, preferred_element_type=jnp.float32)
    total_term = total_term + jnp.dot(d_key, w_key.T, preferred_element_type=jnp.float32)
    d_norm1 = lax.psum_scatter(
        (total_term + jnp.dot(d_value, w_value.T, preferred_element_type=jnp.float32)).astype(
            jnp.bfloat16
        ),
        "mp",
        scatter_dimension=0,
        tiled=True,
    ).astype(jnp.float32)
    gain1_part = jnp.sum(d_norm1 * x_rows * inverse1, axis=0)
    input_grad = d_resid + norm_backward(x_rows, inverse1, norm1_gain, d_norm1)
    gate_full = lax.dynamic_update_slice_in_dim(
        jnp.zeros((heads_here * mp_size,), jnp.float32),
        gate_part,
        lax.axis_index("mp") * heads_here,
        0,
    )
    gain1_sum, gain2_sum, gate_sum = lax.psum((gain1_part, gain2_part, gate_full), ("dp", "mp"))

    def over_dp(grad, dim):
        return lax.psum_scatter(
            grad.astype(jnp.bfloat16), "dp", scatter_dimension=dim, tiled=True
        ).astype(jnp.float32)

    out_sum = lax.psum_scatter(
        over_dp(grad_out, 1).astype(jnp.bfloat16), "mp", scatter_dimension=0, tiled=True
    ).astype(jnp.float32)
    query_sum, key_sum, value_sum, gate_w_sum, up_sum, down_sum = (
        over_dp(grad_query, 0),
        over_dp(grad_key, 0),
        over_dp(grad_value, 0),
        over_dp(grad_gate, 0),
        over_dp(grad_up, 0),
        over_dp(grad_down, 1),
    )
    return (
        output,
        input_grad,
        gain1_sum,
        query_sum,
        key_sum,
        value_sum,
        out_sum,
        gate_sum,
        gain2_sum,
        gate_w_sum,
        up_sum,
        down_sum,
    )


def solution(mesh):
    return jax.shard_map(
        local,
        mesh=mesh,
        in_specs=(
            P(("dp", "mp"), None),
            P(),
            P(None, "mp"),
            P(None, "mp"),
            P(None, "mp"),
            P("mp", None),
            P("mp"),
            P(),
            P(None, "mp"),
            P(None, "mp"),
            P("mp", None),
            P(),
            P(("dp", "mp"), None),
        ),
        out_specs=(
            P(("dp", "mp"), None),
            P(("dp", "mp"), None),
            P(),
            P("dp", "mp"),
            P("dp", "mp"),
            P("dp", "mp"),
            P("mp", "dp"),
            P(),
            P(),
            P("dp", "mp"),
            P("dp", "mp"),
            P("mp", "dp"),
        ),
        check_vma=False,
    )
```

```python
import functools
import math

import jax
import jax.numpy as jnp
from jax import lax
from jax.experimental import pallas as pl
from jax.experimental.pallas import tpu as pltpu
from jax.sharding import PartitionSpec as P

SEG = 2048


eps_norm = 1e-05
neg_fill = -1e30
highest = lax.Precision.HIGHEST


def carried_in(value, axis, combine, identity):
    size, place = (lax.axis_size(axis), lax.axis_index(axis))
    everything = jax.tree.map(lambda part: lax.all_gather(part, axis), value)
    start = jax.tree.map(
        lambda part, zero: jnp.broadcast_to(jnp.asarray(zero, part.dtype), part.shape),
        value,
        identity,
    )

    def carried_hop(k, before):
        reached = k < place
        new = combine(before, jax.tree.map(lambda part: part[k], everything))
        return jax.tree.map(lambda a, b: jnp.where(reached, a, b), new, before)

    return lax.fori_loop(0, size, carried_hop, start)


def prefix(value, axis, combine, identity):
    size, place = (lax.axis_size(axis), lax.axis_index(axis))
    everything = jax.tree.map(
        lambda part, kind: lax.all_gather(part.astype(kind), axis),
        value,
        jax.tree.map(lambda a: jnp.bfloat16 if a.dtype == jnp.float32 else a.dtype, value),
    )
    start = jax.tree.map(
        lambda part, zero: jnp.broadcast_to(jnp.asarray(zero, part.dtype), part.shape),
        value,
        identity,
    )

    def prefix_hop(k, before):
        at = size - 1 - k
        reached = at > place
        new = combine(
            before, jax.tree.map(lambda part, own: part[at].astype(own.dtype), everything, value)
        )
        return jax.tree.map(lambda a, b: jnp.where(reached, a, b), new, before)

    return lax.fori_loop(0, size, prefix_hop, start)


def ring_pairs(n, step):
    return [(j, (j + step) % n) for j in range(n)]


def ring_gather(rows, axis, compute):
    n, place = lax.axis_size(axis), lax.axis_index(axis)
    count = rows.shape[0]
    half = count // 2
    own = compute(rows)
    outs = [
        lax.dynamic_update_slice_in_dim(
            jnp.zeros((n * count,) + part.shape[1:], part.dtype), part, place * count, 0
        )
        for part in own
    ]
    ahead, behind = rows[:half], rows[half:]
    for step in range(1, n):
        ahead = lax.ppermute(ahead, axis, ring_pairs(n, 1))
        behind = lax.ppermute(behind, axis, ring_pairs(n, -1))
        for got, start in (
            (compute(ahead), ((place - step) % n) * count),
            (compute(behind), ((place + step) % n) * count + half),
        ):
            outs = [
                lax.dynamic_update_slice_in_dim(out, part, start, 0)
                for out, part in zip(outs, got)
            ]
    return outs


def ring_scatter(partial, axis, kind=jnp.bfloat16):
    n, place = lax.axis_size(axis), lax.axis_index(axis)
    count = partial.shape[0] // n
    half = count // 2

    def chunk(owner, start):
        return lax.dynamic_slice_in_dim(partial, owner * count + start, half, 0).astype(jnp.float32)

    ahead = chunk((place - 1) % n, 0)
    behind = chunk((place + 1) % n, half)
    for step in range(1, n):
        ahead = lax.ppermute(ahead.astype(kind), axis, ring_pairs(n, 1)).astype(jnp.float32)
        ahead = ahead + chunk((place - 1 - step) % n, 0)
        behind = lax.ppermute(behind.astype(kind), axis, ring_pairs(n, -1)).astype(jnp.float32)
        behind = behind + chunk((place + 1 + step) % n, half)
    return jnp.concatenate([ahead, behind], axis=0)


def inverse_rms(values):
    return lax.rsqrt(jnp.mean(values * values, axis=-1, keepdims=True) + eps_norm)


def norm_backward(values, inverse, gain, upstream):
    scaled = upstream * gain
    inner = jnp.mean(values * scaled, axis=-1, keepdims=True)
    return inverse * scaled - values * inverse * inverse * inverse * inner


def feature(values):
    return jnp.where(values > 0, values + 1.0, jnp.exp(jnp.minimum(values, 0.0)))


def feature_slope(values):
    return jnp.where(values > 0, 1.0, jnp.exp(jnp.minimum(values, 0.0)))


def link_states(earlier, later):
    return (
        earlier[0] * later[0],
        later[0] * earlier[1] + later[1],
        later[0] * earlier[2] + later[2],
    )


def fold_states(state, item):
    return (link_states(state, item), None)


def document_ids(doc_lengths, first, count):
    bounds = jnp.cumsum(doc_lengths)
    position = first + jnp.arange(count, dtype=jnp.int32)
    before = jnp.sum((bounds[None, :] <= position[:, None]).astype(jnp.int32), axis=1)
    return jnp.where(position < bounds[-1], before, doc_lengths.shape[0] + position)


def block_allowed(doc_index, row_start, seg_start, block_rows):
    query_docs = lax.dynamic_slice_in_dim(doc_index, row_start, block_rows, 0)
    query_pos = row_start + jnp.arange(block_rows, dtype=jnp.int32)
    key_pos = seg_start + jnp.arange(SEG, dtype=jnp.int32)
    return (key_pos[None, :] <= query_pos[:, None]) & (doc_index[None, :] == query_docs[:, None])


NEG = -1e30
BQ = 256


def _mask(qi, docq, dock, seg):
    row = (qi * BQ) % seg + lax.broadcasted_iota(jnp.int32, (BQ, seg), 0)
    col = lax.broadcasted_iota(jnp.int32, (BQ, seg), 1)
    return (col <= row) & (docq == dock)


def _fwd_kernel(scale, seg, q_ref, k_ref, v_ref, docq_ref, dock_ref, o_ref, lse_ref):
    qi = pl.program_id(1)
    q = q_ref[0]
    k = k_ref[0]
    v = v_ref[0]
    s = lax.dot_general(q, k, (((1,), (1,)), ((), ())), preferred_element_type=jnp.float32)
    allowed = _mask(qi, docq_ref[...], dock_ref[...], seg)
    s = jnp.where(allowed, s * scale, NEG)
    m = jnp.max(s, axis=1, keepdims=True)
    e = jnp.exp(s - m)
    l = jnp.sum(e, axis=1, keepdims=True)
    p = (e / l).astype(jnp.bfloat16)
    o_ref[0] = jnp.dot(p, v, preferred_element_type=jnp.float32)
    lse_ref[0] = m + jnp.log(l)


def _bwd_kernel(scale, seg, q_ref, k_ref, v_ref, do_ref, lse_ref, docq_ref, dock_ref,
                dq_ref, dk_ref, dv_ref):
    qi = pl.program_id(1)

    @pl.when((qi * BQ) % seg == 0)
    def _():
        dk_ref[...] = jnp.zeros_like(dk_ref)
        dv_ref[...] = jnp.zeros_like(dv_ref)

    q = q_ref[0]
    k = k_ref[0]
    v = v_ref[0]
    do = do_ref[0]
    s = lax.dot_general(q, k, (((1,), (1,)), ((), ())), preferred_element_type=jnp.float32)
    allowed = _mask(qi, docq_ref[...], dock_ref[...], seg)
    s = jnp.where(allowed, s * scale, NEG)
    p = jnp.exp(s - lse_ref[0])
    dp = lax.dot_general(do, v, (((1,), (1,)), ((), ())), preferred_element_type=jnp.float32)
    delta = jnp.sum(p * dp, axis=1, keepdims=True)
    ds = (p * (dp - delta) * scale).astype(jnp.bfloat16)
    dq_ref[0] = jnp.dot(ds, k, preferred_element_type=jnp.float32)
    dk_ref[0] += lax.dot_general(ds, q, (((0,), (0,)), ((), ())), preferred_element_type=jnp.float32)
    dv_ref[0] += lax.dot_general(p.astype(jnp.bfloat16), do, (((0,), (0,)), ((), ())),
                                 preferred_element_type=jnp.float32)


def attention_fwd(q, k, v, doc, scale):
    H, T, d = q.shape
    seg = min(SEG, T)
    nq = T // BQ
    docq = doc.reshape(T, 1)
    dock = doc.reshape(1, T)
    qspec = pl.BlockSpec((1, BQ, d), lambda h, i: (h, i, 0))
    kspec = pl.BlockSpec((1, seg, d), lambda h, i: (h, i * BQ // seg, 0))
    flops = 4 * H * T * seg * d
    return pl.pallas_call(
        functools.partial(_fwd_kernel, scale, seg),
        grid=(H, nq),
        in_specs=[qspec, kspec, kspec,
                  pl.BlockSpec((BQ, 1), lambda h, i: (i, 0)),
                  pl.BlockSpec((1, seg), lambda h, i: (0, i * BQ // seg))],
        out_specs=[pl.BlockSpec((1, BQ, d), lambda h, i: (h, i, 0)),
                   pl.BlockSpec((1, BQ, 1), lambda h, i: (h, i, 0))],
        out_shape=[jax.ShapeDtypeStruct((H, T, d), jnp.float32),
                   jax.ShapeDtypeStruct((H, T, 1), jnp.float32)],
        compiler_params=pltpu.CompilerParams(dimension_semantics=("arbitrary", "arbitrary")),
        cost_estimate=pl.CostEstimate(flops=flops, transcendentals=H * T * seg,
                                      bytes_accessed=H * T * d * 10),
    )(q, k, v, docq, dock)


def attention_bwd(q, k, v, do, lse, doc, scale):
    H, T, d = q.shape
    seg = min(SEG, T)
    nq = T // BQ
    docq = doc.reshape(T, 1)
    dock = doc.reshape(1, T)
    qspec = pl.BlockSpec((1, BQ, d), lambda h, i: (h, i, 0))
    kspec = pl.BlockSpec((1, seg, d), lambda h, i: (h, i * BQ // seg, 0))
    flops = 10 * H * T * seg * d
    return pl.pallas_call(
        functools.partial(_bwd_kernel, scale, seg),
        grid=(H, nq),
        in_specs=[qspec, kspec, kspec, qspec,
                  pl.BlockSpec((1, BQ, 1), lambda h, i: (h, i, 0)),
                  pl.BlockSpec((BQ, 1), lambda h, i: (i, 0)),
                  pl.BlockSpec((1, seg), lambda h, i: (0, i * BQ // seg))],
        out_specs=[qspec, kspec, kspec],
        out_shape=[jax.ShapeDtypeStruct((H, T, d), jnp.float32)] * 3,
        compiler_params=pltpu.CompilerParams(dimension_semantics=("arbitrary", "arbitrary")),
        cost_estimate=pl.CostEstimate(flops=flops, transcendentals=H * T * seg,
                                      bytes_accessed=H * T * d * 24),
    )(q, k, v, do, lse, docq, dock)


def local(
    tokens,
    norm1_gain,
    w_query,
    w_key,
    w_value,
    w_out,
    gate_logit,
    norm2_gain,
    w_gate,
    w_up,
    w_down,
    doc_lengths,
    out_grad,
):
    heads_here = gate_logit.shape[0]
    head_size = w_query.shape[1] // heads_here
    local_rows = tokens.shape[0]
    mp_size = lax.axis_size("mp")
    dp_size = lax.axis_size("dp")
    group_rows = local_rows * mp_size
    seg_count = group_rows // SEG
    score_scale = 1.0 / math.sqrt(head_size)
    group_first = lax.axis_index("dp") * group_rows
    shifted_ids = document_ids(doc_lengths, group_first - 1, group_rows + 1)
    doc_index = shifted_ids[1:]
    before_doc = jnp.where(group_first > 0, shifted_ids[0], -1)
    seg_docs = doc_index.reshape(seg_count, SEG)
    seg_first = seg_docs[:, 0]
    seg_last = seg_docs[:, -1]
    prev_last = jnp.concatenate([before_doc[None], seg_last[:-1]])
    cont_flag = jnp.where(seg_first == prev_last, 1.0, 0.0).astype(jnp.float32)
    keep_flag = jnp.where(seg_last == prev_last, 1.0, 0.0).astype(jnp.float32)
    read_mask = jnp.where(seg_docs == seg_first[:, None], 1.0, 0.0).astype(jnp.float32)
    write_mask = jnp.where(seg_docs == seg_last[:, None], 1.0, 0.0).astype(jnp.float32)
    width = w_out.shape[1]

    def to_heads(rows):
        return rows.reshape(group_rows, heads_here, head_size).transpose(1, 0, 2)

    def from_heads(heads):
        return heads.transpose(1, 0, 2).reshape(group_rows, heads_here * head_size)

    seg_shape = (heads_here, seg_count, SEG, head_size)
    piece = width // dp_size
    w_out_piece = lax.dynamic_slice_in_dim(w_out, lax.axis_index("dp") * piece, piece, axis=1)
    w_out_full = lax.all_gather(
        lax.all_gather(w_out_piece, "mp", axis=0, tiled=True), "dp", axis=1, tiled=True
    )
    x_rows = tokens.astype(jnp.float32)
    inverse1 = inverse_rms(x_rows)
    normed1 = (x_rows * inverse1 * norm1_gain).astype(jnp.bfloat16)
    def project_qkv(rows):
        return (rows,) + tuple(
            jnp.dot(rows, weight, preferred_element_type=jnp.float32).astype(jnp.bfloat16)
            for weight in (w_query, w_key, w_value)
        )

    normed1_all, query_rows, key_rows, value_rows = ring_gather(normed1, "mp", project_qkv)
    query_h, key_h, value_h = (to_heads(a) for a in (query_rows, key_rows, value_rows))
    dot_out, log_sums = attention_fwd(query_h, key_h, value_h, doc_index, score_scale)
    query_f = query_h.astype(jnp.float32).reshape(seg_shape)
    key_f = key_h.astype(jnp.float32).reshape(seg_shape)
    value_f = value_h.astype(jnp.float32).reshape(seg_shape)
    sig_q = feature(query_f)
    sig_k = feature(key_f)
    updates = jnp.einsum("st,hstd,hste->shde", write_mask, sig_k, value_f, precision=highest)
    norm_updates = jnp.einsum("st,hstd->shd", write_mask, sig_k, precision=highest)
    start_state = (
        jnp.ones((1,), jnp.float32),
        jnp.zeros(updates.shape[1:], jnp.float32),
        jnp.zeros(norm_updates.shape[1:], jnp.float32),
    )
    summary, _ = lax.scan(fold_states, start_state, (keep_flag[:, None], updates, norm_updates))
    _, memory_in, norm_in = carried_in(summary, "dp", link_states, start_state)

    def carry_forward(state, item):
        flag, read_flag, update, norm_update = item
        memory, norm_sum = state
        return (
            (flag * memory + update, flag * norm_sum + norm_update),
            (read_flag * memory, read_flag * norm_sum),
        )

    _, (read_mem, read_norm) = lax.scan(
        carry_forward, (memory_in, norm_in), (keep_flag, cont_flag, updates, norm_updates)
    )
    numer = jnp.einsum("hstd,shde->hste", sig_q, read_mem, precision=highest)
    denom_raw = jnp.einsum("hstd,shd->hst", sig_q, read_norm, precision=highest)
    denom = jnp.maximum(denom_raw, 1.0)
    mem_out = (read_mask[None, :, :, None] * numer / denom[..., None]).reshape(dot_out.shape)
    gate_vec = jax.nn.sigmoid(gate_logit)
    gate = gate_vec[:, None, None]
    mixed_cols = from_heads(gate * mem_out + (1.0 - gate) * dot_out).astype(jnp.bfloat16)
    mixed = lax.all_to_all(mixed_cols, "mp", 0, 1, tiled=True)
    attn_sum = jnp.dot(mixed, w_out_full, preferred_element_type=jnp.float32)
    resid = x_rows + attn_sum
    inverse2 = inverse_rms(resid)
    normed2 = (resid * inverse2 * norm2_gain).astype(jnp.bfloat16)
    def project_ffn(rows):
        return (rows,) + tuple(
            jnp.dot(rows, weight, preferred_element_type=jnp.float32).astype(jnp.bfloat16)
            for weight in (w_gate, w_up)
        )

    normed2_all, gate_pre, up_pre = ring_gather(normed2, "mp", project_ffn)
    gate_f = gate_pre.astype(jnp.float32)
    up_f = up_pre.astype(jnp.float32)
    sig_gate = jax.nn.sigmoid(gate_f)
    act = (gate_f * sig_gate * up_f).astype(jnp.bfloat16)
    mlp_sum = ring_scatter(jnp.dot(act, w_down, preferred_element_type=jnp.float32), "mp")
    output = (resid + mlp_sum).astype(jnp.bfloat16)
    (grad_rows_all,) = ring_gather(out_grad, "mp", lambda rows: (rows,))
    d_act = jnp.dot(grad_rows_all, w_down.T, preferred_element_type=jnp.float32)
    grad_down = jnp.dot(act.T, grad_rows_all, preferred_element_type=jnp.float32)
    d_gate = (d_act * up_f * sig_gate * (1.0 + gate_f * (1.0 - sig_gate))).astype(jnp.bfloat16)
    d_up = (d_act * gate_f * sig_gate).astype(jnp.bfloat16)
    grad_gate = jnp.dot(normed2_all.T, d_gate, preferred_element_type=jnp.float32)
    grad_up = jnp.dot(normed2_all.T, d_up, preferred_element_type=jnp.float32)
    d_norm2 = ring_scatter(
        jnp.dot(d_gate, w_gate.T, preferred_element_type=jnp.float32)
        + jnp.dot(d_up, w_up.T, preferred_element_type=jnp.float32),
        "mp",
    )
    gain2_part = jnp.sum(d_norm2 * resid * inverse2, axis=0)
    d_resid = out_grad.astype(jnp.float32) + norm_backward(resid, inverse2, norm2_gain, d_norm2)
    d_resid_low = d_resid.astype(jnp.bfloat16)
    grad_out = jnp.dot(mixed.T, d_resid_low, preferred_element_type=jnp.float32)
    d_mixed_rows = jnp.dot(d_resid_low, w_out_full.T, preferred_element_type=jnp.float32)
    d_mixed = to_heads(
        lax.all_to_all(d_mixed_rows.astype(jnp.bfloat16), "mp", 1, 0, tiled=True)
    ).astype(jnp.float32)
    gate_part = jnp.sum(d_mixed * (mem_out - dot_out), axis=(1, 2)) * gate_vec * (1.0 - gate_vec)
    d_dot = ((1.0 - gate) * d_mixed).astype(jnp.bfloat16)
    d_mem = (gate * d_mixed).reshape(seg_shape)
    dq_dot, dk_dot, dv_dot = attention_bwd(
        query_h, key_h, value_h, d_dot, log_sums, doc_index, score_scale
    )
    d_numer = read_mask[None, :, :, None] * d_mem / denom[..., None]
    d_denom = -jnp.sum(d_numer * numer, axis=-1) / denom * jnp.where(denom_raw > 1.0, 1.0, 0.0)
    d_sig_q = (
        jnp.einsum("hste,shde->hstd", d_numer, read_mem, precision=highest)
        + d_denom[..., None] * read_norm.transpose(1, 0, 2)[:, :, None]
    )
    d_read_mem = jnp.einsum("hstd,hste->shde", sig_q, d_numer, precision=highest)
    d_read_norm = jnp.einsum("hst,hstd->shd", d_denom, sig_q, precision=highest)
    back_mem = cont_flag[:, None, None, None] * d_read_mem
    back_norm = cont_flag[:, None, None] * d_read_norm
    back_summary, _ = lax.scan(
        fold_states, start_state, (keep_flag[:, None], back_mem, back_norm), reverse=True
    )
    _, grad_in, grad_norm_in = prefix(back_summary, "dp", link_states, start_state)

    def carry_back(state, item):
        flag, mem_read, norm_read = item
        grad_memory, grad_norm = state
        return (
            (flag * grad_memory + mem_read, flag * grad_norm + norm_read),
            (grad_memory, grad_norm),
        )

    _, (d_carried, d_carried_norm) = lax.scan(
        carry_back, (grad_in, grad_norm_in), (keep_flag, back_mem, back_norm), reverse=True
    )
    write4 = write_mask[None, :, :, None]
    d_sig_k = write4 * (
        jnp.einsum("hste,shde->hstd", value_f, d_carried, precision=highest)
        + d_carried_norm.transpose(1, 0, 2)[:, :, None]
    )
    d_val_mem = write4 * jnp.einsum("hstd,shde->hste", sig_k, d_carried, precision=highest)
    d_query = from_heads(
        dq_dot + (d_sig_q * feature_slope(query_f)).reshape(dq_dot.shape)
    ).astype(jnp.bfloat16)
    d_key = from_heads(
        dk_dot + (d_sig_k * feature_slope(key_f)).reshape(dk_dot.shape)
    ).astype(jnp.bfloat16)
    d_value = from_heads(dv_dot + d_val_mem.reshape(dv_dot.shape)).astype(jnp.bfloat16)
    grad_query = jnp.dot(normed1_all.T, d_query, preferred_element_type=jnp.float32)
    grad_key = jnp.dot(normed1_all.T, d_key, preferred_element_type=jnp.float32)
    grad_value = jnp.dot(normed1_all.T, d_value, preferred_element_type=jnp.float32)
    total_term = jnp.dot(d_query, w_query.T, preferred_element_type=jnp.float32)
    total_term = total_term + jnp.dot(d_key, w_key.T, preferred_element_type=jnp.float32)
    d_norm1 = ring_scatter(
        total_term + jnp.dot(d_value, w_value.T, preferred_element_type=jnp.float32), "mp"
    )
    gain1_part = jnp.sum(d_norm1 * x_rows * inverse1, axis=0)
    input_grad = d_resid + norm_backward(x_rows, inverse1, norm1_gain, d_norm1)
    gate_full = lax.dynamic_update_slice_in_dim(
        jnp.zeros((heads_here * mp_size,), jnp.float32),
        gate_part,
        lax.axis_index("mp") * heads_here,
        0,
    )
    gain1_sum, gain2_sum, gate_sum = lax.psum((gain1_part, gain2_part, gate_full), ("dp", "mp"))

    def over_dp(grad, dim):
        return lax.psum_scatter(
            grad.astype(jnp.bfloat16), "dp", scatter_dimension=dim, tiled=True
        ).astype(jnp.float32)

    out_sum = lax.psum_scatter(
        over_dp(grad_out, 1).astype(jnp.bfloat16), "mp", scatter_dimension=0, tiled=True
    ).astype(jnp.float32)
    query_sum, key_sum, value_sum, gate_w_sum, up_sum, down_sum = (
        over_dp(grad_query, 0),
        over_dp(grad_key, 0),
        over_dp(grad_value, 0),
        over_dp(grad_gate, 0),
        over_dp(grad_up, 0),
        over_dp(grad_down, 1),
    )
    return (
        output,
        input_grad,
        gain1_sum,
        query_sum,
        key_sum,
        value_sum,
        out_sum,
        gate_sum,
        gain2_sum,
        gate_w_sum,
        up_sum,
        down_sum,
    )


def solution(mesh):
    return jax.shard_map(
        local,
        mesh=mesh,
        in_specs=(
            P(("dp", "mp"), None),
            P(),
            P(None, "mp"),
            P(None, "mp"),
            P(None, "mp"),
            P("mp", None),
            P("mp"),
            P(),
            P(None, "mp"),
            P(None, "mp"),
            P("mp", None),
            P(),
            P(("dp", "mp"), None),
        ),
        out_specs=(
            P(("dp", "mp"), None),
            P(("dp", "mp"), None),
            P(),
            P("dp", "mp"),
            P("dp", "mp"),
            P("dp", "mp"),
            P("mp", "dp"),
            P(),
            P(),
            P("dp", "mp"),
            P("dp", "mp"),
            P("mp", "dp"),
        ),
        check_vma=False,
    )
```

```python
import functools
import math

import jax
import jax.numpy as jnp
from jax import lax
from jax.experimental import pallas as pl
from jax.experimental.pallas import tpu as pltpu
from jax.sharding import PartitionSpec as P

SEG = 2048


eps_norm = 1e-05
neg_fill = -1e30
highest = lax.Precision.HIGHEST


def gather_states(state, axis, kind):
    flag, memory, norm = state
    heads, size = norm.shape
    packed = jnp.concatenate(
        [memory.reshape(heads * size, size), norm, jnp.broadcast_to(flag.reshape(1, 1), (1, size))],
        axis=0,
    )
    everything = lax.all_gather(packed.astype(kind), axis).astype(jnp.float32)
    return (
        everything[:, heads * size + heads, 0],
        everything[:, : heads * size].reshape((-1, heads, size, size)),
        everything[:, heads * size : heads * size + heads],
    )


def combine_selected(weights, states):
    _, memory, norm = states
    return (
        jnp.sum(weights[:, None, None, None] * memory, axis=0),
        jnp.sum(weights[:, None, None] * norm, axis=0),
    )


def carried_in(value, axis):
    size, place = (lax.axis_size(axis), lax.axis_index(axis))
    states = gather_states(value, axis, jnp.float32)
    flags = states[0]
    k = jnp.arange(size)[:, None]
    j = jnp.arange(size)[None, :]
    factors = jnp.where((j > k) & (j < place), flags[None, :], 1.0)
    weights = jnp.where(jnp.arange(size) < place, jnp.prod(factors, axis=1), 0.0)
    return combine_selected(weights, states)


def prefix(value, axis):
    size, place = (lax.axis_size(axis), lax.axis_index(axis))
    states = gather_states(value, axis, jnp.bfloat16)
    flags = states[0]
    k = jnp.arange(size)[:, None]
    j = jnp.arange(size)[None, :]
    factors = jnp.where((j > place) & (j < k), flags[None, :], 1.0)
    weights = jnp.where(jnp.arange(size) > place, jnp.prod(factors, axis=1), 0.0)
    return combine_selected(weights, states)


def ring_pairs(n, step):
    return [(j, (j + step) % n) for j in range(n)]


def ring_gather(rows, axis, compute):
    n, place = lax.axis_size(axis), lax.axis_index(axis)
    count = rows.shape[0]
    half = count // 2
    own = compute(rows)
    outs = [
        lax.dynamic_update_slice_in_dim(
            jnp.zeros((n * count,) + part.shape[1:], part.dtype), part, place * count, 0
        )
        for part in own
    ]
    ahead, behind = rows[:half], rows[half:]
    for step in range(1, n):
        ahead = lax.ppermute(ahead, axis, ring_pairs(n, 1))
        behind = lax.ppermute(behind, axis, ring_pairs(n, -1))
        for got, start in (
            (compute(ahead), ((place - step) % n) * count),
            (compute(behind), ((place + step) % n) * count + half),
        ):
            outs = [
                lax.dynamic_update_slice_in_dim(out, part, start, 0)
                for out, part in zip(outs, got)
            ]
    return outs


def ring_scatter(partial, axis, kind=jnp.bfloat16):
    n, place = lax.axis_size(axis), lax.axis_index(axis)
    count = partial.shape[0] // n
    half = count // 2

    def chunk(owner, start):
        return lax.dynamic_slice_in_dim(partial, owner * count + start, half, 0).astype(jnp.float32)

    ahead = chunk((place - 1) % n, 0)
    behind = chunk((place + 1) % n, half)
    for step in range(1, n):
        ahead = lax.ppermute(ahead.astype(kind), axis, ring_pairs(n, 1)).astype(jnp.float32)
        ahead = ahead + chunk((place - 1 - step) % n, 0)
        behind = lax.ppermute(behind.astype(kind), axis, ring_pairs(n, -1)).astype(jnp.float32)
        behind = behind + chunk((place + 1 + step) % n, half)
    return jnp.concatenate([ahead, behind], axis=0)


def inverse_rms(values):
    return lax.rsqrt(jnp.mean(values * values, axis=-1, keepdims=True) + eps_norm)


def norm_backward(values, inverse, gain, upstream):
    scaled = upstream * gain
    inner = jnp.mean(values * scaled, axis=-1, keepdims=True)
    return inverse * scaled - values * inverse * inverse * inverse * inner


def feature(values):
    return jnp.where(values > 0, values + 1.0, jnp.exp(jnp.minimum(values, 0.0)))


def feature_slope(values):
    return jnp.where(values > 0, 1.0, jnp.exp(jnp.minimum(values, 0.0)))


def link_states(earlier, later):
    return (
        earlier[0] * later[0],
        later[0] * earlier[1] + later[1],
        later[0] * earlier[2] + later[2],
    )


def fold_states(state, item):
    return (link_states(state, item), None)


def document_ids(doc_lengths, first, count):
    bounds = jnp.cumsum(doc_lengths)
    position = first + jnp.arange(count, dtype=jnp.int32)
    before = jnp.sum((bounds[None, :] <= position[:, None]).astype(jnp.int32), axis=1)
    return jnp.where(position < bounds[-1], before, doc_lengths.shape[0] + position)


def block_allowed(doc_index, row_start, seg_start, block_rows):
    query_docs = lax.dynamic_slice_in_dim(doc_index, row_start, block_rows, 0)
    query_pos = row_start + jnp.arange(block_rows, dtype=jnp.int32)
    key_pos = seg_start + jnp.arange(SEG, dtype=jnp.int32)
    return (key_pos[None, :] <= query_pos[:, None]) & (doc_index[None, :] == query_docs[:, None])


NEG = -1e30
BQ = 256


def _mask(qi, docq, dock, seg):
    row = (qi * BQ) % seg + lax.broadcasted_iota(jnp.int32, (BQ, seg), 0)
    col = lax.broadcasted_iota(jnp.int32, (BQ, seg), 1)
    return (col <= row) & (docq == dock)


def _fwd_kernel(scale, seg, q_ref, k_ref, v_ref, docq_ref, dock_ref, o_ref, lse_ref):
    qi = pl.program_id(1)
    q = q_ref[0]
    k = k_ref[0]
    v = v_ref[0]
    s = lax.dot_general(q, k, (((1,), (1,)), ((), ())), preferred_element_type=jnp.float32)
    allowed = _mask(qi, docq_ref[...], dock_ref[...], seg)
    s = jnp.where(allowed, s * scale, NEG)
    m = jnp.max(s, axis=1, keepdims=True)
    e = jnp.exp(s - m)
    l = jnp.sum(e, axis=1, keepdims=True)
    p = (e / l).astype(jnp.bfloat16)
    o_ref[0] = jnp.dot(p, v, preferred_element_type=jnp.float32)
    lse_ref[0] = m + jnp.log(l)


def _bwd_kernel(scale, seg, q_ref, k_ref, v_ref, do_ref, lse_ref, docq_ref, dock_ref,
                dq_ref, dk_ref, dv_ref):
    qi = pl.program_id(1)

    @pl.when((qi * BQ) % seg == 0)
    def _():
        dk_ref[...] = jnp.zeros_like(dk_ref)
        dv_ref[...] = jnp.zeros_like(dv_ref)

    q = q_ref[0]
    k = k_ref[0]
    v = v_ref[0]
    do = do_ref[0]
    s = lax.dot_general(q, k, (((1,), (1,)), ((), ())), preferred_element_type=jnp.float32)
    allowed = _mask(qi, docq_ref[...], dock_ref[...], seg)
    s = jnp.where(allowed, s * scale, NEG)
    p = jnp.exp(s - lse_ref[0])
    dp = lax.dot_general(do, v, (((1,), (1,)), ((), ())), preferred_element_type=jnp.float32)
    delta = jnp.sum(p * dp, axis=1, keepdims=True)
    ds = (p * (dp - delta) * scale).astype(jnp.bfloat16)
    dq_ref[0] = jnp.dot(ds, k, preferred_element_type=jnp.float32)
    dk_ref[0] += lax.dot_general(ds, q, (((0,), (0,)), ((), ())), preferred_element_type=jnp.float32)
    dv_ref[0] += lax.dot_general(p.astype(jnp.bfloat16), do, (((0,), (0,)), ((), ())),
                                 preferred_element_type=jnp.float32)


def attention_fwd(q, k, v, doc, scale):
    H, T, d = q.shape
    seg = min(SEG, T)
    nq = T // BQ
    docq = doc.reshape(T, 1)
    dock = doc.reshape(1, T)
    qspec = pl.BlockSpec((1, BQ, d), lambda h, i: (h, i, 0))
    kspec = pl.BlockSpec((1, seg, d), lambda h, i: (h, i * BQ // seg, 0))
    flops = 4 * H * T * seg * d
    return pl.pallas_call(
        functools.partial(_fwd_kernel, scale, seg),
        grid=(H, nq),
        in_specs=[qspec, kspec, kspec,
                  pl.BlockSpec((BQ, 1), lambda h, i: (i, 0)),
                  pl.BlockSpec((1, seg), lambda h, i: (0, i * BQ // seg))],
        out_specs=[pl.BlockSpec((1, BQ, d), lambda h, i: (h, i, 0)),
                   pl.BlockSpec((1, BQ, 1), lambda h, i: (h, i, 0))],
        out_shape=[jax.ShapeDtypeStruct((H, T, d), jnp.float32),
                   jax.ShapeDtypeStruct((H, T, 1), jnp.float32)],
        compiler_params=pltpu.CompilerParams(dimension_semantics=("arbitrary", "arbitrary")),
        cost_estimate=pl.CostEstimate(flops=flops, transcendentals=H * T * seg,
                                      bytes_accessed=H * T * d * 10),
    )(q, k, v, docq, dock)


def attention_bwd(q, k, v, do, lse, doc, scale):
    H, T, d = q.shape
    seg = min(SEG, T)
    nq = T // BQ
    docq = doc.reshape(T, 1)
    dock = doc.reshape(1, T)
    qspec = pl.BlockSpec((1, BQ, d), lambda h, i: (h, i, 0))
    kspec = pl.BlockSpec((1, seg, d), lambda h, i: (h, i * BQ // seg, 0))
    flops = 10 * H * T * seg * d
    return pl.pallas_call(
        functools.partial(_bwd_kernel, scale, seg),
        grid=(H, nq),
        in_specs=[qspec, kspec, kspec, qspec,
                  pl.BlockSpec((1, BQ, 1), lambda h, i: (h, i, 0)),
                  pl.BlockSpec((BQ, 1), lambda h, i: (i, 0)),
                  pl.BlockSpec((1, seg), lambda h, i: (0, i * BQ // seg))],
        out_specs=[qspec, kspec, kspec],
        out_shape=[jax.ShapeDtypeStruct((H, T, d), jnp.float32)] * 3,
        compiler_params=pltpu.CompilerParams(dimension_semantics=("arbitrary", "arbitrary")),
        cost_estimate=pl.CostEstimate(flops=flops, transcendentals=H * T * seg,
                                      bytes_accessed=H * T * d * 24),
    )(q, k, v, do, lse, docq, dock)


def local(
    tokens,
    norm1_gain,
    w_query,
    w_key,
    w_value,
    w_out,
    gate_logit,
    norm2_gain,
    w_gate,
    w_up,
    w_down,
    doc_lengths,
    out_grad,
):
    heads_here = gate_logit.shape[0]
    head_size = w_query.shape[1] // heads_here
    local_rows = tokens.shape[0]
    mp_size = lax.axis_size("mp")
    dp_size = lax.axis_size("dp")
    group_rows = local_rows * mp_size
    seg_count = group_rows // SEG
    score_scale = 1.0 / math.sqrt(head_size)
    group_first = lax.axis_index("dp") * group_rows
    shifted_ids = document_ids(doc_lengths, group_first - 1, group_rows + 1)
    doc_index = shifted_ids[1:]
    before_doc = jnp.where(group_first > 0, shifted_ids[0], -1)
    seg_docs = doc_index.reshape(seg_count, SEG)
    seg_first = seg_docs[:, 0]
    seg_last = seg_docs[:, -1]
    prev_last = jnp.concatenate([before_doc[None], seg_last[:-1]])
    cont_flag = jnp.where(seg_first == prev_last, 1.0, 0.0).astype(jnp.float32)
    keep_flag = jnp.where(seg_last == prev_last, 1.0, 0.0).astype(jnp.float32)
    read_mask = jnp.where(seg_docs == seg_first[:, None], 1.0, 0.0).astype(jnp.float32)
    write_mask = jnp.where(seg_docs == seg_last[:, None], 1.0, 0.0).astype(jnp.float32)
    width = w_out.shape[1]

    def to_heads(rows):
        return rows.reshape(group_rows, heads_here, head_size).transpose(1, 0, 2)

    def from_heads(heads):
        return heads.transpose(1, 0, 2).reshape(group_rows, heads_here * head_size)

    seg_shape = (heads_here, seg_count, SEG, head_size)
    piece = width // dp_size
    w_out_piece = lax.dynamic_slice_in_dim(w_out, lax.axis_index("dp") * piece, piece, axis=1)
    w_out_full = lax.all_gather(
        lax.all_gather(w_out_piece, "mp", axis=0, tiled=True), "dp", axis=1, tiled=True
    )
    x_rows = tokens.astype(jnp.float32)
    inverse1 = inverse_rms(x_rows)
    normed1 = (x_rows * inverse1 * norm1_gain).astype(jnp.bfloat16)
    def project_qkv(rows):
        return (rows,) + tuple(
            jnp.dot(rows, weight, preferred_element_type=jnp.float32).astype(jnp.bfloat16)
            for weight in (w_query, w_key, w_value)
        )

    normed1_all, query_rows, key_rows, value_rows = ring_gather(normed1, "mp", project_qkv)
    query_h, key_h, value_h = (to_heads(a) for a in (query_rows, key_rows, value_rows))
    grad_rows, query_h = lax.optimization_barrier((out_grad, query_h))
    dot_out, log_sums = attention_fwd(query_h, key_h, value_h, doc_index, score_scale)
    query_f = query_h.astype(jnp.float32).reshape(seg_shape)
    key_f = key_h.astype(jnp.float32).reshape(seg_shape)
    value_f = value_h.astype(jnp.float32).reshape(seg_shape)
    sig_q = feature(query_f)
    sig_k = feature(key_f)
    updates = jnp.einsum("st,hstd,hste->shde", write_mask, sig_k, value_f, precision=highest)
    norm_updates = jnp.einsum("st,hstd->shd", write_mask, sig_k, precision=highest)
    start_state = (
        jnp.ones((1,), jnp.float32),
        jnp.zeros(updates.shape[1:], jnp.float32),
        jnp.zeros(norm_updates.shape[1:], jnp.float32),
    )
    summary, _ = lax.scan(fold_states, start_state, (keep_flag[:, None], updates, norm_updates))
    memory_in, norm_in = carried_in(summary, "dp")

    def carry_forward(state, item):
        flag, read_flag, update, norm_update = item
        memory, norm_sum = state
        return (
            (flag * memory + update, flag * norm_sum + norm_update),
            (read_flag * memory, read_flag * norm_sum),
        )

    _, (read_mem, read_norm) = lax.scan(
        carry_forward, (memory_in, norm_in), (keep_flag, cont_flag, updates, norm_updates)
    )
    numer = jnp.einsum("hstd,shde->hste", sig_q, read_mem, precision=highest)
    denom_raw = jnp.einsum("hstd,shd->hst", sig_q, read_norm, precision=highest)
    denom = jnp.maximum(denom_raw, 1.0)
    mem_out = (read_mask[None, :, :, None] * numer / denom[..., None]).reshape(dot_out.shape)
    gate_vec = jax.nn.sigmoid(gate_logit)
    gate = gate_vec[:, None, None]
    mixed_cols = from_heads(gate * mem_out + (1.0 - gate) * dot_out).astype(jnp.bfloat16)
    mixed = lax.all_to_all(mixed_cols, "mp", 0, 1, tiled=True)
    attn_sum = jnp.dot(mixed, w_out_full, preferred_element_type=jnp.float32)
    resid = x_rows + attn_sum
    inverse2 = inverse_rms(resid)
    normed2 = (resid * inverse2 * norm2_gain).astype(jnp.bfloat16)
    def project_ffn(rows):
        return (rows,) + tuple(
            jnp.dot(rows, weight, preferred_element_type=jnp.float32).astype(jnp.bfloat16)
            for weight in (w_gate, w_up)
        )

    normed2_all, gate_pre, up_pre = ring_gather(normed2, "mp", project_ffn)
    gate_f = gate_pre.astype(jnp.float32)
    up_f = up_pre.astype(jnp.float32)
    sig_gate = jax.nn.sigmoid(gate_f)
    act = (gate_f * sig_gate * up_f).astype(jnp.bfloat16)
    mlp_part = jnp.dot(act, w_down, preferred_element_type=jnp.float32)
    grad_rows_all = lax.all_gather(grad_rows, "mp", axis=0, tiled=True)
    d_act = jnp.dot(grad_rows_all, w_down.T, preferred_element_type=jnp.float32)
    grad_down = jnp.dot(act.T, grad_rows_all, preferred_element_type=jnp.float32)
    d_gate = (d_act * up_f * sig_gate * (1.0 + gate_f * (1.0 - sig_gate))).astype(jnp.bfloat16)
    d_up = (d_act * gate_f * sig_gate).astype(jnp.bfloat16)
    grad_gate = jnp.dot(normed2_all.T, d_gate, preferred_element_type=jnp.float32)
    grad_up = jnp.dot(normed2_all.T, d_up, preferred_element_type=jnp.float32)
    d_norm2 = ring_scatter(
        jnp.dot(d_gate, w_gate.T, preferred_element_type=jnp.float32)
        + jnp.dot(d_up, w_up.T, preferred_element_type=jnp.float32),
        "mp",
    )
    gain2_part = jnp.sum(d_norm2 * resid * inverse2, axis=0)
    d_resid = out_grad.astype(jnp.float32) + norm_backward(resid, inverse2, norm2_gain, d_norm2)
    d_resid_low = d_resid.astype(jnp.bfloat16)
    grad_out = jnp.dot(mixed.T, d_resid_low, preferred_element_type=jnp.float32)
    d_mixed_rows = jnp.dot(d_resid_low, w_out_full.T, preferred_element_type=jnp.float32)
    d_mixed = to_heads(
        lax.all_to_all(d_mixed_rows.astype(jnp.bfloat16), "mp", 1, 0, tiled=True)
    ).astype(jnp.float32)
    mlp_part, d_mixed = lax.optimization_barrier((mlp_part, d_mixed))
    output = (resid + ring_scatter(mlp_part, "mp")).astype(jnp.bfloat16)
    gate_part = jnp.sum(d_mixed * (mem_out - dot_out), axis=(1, 2)) * gate_vec * (1.0 - gate_vec)
    d_dot = ((1.0 - gate) * d_mixed).astype(jnp.bfloat16)
    d_mem = (gate * d_mixed).reshape(seg_shape)
    dq_dot, dk_dot, dv_dot = attention_bwd(
        query_h, key_h, value_h, d_dot, log_sums, doc_index, score_scale
    )
    d_numer = read_mask[None, :, :, None] * d_mem / denom[..., None]
    d_denom = -jnp.sum(d_numer * numer, axis=-1) / denom * jnp.where(denom_raw > 1.0, 1.0, 0.0)
    d_sig_q = (
        jnp.einsum("hste,shde->hstd", d_numer, read_mem, precision=highest)
        + d_denom[..., None] * read_norm.transpose(1, 0, 2)[:, :, None]
    )
    d_read_mem = jnp.einsum("hstd,hste->shde", sig_q, d_numer, precision=highest)
    d_read_norm = jnp.einsum("hst,hstd->shd", d_denom, sig_q, precision=highest)
    back_mem = cont_flag[:, None, None, None] * d_read_mem
    back_norm = cont_flag[:, None, None] * d_read_norm
    back_summary, _ = lax.scan(
        fold_states, start_state, (keep_flag[:, None], back_mem, back_norm), reverse=True
    )
    grad_in, grad_norm_in = prefix(back_summary, "dp")

    def carry_back(state, item):
        flag, mem_read, norm_read = item
        grad_memory, grad_norm = state
        return (
            (flag * grad_memory + mem_read, flag * grad_norm + norm_read),
            (grad_memory, grad_norm),
        )

    _, (d_carried, d_carried_norm) = lax.scan(
        carry_back, (grad_in, grad_norm_in), (keep_flag, back_mem, back_norm), reverse=True
    )
    write4 = write_mask[None, :, :, None]
    d_sig_k = write4 * (
        jnp.einsum("hste,shde->hstd", value_f, d_carried, precision=highest)
        + d_carried_norm.transpose(1, 0, 2)[:, :, None]
    )
    d_val_mem = write4 * jnp.einsum("hstd,shde->hste", sig_k, d_carried, precision=highest)
    d_query = from_heads(
        dq_dot + (d_sig_q * feature_slope(query_f)).reshape(dq_dot.shape)
    ).astype(jnp.bfloat16)
    d_key = from_heads(
        dk_dot + (d_sig_k * feature_slope(key_f)).reshape(dk_dot.shape)
    ).astype(jnp.bfloat16)
    d_value = from_heads(dv_dot + d_val_mem.reshape(dv_dot.shape)).astype(jnp.bfloat16)
    grad_query = jnp.dot(normed1_all.T, d_query, preferred_element_type=jnp.float32)
    grad_key = jnp.dot(normed1_all.T, d_key, preferred_element_type=jnp.float32)
    grad_value = jnp.dot(normed1_all.T, d_value, preferred_element_type=jnp.float32)
    total_term = jnp.dot(d_query, w_query.T, preferred_element_type=jnp.float32)
    total_term = total_term + jnp.dot(d_key, w_key.T, preferred_element_type=jnp.float32)
    d_norm1 = ring_scatter(
        total_term + jnp.dot(d_value, w_value.T, preferred_element_type=jnp.float32), "mp"
    )
    gain1_part = jnp.sum(d_norm1 * x_rows * inverse1, axis=0)
    input_grad = d_resid + norm_backward(x_rows, inverse1, norm1_gain, d_norm1)
    gate_full = lax.dynamic_update_slice_in_dim(
        jnp.zeros((heads_here * mp_size,), jnp.float32),
        gate_part,
        lax.axis_index("mp") * heads_here,
        0,
    )
    gain1_sum, gain2_sum, gate_sum = lax.psum(
        lax.psum((gain1_part, gain2_part, gate_full), "mp"), "dp"
    )

    def over_dp(grad, dim):
        return lax.psum_scatter(
            grad.astype(jnp.bfloat16), "dp", scatter_dimension=dim, tiled=True
        ).astype(jnp.float32)

    out_sum = lax.psum_scatter(
        over_dp(grad_out, 1).astype(jnp.bfloat16), "mp", scatter_dimension=0, tiled=True
    ).astype(jnp.float32)
    query_sum, key_sum, value_sum, gate_w_sum, up_sum, down_sum = (
        over_dp(grad_query, 0),
        over_dp(grad_key, 0),
        over_dp(grad_value, 0),
        over_dp(grad_gate, 0),
        over_dp(grad_up, 0),
        over_dp(grad_down, 1),
    )
    return (
        output,
        input_grad,
        gain1_sum,
        query_sum,
        key_sum,
        value_sum,
        out_sum,
        gate_sum,
        gain2_sum,
        gate_w_sum,
        up_sum,
        down_sum,
    )


def solution(mesh):
    return jax.shard_map(
        local,
        mesh=mesh,
        in_specs=(
            P(("dp", "mp"), None),
            P(),
            P(None, "mp"),
            P(None, "mp"),
            P(None, "mp"),
            P("mp", None),
            P("mp"),
            P(),
            P(None, "mp"),
            P(None, "mp"),
            P("mp", None),
            P(),
            P(("dp", "mp"), None),
        ),
        out_specs=(
            P(("dp", "mp"), None),
            P(("dp", "mp"), None),
            P(),
            P("dp", "mp"),
            P("dp", "mp"),
            P("dp", "mp"),
            P("mp", "dp"),
            P(),
            P(),
            P("dp", "mp"),
            P("dp", "mp"),
            P("mp", "dp"),
        ),
        check_vma=False,
    )
```

```python
import functools
import math

import jax
import jax.numpy as jnp
from jax import lax
from jax.experimental import pallas as pl
from jax.experimental.pallas import tpu as pltpu
from jax.sharding import PartitionSpec as P


SEG = 2048


eps_norm = 1e-05
highest = lax.Precision.HIGHEST


def gather_states(state, axis, kind):
    flag, memory, norm = state
    heads, size = norm.shape
    packed = jnp.concatenate(
        [memory.reshape(heads * size, size), norm, jnp.broadcast_to(flag.reshape(1, 1), (1, size))],
        axis=0,
    )
    everything = lax.all_gather(packed.astype(kind), axis).astype(jnp.float32)
    return (
        everything[:, heads * size + heads, 0],
        everything[:, : heads * size].reshape((-1, heads, size, size)),
        everything[:, heads * size : heads * size + heads],
    )


def combine_selected(weights, states):
    _, memory, norm = states
    return (
        jnp.sum(weights[:, None, None, None] * memory, axis=0),
        jnp.sum(weights[:, None, None] * norm, axis=0),
    )


def carried_in(value, axis):
    size, place = (lax.axis_size(axis), lax.axis_index(axis))
    states = gather_states(value, axis, jnp.float32)
    flags = states[0]
    k = jnp.arange(size)[:, None]
    j = jnp.arange(size)[None, :]
    factors = jnp.where((j > k) & (j < place), flags[None, :], 1.0)
    weights = jnp.where(jnp.arange(size) < place, jnp.prod(factors, axis=1), 0.0)
    return combine_selected(weights, states)


def prefix(value, axis):
    size, place = (lax.axis_size(axis), lax.axis_index(axis))
    states = gather_states(value, axis, jnp.bfloat16)
    flags = states[0]
    k = jnp.arange(size)[:, None]
    j = jnp.arange(size)[None, :]
    factors = jnp.where((j > place) & (j < k), flags[None, :], 1.0)
    weights = jnp.where(jnp.arange(size) > place, jnp.prod(factors, axis=1), 0.0)
    return combine_selected(weights, states)


def ring_pairs(n, step):
    return [(j, (j + step) % n) for j in range(n)]


def ring_gather(rows, axis, compute):
    n, place = lax.axis_size(axis), lax.axis_index(axis)
    count = rows.shape[0]
    half = count // 2
    own = compute(rows)
    outs = [
        lax.dynamic_update_slice_in_dim(
            jnp.zeros((n * count,) + part.shape[1:], part.dtype), part, place * count, 0
        )
        for part in own
    ]
    ahead, behind = rows[:half], rows[half:]
    for step in range(1, n):
        ahead = lax.ppermute(ahead, axis, ring_pairs(n, 1))
        behind = lax.ppermute(behind, axis, ring_pairs(n, -1))
        for got, start in (
            (compute(ahead), ((place - step) % n) * count),
            (compute(behind), ((place + step) % n) * count + half),
        ):
            outs = [
                lax.dynamic_update_slice_in_dim(out, part, start, 0)
                for out, part in zip(outs, got)
            ]
    return outs


def ring_scatter(partial, axis, kind=jnp.bfloat16):
    n, place = lax.axis_size(axis), lax.axis_index(axis)
    count = partial.shape[0] // n
    half = count // 2

    def chunk(owner, start):
        return lax.dynamic_slice_in_dim(partial, owner * count + start, half, 0).astype(jnp.float32)

    ahead = chunk((place - 1) % n, 0)
    behind = chunk((place + 1) % n, half)
    for step in range(1, n):
        ahead = lax.ppermute(ahead.astype(kind), axis, ring_pairs(n, 1))
        behind = lax.ppermute(behind.astype(kind), axis, ring_pairs(n, -1))
        ahead = ahead.astype(jnp.float32) + chunk((place - 1 - step) % n, 0)
        behind = behind.astype(jnp.float32) + chunk((place + 1 + step) % n, half)
    return jnp.concatenate([ahead, behind], axis=0)


def inverse_rms(values):
    return lax.rsqrt(jnp.mean(values * values, axis=-1, keepdims=True) + eps_norm)


def norm_backward(values, inverse, gain, upstream):
    scaled = upstream * gain
    inner = jnp.mean(values * scaled, axis=-1, keepdims=True)
    return inverse * scaled - values * inverse * inverse * inverse * inner


def feature(values):
    return jnp.where(values > 0, values + 1.0, jnp.exp(jnp.minimum(values, 0.0)))


def feature_slope(values):
    return jnp.where(values > 0, 1.0, jnp.exp(jnp.minimum(values, 0.0)))


def link_states(earlier, later):
    return (
        earlier[0] * later[0],
        later[0] * earlier[1] + later[1],
        later[0] * earlier[2] + later[2],
    )


def fold_states(state, item):
    return (link_states(state, item), None)


def document_ids(doc_lengths, first, count):
    bounds = jnp.cumsum(doc_lengths)
    position = first + jnp.arange(count, dtype=jnp.int32)
    before = jnp.sum((bounds[None, :] <= position[:, None]).astype(jnp.int32), axis=1)
    return jnp.where(position < bounds[-1], before, doc_lengths.shape[0] + position)


NEG = -1e30
BQ = 256


def _mask(qi, docq, dock, seg):
    row = (qi * BQ) % seg + lax.broadcasted_iota(jnp.int32, (BQ, seg), 0)
    col = lax.broadcasted_iota(jnp.int32, (BQ, seg), 1)
    return (col <= row) & (docq == dock)


def _fwd_kernel(scale, seg, q_ref, k_ref, v_ref, docq_ref, dock_ref, o_ref, lse_ref):
    qi = pl.program_id(1)
    q = q_ref[0]
    k = k_ref[0]
    v = v_ref[0]
    s = lax.dot_general(q, k, (((1,), (1,)), ((), ())), preferred_element_type=jnp.float32)
    allowed = _mask(qi, docq_ref[...], dock_ref[...], seg)
    s = jnp.where(allowed, s * scale, NEG)
    m = jnp.max(s, axis=1, keepdims=True)
    e = jnp.exp(s - m)
    l = jnp.sum(e, axis=1, keepdims=True)
    p = (e / l).astype(jnp.bfloat16)
    o_ref[0] = jnp.dot(p, v, preferred_element_type=jnp.float32)
    lse_ref[0] = m + jnp.log(l)


def _bwd_kernel(scale, seg, q_ref, k_ref, v_ref, do_ref, lse_ref, docq_ref, dock_ref,
                dq_ref, dk_ref, dv_ref):
    qi = pl.program_id(1)

    @pl.when((qi * BQ) % seg == 0)
    def _():
        dk_ref[...] = jnp.zeros_like(dk_ref)
        dv_ref[...] = jnp.zeros_like(dv_ref)

    q = q_ref[0]
    k = k_ref[0]
    v = v_ref[0]
    do = do_ref[0]
    s = lax.dot_general(q, k, (((1,), (1,)), ((), ())), preferred_element_type=jnp.float32)
    allowed = _mask(qi, docq_ref[...], dock_ref[...], seg)
    s = jnp.where(allowed, s * scale, NEG)
    p = jnp.exp(s - lse_ref[0])
    dp = lax.dot_general(do, v, (((1,), (1,)), ((), ())), preferred_element_type=jnp.float32)
    delta = jnp.sum(p * dp, axis=1, keepdims=True)
    ds = (p * (dp - delta) * scale).astype(jnp.bfloat16)
    dq_ref[0] = jnp.dot(ds, k, preferred_element_type=jnp.float32)
    dk_ref[0] += lax.dot_general(ds, q, (((0,), (0,)), ((), ())), preferred_element_type=jnp.float32)
    dv_ref[0] += lax.dot_general(p.astype(jnp.bfloat16), do, (((0,), (0,)), ((), ())),
                                 preferred_element_type=jnp.float32)


def attention_fwd(q, k, v, doc, scale):
    H, T, d = q.shape
    seg = min(SEG, T)
    nq = T // BQ
    docq = doc.reshape(T, 1)
    dock = doc.reshape(1, T)
    qspec = pl.BlockSpec((1, BQ, d), lambda h, i: (h, i, 0))
    kspec = pl.BlockSpec((1, seg, d), lambda h, i: (h, i * BQ // seg, 0))
    flops = 4 * H * T * seg * d
    return pl.pallas_call(
        functools.partial(_fwd_kernel, scale, seg),
        grid=(H, nq),
        in_specs=[qspec, kspec, kspec,
                  pl.BlockSpec((BQ, 1), lambda h, i: (i, 0)),
                  pl.BlockSpec((1, seg), lambda h, i: (0, i * BQ // seg))],
        out_specs=[pl.BlockSpec((1, BQ, d), lambda h, i: (h, i, 0)),
                   pl.BlockSpec((1, BQ, 1), lambda h, i: (h, i, 0))],
        out_shape=[jax.ShapeDtypeStruct((H, T, d), jnp.float32),
                   jax.ShapeDtypeStruct((H, T, 1), jnp.float32)],
        compiler_params=pltpu.CompilerParams(dimension_semantics=("arbitrary", "arbitrary")),
        cost_estimate=pl.CostEstimate(flops=flops, transcendentals=H * T * seg,
                                      bytes_accessed=H * T * d * 10),
    )(q, k, v, docq, dock)


def attention_bwd(q, k, v, do, lse, doc, scale):
    H, T, d = q.shape
    seg = min(SEG, T)
    nq = T // BQ
    docq = doc.reshape(T, 1)
    dock = doc.reshape(1, T)
    qspec = pl.BlockSpec((1, BQ, d), lambda h, i: (h, i, 0))
    kspec = pl.BlockSpec((1, seg, d), lambda h, i: (h, i * BQ // seg, 0))
    flops = 10 * H * T * seg * d
    return pl.pallas_call(
        functools.partial(_bwd_kernel, scale, seg),
        grid=(H, nq),
        in_specs=[qspec, kspec, kspec, qspec,
                  pl.BlockSpec((1, BQ, 1), lambda h, i: (h, i, 0)),
                  pl.BlockSpec((BQ, 1), lambda h, i: (i, 0)),
                  pl.BlockSpec((1, seg), lambda h, i: (0, i * BQ // seg))],
        out_specs=[qspec, kspec, kspec],
        out_shape=[jax.ShapeDtypeStruct((H, T, d), jnp.float32)] * 3,
        compiler_params=pltpu.CompilerParams(dimension_semantics=("arbitrary", "arbitrary")),
        cost_estimate=pl.CostEstimate(flops=flops, transcendentals=H * T * seg,
                                      bytes_accessed=H * T * d * 24),
    )(q, k, v, do, lse, docq, dock)


def local(
    tokens,
    norm1_gain,
    w_query,
    w_key,
    w_value,
    w_out,
    gate_logit,
    norm2_gain,
    w_gate,
    w_up,
    w_down,
    doc_lengths,
    out_grad,
):
    heads_here = gate_logit.shape[0]
    head_size = w_query.shape[1] // heads_here
    local_rows = tokens.shape[0]
    mp_size = lax.axis_size("mp")
    dp_size = lax.axis_size("dp")
    group_rows = local_rows * mp_size
    seg_count = group_rows // SEG
    score_scale = 1.0 / math.sqrt(head_size)
    group_first = lax.axis_index("dp") * group_rows
    shifted_ids = document_ids(doc_lengths, group_first - 1, group_rows + 1)
    doc_index = shifted_ids[1:]
    before_doc = jnp.where(group_first > 0, shifted_ids[0], -1)
    seg_docs = doc_index.reshape(seg_count, SEG)
    seg_first = seg_docs[:, 0]
    seg_last = seg_docs[:, -1]
    prev_last = jnp.concatenate([before_doc[None], seg_last[:-1]])
    cont_flag = jnp.where(seg_first == prev_last, 1.0, 0.0).astype(jnp.float32)
    keep_flag = jnp.where(seg_last == prev_last, 1.0, 0.0).astype(jnp.float32)
    read_mask = jnp.where(seg_docs == seg_first[:, None], 1.0, 0.0).astype(jnp.float32)
    write_mask = jnp.where(seg_docs == seg_last[:, None], 1.0, 0.0).astype(jnp.float32)
    width = w_out.shape[1]

    def to_heads(rows):
        return rows.reshape(group_rows, heads_here, head_size).transpose(1, 0, 2)

    def from_heads(heads):
        return heads.transpose(1, 0, 2).reshape(group_rows, heads_here * head_size)

    seg_shape = (heads_here, seg_count, SEG, head_size)
    piece = width // dp_size
    w_out_piece = lax.dynamic_slice_in_dim(w_out, lax.axis_index("dp") * piece, piece, axis=1)
    w_out_full = lax.all_gather(
        lax.all_gather(w_out_piece, "mp", axis=0, tiled=True), "dp", axis=1, tiled=True
    )
    x_rows = tokens.astype(jnp.float32)
    inverse1 = inverse_rms(x_rows)
    normed1 = (x_rows * inverse1 * norm1_gain).astype(jnp.bfloat16)

    def project_qkv(rows):
        return (rows,) + tuple(
            jnp.dot(rows, weight, preferred_element_type=jnp.float32).astype(jnp.bfloat16)
            for weight in (w_query, w_key, w_value)
        )

    normed1_all, query_rows, key_rows, value_rows = ring_gather(normed1, "mp", project_qkv)
    query_h, key_h, value_h = (to_heads(a) for a in (query_rows, key_rows, value_rows))
    grad_rows, query_h = lax.optimization_barrier((out_grad, query_h))
    dot_out, log_sums = attention_fwd(query_h, key_h, value_h, doc_index, score_scale)
    query_f = query_h.astype(jnp.float32).reshape(seg_shape)
    key_f = key_h.astype(jnp.float32).reshape(seg_shape)
    value_f = value_h.astype(jnp.float32).reshape(seg_shape)
    sig_q = feature(query_f)
    sig_k = feature(key_f)
    updates = jnp.einsum("st,hstd,hste->shde", write_mask, sig_k, value_f, precision=highest)
    norm_updates = jnp.einsum("st,hstd->shd", write_mask, sig_k, precision=highest)
    start_state = (
        jnp.ones((1,), jnp.float32),
        jnp.zeros(updates.shape[1:], jnp.float32),
        jnp.zeros(norm_updates.shape[1:], jnp.float32),
    )
    summary, _ = lax.scan(fold_states, start_state, (keep_flag[:, None], updates, norm_updates))
    memory_in, norm_in = carried_in(summary, "dp")

    def carry_forward(state, item):
        flag, read_flag, update, norm_update = item
        memory, norm_sum = state
        return (
            (flag * memory + update, flag * norm_sum + norm_update),
            (read_flag * memory, read_flag * norm_sum),
        )

    _, (read_mem, read_norm) = lax.scan(
        carry_forward, (memory_in, norm_in), (keep_flag, cont_flag, updates, norm_updates)
    )
    numer = jnp.einsum("hstd,shde->hste", sig_q, read_mem, precision=highest)
    denom_raw = jnp.einsum("hstd,shd->hst", sig_q, read_norm, precision=highest)
    denom = jnp.maximum(denom_raw, 1.0)
    mem_out = (read_mask[None, :, :, None] * numer / denom[..., None]).reshape(dot_out.shape)
    gate_vec = jax.nn.sigmoid(gate_logit)
    gate = gate_vec[:, None, None]
    mixed_cols = from_heads(gate * mem_out + (1.0 - gate) * dot_out).astype(jnp.bfloat16)
    mixed = lax.all_to_all(mixed_cols, "mp", 0, 1, tiled=True)
    attn_sum = jnp.dot(mixed, w_out_full, preferred_element_type=jnp.float32)
    resid = x_rows + attn_sum
    inverse2 = inverse_rms(resid)
    normed2 = (resid * inverse2 * norm2_gain).astype(jnp.bfloat16)

    def project_ffn(rows):
        return (rows,) + tuple(
            jnp.dot(rows, weight, preferred_element_type=jnp.float32).astype(jnp.bfloat16)
            for weight in (w_gate, w_up)
        )

    normed2_all, gate_pre, up_pre = ring_gather(normed2, "mp", project_ffn)
    gate_f = gate_pre.astype(jnp.float32)
    up_f = up_pre.astype(jnp.float32)
    sig_gate = jax.nn.sigmoid(gate_f)
    act = (gate_f * sig_gate * up_f).astype(jnp.bfloat16)
    mlp_part = jnp.dot(act, w_down, preferred_element_type=jnp.float32)
    (grad_rows_all,) = ring_gather(grad_rows, "mp", lambda rows: (rows,))
    d_act = jnp.dot(grad_rows_all, w_down.T, preferred_element_type=jnp.float32)
    grad_down = jnp.dot(act.T, grad_rows_all, preferred_element_type=jnp.float32)
    d_gate = (d_act * up_f * sig_gate * (1.0 + gate_f * (1.0 - sig_gate))).astype(jnp.bfloat16)
    d_up = (d_act * gate_f * sig_gate).astype(jnp.bfloat16)
    grad_gate = jnp.dot(normed2_all.T, d_gate, preferred_element_type=jnp.float32)
    grad_up = jnp.dot(normed2_all.T, d_up, preferred_element_type=jnp.float32)
    d_norm2 = ring_scatter(
        jnp.dot(d_gate, w_gate.T, preferred_element_type=jnp.float32)
        + jnp.dot(d_up, w_up.T, preferred_element_type=jnp.float32),
        "mp",
    )
    gain2_part = jnp.sum(d_norm2 * resid * inverse2, axis=0)
    d_resid = out_grad.astype(jnp.float32) + norm_backward(resid, inverse2, norm2_gain, d_norm2)
    d_resid_low = d_resid.astype(jnp.bfloat16)
    grad_out = jnp.dot(mixed.T, d_resid_low, preferred_element_type=jnp.float32)
    d_mixed_rows = jnp.dot(d_resid_low, w_out_full.T, preferred_element_type=jnp.float32)
    d_mixed = to_heads(
        lax.all_to_all(d_mixed_rows.astype(jnp.bfloat16), "mp", 1, 0, tiled=True)
    ).astype(jnp.float32)
    mlp_part, d_mixed = lax.optimization_barrier((mlp_part, d_mixed))
    output = (resid + ring_scatter(mlp_part, "mp")).astype(jnp.bfloat16)
    gate_part = jnp.sum(d_mixed * (mem_out - dot_out), axis=(1, 2)) * gate_vec * (1.0 - gate_vec)
    d_dot = ((1.0 - gate) * d_mixed).astype(jnp.bfloat16)
    d_mem = (gate * d_mixed).reshape(seg_shape)
    dq_dot, dk_dot, dv_dot = attention_bwd(
        query_h, key_h, value_h, d_dot, log_sums, doc_index, score_scale
    )
    d_numer = read_mask[None, :, :, None] * d_mem / denom[..., None]
    d_denom = -jnp.sum(d_numer * numer, axis=-1) / denom * jnp.where(denom_raw > 1.0, 1.0, 0.0)
    d_sig_q = (
        jnp.einsum("hste,shde->hstd", d_numer, read_mem, precision=highest)
        + d_denom[..., None] * read_norm.transpose(1, 0, 2)[:, :, None]
    )
    d_read_mem = jnp.einsum("hstd,hste->shde", sig_q, d_numer, precision=highest)
    d_read_norm = jnp.einsum("hst,hstd->shd", d_denom, sig_q, precision=highest)
    back_mem = cont_flag[:, None, None, None] * d_read_mem
    back_norm = cont_flag[:, None, None] * d_read_norm
    back_summary, _ = lax.scan(
        fold_states, start_state, (keep_flag[:, None], back_mem, back_norm), reverse=True
    )
    grad_in, grad_norm_in = prefix(back_summary, "dp")

    def carry_back(state, item):
        flag, mem_read, norm_read = item
        grad_memory, grad_norm = state
        return (
            (flag * grad_memory + mem_read, flag * grad_norm + norm_read),
            (grad_memory, grad_norm),
        )

    _, (d_carried, d_carried_norm) = lax.scan(
        carry_back, (grad_in, grad_norm_in), (keep_flag, back_mem, back_norm), reverse=True
    )
    write4 = write_mask[None, :, :, None]
    d_sig_k = write4 * (
        jnp.einsum("hste,shde->hstd", value_f, d_carried, precision=highest)
        + d_carried_norm.transpose(1, 0, 2)[:, :, None]
    )
    d_val_mem = write4 * jnp.einsum("hstd,shde->hste", sig_k, d_carried, precision=highest)
    d_query = from_heads(
        dq_dot + (d_sig_q * feature_slope(query_f)).reshape(dq_dot.shape)
    ).astype(jnp.bfloat16)
    d_key = from_heads(
        dk_dot + (d_sig_k * feature_slope(key_f)).reshape(dk_dot.shape)
    ).astype(jnp.bfloat16)
    d_value = from_heads(dv_dot + d_val_mem.reshape(dv_dot.shape)).astype(jnp.bfloat16)
    grad_query = jnp.dot(normed1_all.T, d_query, preferred_element_type=jnp.float32)
    grad_key = jnp.dot(normed1_all.T, d_key, preferred_element_type=jnp.float32)
    grad_value = jnp.dot(normed1_all.T, d_value, preferred_element_type=jnp.float32)
    total_term = jnp.dot(d_query, w_query.T, preferred_element_type=jnp.float32)
    total_term = total_term + jnp.dot(d_key, w_key.T, preferred_element_type=jnp.float32)
    d_norm1 = ring_scatter(
        total_term + jnp.dot(d_value, w_value.T, preferred_element_type=jnp.float32), "mp"
    )
    gain1_part = jnp.sum(d_norm1 * x_rows * inverse1, axis=0)
    input_grad = d_resid + norm_backward(x_rows, inverse1, norm1_gain, d_norm1)
    gate_full = lax.dynamic_update_slice_in_dim(
        jnp.zeros((heads_here * mp_size,), jnp.float32),
        gate_part,
        lax.axis_index("mp") * heads_here,
        0,
    )
    gain1_sum, gain2_sum, gate_sum = lax.psum(
        lax.psum((gain1_part, gain2_part, gate_full), "mp"), "dp"
    )

    def over_dp(grad, dim):
        return lax.psum_scatter(
            grad.astype(jnp.bfloat16), "dp", scatter_dimension=dim, tiled=True
        ).astype(jnp.float32)

    out_sum = lax.psum_scatter(
        over_dp(grad_out, 1).astype(jnp.bfloat16), "mp", scatter_dimension=0, tiled=True
    ).astype(jnp.float32)
    query_sum, key_sum, value_sum, gate_w_sum, up_sum, down_sum = (
        over_dp(grad_query, 0),
        over_dp(grad_key, 0),
        over_dp(grad_value, 0),
        over_dp(grad_gate, 0),
        over_dp(grad_up, 0),
        over_dp(grad_down, 1),
    )
    return (
        output,
        input_grad,
        gain1_sum,
        query_sum,
        key_sum,
        value_sum,
        out_sum,
        gate_sum,
        gain2_sum,
        gate_w_sum,
        up_sum,
        down_sum,
    )


def solution(mesh):
    return jax.shard_map(
        local,
        mesh=mesh,
        in_specs=(
            P(("dp", "mp"), None),
            P(),
            P(None, "mp"),
            P(None, "mp"),
            P(None, "mp"),
            P("mp", None),
            P("mp"),
            P(),
            P(None, "mp"),
            P(None, "mp"),
            P("mp", None),
            P(),
            P(("dp", "mp"), None),
        ),
        out_specs=(
            P(("dp", "mp"), None),
            P(("dp", "mp"), None),
            P(),
            P("dp", "mp"),
            P("dp", "mp"),
            P("dp", "mp"),
            P("mp", "dp"),
            P(),
            P(),
            P("dp", "mp"),
            P("dp", "mp"),
            P("mp", "dp"),
        ),
        check_vma=False,
    )
```

```python
import functools
import math

import jax
import jax.numpy as jnp
from jax import lax
from jax.experimental import pallas as pl
from jax.experimental.pallas import tpu as pltpu
from jax.sharding import PartitionSpec as P


SEG = 2048


eps_norm = 1e-05
highest = lax.Precision.HIGHEST


def gather_states(state, axis, kind):
    flag, memory, norm = state
    heads, size = norm.shape
    packed = jnp.concatenate(
        [memory.reshape(heads * size, size), norm, jnp.broadcast_to(flag.reshape(1, 1), (1, size))],
        axis=0,
    )
    everything = lax.all_gather(packed.astype(kind), axis).astype(jnp.float32)
    return (
        everything[:, heads * size + heads, 0],
        everything[:, : heads * size].reshape((-1, heads, size, size)),
        everything[:, heads * size : heads * size + heads],
    )


def combine_selected(weights, states):
    _, memory, norm = states
    return (
        jnp.sum(weights[:, None, None, None] * memory, axis=0),
        jnp.sum(weights[:, None, None] * norm, axis=0),
    )


def carried_in(value, axis):
    size, place = (lax.axis_size(axis), lax.axis_index(axis))
    states = gather_states(value, axis, jnp.float32)
    flags = states[0]
    k = jnp.arange(size)[:, None]
    j = jnp.arange(size)[None, :]
    factors = jnp.where((j > k) & (j < place), flags[None, :], 1.0)
    weights = jnp.where(jnp.arange(size) < place, jnp.prod(factors, axis=1), 0.0)
    return combine_selected(weights, states)


def prefix(value, axis):
    size, place = (lax.axis_size(axis), lax.axis_index(axis))
    states = gather_states(value, axis, jnp.bfloat16)
    flags = states[0]
    k = jnp.arange(size)[:, None]
    j = jnp.arange(size)[None, :]
    factors = jnp.where((j > place) & (j < k), flags[None, :], 1.0)
    weights = jnp.where(jnp.arange(size) > place, jnp.prod(factors, axis=1), 0.0)
    return combine_selected(weights, states)


def ring_pairs(n, step):
    return [(j, (j + step) % n) for j in range(n)]


def ring_gather(rows, axis, compute):
    n, place = lax.axis_size(axis), lax.axis_index(axis)
    count = rows.shape[0]
    half = count // 2
    own = compute(rows, place * count)
    outs = [
        lax.dynamic_update_slice_in_dim(
            jnp.zeros((n * count,) + part.shape[1:], part.dtype), part, place * count, 0
        )
        for part in own
    ]
    ahead, behind = rows[:half], rows[half:]
    for step in range(1, n):
        ahead = lax.ppermute(ahead, axis, ring_pairs(n, 1))
        behind = lax.ppermute(behind, axis, ring_pairs(n, -1))
        for got, start in (
            (compute(ahead, ((place - step) % n) * count), ((place - step) % n) * count),
            (compute(behind, ((place + step) % n) * count + half), ((place + step) % n) * count + half),
        ):
            outs = [
                lax.dynamic_update_slice_in_dim(out, part, start, 0)
                for out, part in zip(outs, got)
            ]
    return outs


def ring_scatter(partial, axis, kind=jnp.bfloat16):
    n, place = lax.axis_size(axis), lax.axis_index(axis)
    count = partial.shape[0] // n
    half = count // 2

    def chunk(owner, start):
        return lax.dynamic_slice_in_dim(partial, owner * count + start, half, 0).astype(jnp.float32)

    ahead = chunk((place - 1) % n, 0)
    behind = chunk((place + 1) % n, half)
    for step in range(1, n):
        ahead = lax.ppermute(ahead.astype(kind), axis, ring_pairs(n, 1))
        behind = lax.ppermute(behind.astype(kind), axis, ring_pairs(n, -1))
        ahead = ahead.astype(jnp.float32) + chunk((place - 1 - step) % n, 0)
        behind = behind.astype(jnp.float32) + chunk((place + 1 + step) % n, half)
    return jnp.concatenate([ahead, behind], axis=0)


def inverse_rms(values):
    return lax.rsqrt(jnp.mean(values * values, axis=-1, keepdims=True) + eps_norm)


def norm_backward(values, inverse, gain, upstream):
    scaled = upstream * gain
    inner = jnp.mean(values * scaled, axis=-1, keepdims=True)
    return inverse * scaled - values * inverse * inverse * inverse * inner


def feature(values):
    return jnp.where(values > 0, values + 1.0, jnp.exp(jnp.minimum(values, 0.0)))


def feature_slope(values):
    return jnp.where(values > 0, 1.0, jnp.exp(jnp.minimum(values, 0.0)))


def link_states(earlier, later):
    return (
        earlier[0] * later[0],
        later[0] * earlier[1] + later[1],
        later[0] * earlier[2] + later[2],
    )


def fold_states(state, item):
    return (link_states(state, item), None)


def document_ids(doc_lengths, first, count):
    bounds = jnp.cumsum(doc_lengths)
    position = first + jnp.arange(count, dtype=jnp.int32)
    before = jnp.sum((bounds[None, :] <= position[:, None]).astype(jnp.int32), axis=1)
    return jnp.where(position < bounds[-1], before, doc_lengths.shape[0] + position)


NEG = -1e30
BQ = 256


def _mask(qi, docq, dock, seg):
    row = (qi * BQ) % seg + lax.broadcasted_iota(jnp.int32, (BQ, seg), 0)
    col = lax.broadcasted_iota(jnp.int32, (BQ, seg), 1)
    return (col <= row) & (docq == dock)


def _fwd_kernel(scale, seg, q_ref, k_ref, v_ref, docq_ref, dock_ref, o_ref, lse_ref):
    qi = pl.program_id(1)
    q = q_ref[0]
    k = k_ref[0]
    v = v_ref[0]
    s = lax.dot_general(q, k, (((1,), (1,)), ((), ())), preferred_element_type=jnp.float32)
    allowed = _mask(qi, docq_ref[...], dock_ref[...], seg)
    s = jnp.where(allowed, s * scale, NEG)
    m = jnp.max(s, axis=1, keepdims=True)
    e = jnp.exp(s - m)
    l = jnp.sum(e, axis=1, keepdims=True)
    p = (e / l).astype(jnp.bfloat16)
    o_ref[0] = jnp.dot(p, v, preferred_element_type=jnp.float32)
    lse_ref[0] = m + jnp.log(l)


def _bwd_kernel(scale, seg, q_ref, k_ref, v_ref, do_ref, lse_ref, docq_ref, dock_ref,
                dq_ref, dk_ref, dv_ref):
    qi = pl.program_id(1)

    @pl.when((qi * BQ) % seg == 0)
    def _():
        dk_ref[...] = jnp.zeros_like(dk_ref)
        dv_ref[...] = jnp.zeros_like(dv_ref)

    q = q_ref[0]
    k = k_ref[0]
    v = v_ref[0]
    do = do_ref[0]
    s = lax.dot_general(q, k, (((1,), (1,)), ((), ())), preferred_element_type=jnp.float32)
    allowed = _mask(qi, docq_ref[...], dock_ref[...], seg)
    s = jnp.where(allowed, s * scale, NEG)
    p = jnp.exp(s - lse_ref[0])
    dp = lax.dot_general(do, v, (((1,), (1,)), ((), ())), preferred_element_type=jnp.float32)
    delta = jnp.sum(p * dp, axis=1, keepdims=True)
    ds = (p * (dp - delta) * scale).astype(jnp.bfloat16)
    dq_ref[0] = jnp.dot(ds, k, preferred_element_type=jnp.float32)
    dk_ref[0] += lax.dot_general(ds, q, (((0,), (0,)), ((), ())), preferred_element_type=jnp.float32)
    dv_ref[0] += lax.dot_general(p.astype(jnp.bfloat16), do, (((0,), (0,)), ((), ())),
                                 preferred_element_type=jnp.float32)


def attention_fwd(q, k, v, doc, scale):
    H, T, d = q.shape
    seg = min(SEG, T)
    nq = T // BQ
    docq = doc.reshape(T, 1)
    dock = doc.reshape(1, T)
    qspec = pl.BlockSpec((1, BQ, d), lambda h, i: (h, i, 0))
    kspec = pl.BlockSpec((1, seg, d), lambda h, i: (h, i * BQ // seg, 0))
    flops = 4 * H * T * seg * d
    return pl.pallas_call(
        functools.partial(_fwd_kernel, scale, seg),
        grid=(H, nq),
        in_specs=[qspec, kspec, kspec,
                  pl.BlockSpec((BQ, 1), lambda h, i: (i, 0)),
                  pl.BlockSpec((1, seg), lambda h, i: (0, i * BQ // seg))],
        out_specs=[pl.BlockSpec((1, BQ, d), lambda h, i: (h, i, 0)),
                   pl.BlockSpec((1, BQ, 1), lambda h, i: (h, i, 0))],
        out_shape=[jax.ShapeDtypeStruct((H, T, d), jnp.float32),
                   jax.ShapeDtypeStruct((H, T, 1), jnp.float32)],
        compiler_params=pltpu.CompilerParams(dimension_semantics=("arbitrary", "arbitrary")),
        cost_estimate=pl.CostEstimate(flops=flops, transcendentals=H * T * seg,
                                      bytes_accessed=H * T * d * 10),
    )(q, k, v, docq, dock)


def attention_bwd(q, k, v, do, lse, doc, scale):
    H, T, d = q.shape
    seg = min(SEG, T)
    nq = T // BQ
    docq = doc.reshape(T, 1)
    dock = doc.reshape(1, T)
    qspec = pl.BlockSpec((1, BQ, d), lambda h, i: (h, i, 0))
    kspec = pl.BlockSpec((1, seg, d), lambda h, i: (h, i * BQ // seg, 0))
    flops = 10 * H * T * seg * d
    return pl.pallas_call(
        functools.partial(_bwd_kernel, scale, seg),
        grid=(H, nq),
        in_specs=[qspec, kspec, kspec, qspec,
                  pl.BlockSpec((1, BQ, 1), lambda h, i: (h, i, 0)),
                  pl.BlockSpec((BQ, 1), lambda h, i: (i, 0)),
                  pl.BlockSpec((1, seg), lambda h, i: (0, i * BQ // seg))],
        out_specs=[qspec, kspec, kspec],
        out_shape=[jax.ShapeDtypeStruct((H, T, d), jnp.float32)] * 3,
        compiler_params=pltpu.CompilerParams(dimension_semantics=("arbitrary", "arbitrary")),
        cost_estimate=pl.CostEstimate(flops=flops, transcendentals=H * T * seg,
                                      bytes_accessed=H * T * d * 24),
    )(q, k, v, do, lse, docq, dock)


def local(
    tokens,
    norm1_gain,
    w_query,
    w_key,
    w_value,
    w_out,
    gate_logit,
    norm2_gain,
    w_gate,
    w_up,
    w_down,
    doc_lengths,
    out_grad,
):
    heads_here = gate_logit.shape[0]
    head_size = w_query.shape[1] // heads_here
    local_rows = tokens.shape[0]
    mp_size = lax.axis_size("mp")
    dp_size = lax.axis_size("dp")
    group_rows = local_rows * mp_size
    seg_count = group_rows // SEG
    score_scale = 1.0 / math.sqrt(head_size)
    group_first = lax.axis_index("dp") * group_rows
    shifted_ids = document_ids(doc_lengths, group_first - 1, group_rows + 1)
    doc_index = shifted_ids[1:]
    before_doc = jnp.where(group_first > 0, shifted_ids[0], -1)
    seg_docs = doc_index.reshape(seg_count, SEG)
    seg_first = seg_docs[:, 0]
    seg_last = seg_docs[:, -1]
    prev_last = jnp.concatenate([before_doc[None], seg_last[:-1]])
    cont_flag = jnp.where(seg_first == prev_last, 1.0, 0.0).astype(jnp.float32)
    keep_flag = jnp.where(seg_last == prev_last, 1.0, 0.0).astype(jnp.float32)
    read_mask = jnp.where(seg_docs == seg_first[:, None], 1.0, 0.0).astype(jnp.float32)
    write_mask = jnp.where(seg_docs == seg_last[:, None], 1.0, 0.0).astype(jnp.float32)
    width = w_out.shape[1]

    def to_heads(rows):
        return rows.reshape(group_rows, heads_here, head_size).transpose(1, 0, 2)

    def from_heads(heads):
        return heads.transpose(1, 0, 2).reshape(group_rows, heads_here * head_size)

    seg_shape = (heads_here, seg_count, SEG, head_size)
    piece = width // dp_size
    w_out_piece = lax.dynamic_slice_in_dim(w_out, lax.axis_index("dp") * piece, piece, axis=1)
    w_out_full = lax.all_gather(
        lax.all_gather(w_out_piece, "mp", axis=0, tiled=True), "dp", axis=1, tiled=True
    )
    x_rows = tokens.astype(jnp.float32)
    inverse1 = inverse_rms(x_rows)
    normed1 = (x_rows * inverse1 * norm1_gain).astype(jnp.bfloat16)

    def project_qkv(rows, first):
        return (rows,) + tuple(
            jnp.dot(rows, weight, preferred_element_type=jnp.float32).astype(jnp.bfloat16)
            for weight in (w_query, w_key, w_value)
        )

    normed1_all, query_rows, key_rows, value_rows = ring_gather(normed1, "mp", project_qkv)
    query_h, key_h, value_h = (to_heads(a) for a in (query_rows, key_rows, value_rows))
    grad_rows, query_h = lax.optimization_barrier((out_grad, query_h))
    dot_out, log_sums = attention_fwd(query_h, key_h, value_h, doc_index, score_scale)
    query_f = query_h.astype(jnp.float32).reshape(seg_shape)
    key_f = key_h.astype(jnp.float32).reshape(seg_shape)
    value_f = value_h.astype(jnp.float32).reshape(seg_shape)
    sig_q = feature(query_f)
    sig_k = feature(key_f)
    updates = jnp.einsum("st,hstd,hste->shde", write_mask, sig_k, value_f, precision=highest)
    norm_updates = jnp.einsum("st,hstd->shd", write_mask, sig_k, precision=highest)
    start_state = (
        jnp.ones((1,), jnp.float32),
        jnp.zeros(updates.shape[1:], jnp.float32),
        jnp.zeros(norm_updates.shape[1:], jnp.float32),
    )
    summary, _ = lax.scan(fold_states, start_state, (keep_flag[:, None], updates, norm_updates))
    memory_in, norm_in = carried_in(summary, "dp")

    def carry_forward(state, item):
        flag, read_flag, update, norm_update = item
        memory, norm_sum = state
        return (
            (flag * memory + update, flag * norm_sum + norm_update),
            (read_flag * memory, read_flag * norm_sum),
        )

    _, (read_mem, read_norm) = lax.scan(
        carry_forward, (memory_in, norm_in), (keep_flag, cont_flag, updates, norm_updates)
    )
    numer = jnp.einsum("hstd,shde->hste", sig_q, read_mem, precision=highest)
    denom_raw = jnp.einsum("hstd,shd->hst", sig_q, read_norm, precision=highest)
    denom = jnp.maximum(denom_raw, 1.0)
    mem_out = (read_mask[None, :, :, None] * numer / denom[..., None]).reshape(dot_out.shape)
    gate_vec = jax.nn.sigmoid(gate_logit)
    gate = gate_vec[:, None, None]
    mixed_cols = from_heads(gate * mem_out + (1.0 - gate) * dot_out).astype(jnp.bfloat16)
    mixed = lax.all_to_all(mixed_cols, "mp", 0, 1, tiled=True)
    attn_sum = jnp.dot(mixed, w_out_full, preferred_element_type=jnp.float32)
    resid = x_rows + attn_sum
    inverse2 = inverse_rms(resid)
    normed2 = (resid * inverse2 * norm2_gain).astype(jnp.bfloat16)
    (grad_rows_all,) = ring_gather(grad_rows, "mp", lambda rows, first: (rows,))

    def ffn_rows(rows, first):
        grad_rows = lax.dynamic_slice_in_dim(grad_rows_all, first, rows.shape[0], 0)
        gate_f = jnp.dot(rows, w_gate, preferred_element_type=jnp.float32)
        up_f = jnp.dot(rows, w_up, preferred_element_type=jnp.float32)
        gate_f = gate_f.astype(jnp.bfloat16).astype(jnp.float32)
        up_f = up_f.astype(jnp.bfloat16).astype(jnp.float32)
        sig_gate = jax.nn.sigmoid(gate_f)
        act = (gate_f * sig_gate * up_f).astype(jnp.bfloat16)
        d_act = jnp.dot(grad_rows, w_down.T, preferred_element_type=jnp.float32)
        d_gate = (d_act * up_f * sig_gate * (1.0 + gate_f * (1.0 - sig_gate))).astype(jnp.bfloat16)
        d_up = (d_act * gate_f * sig_gate).astype(jnp.bfloat16)
        mlp_rows = jnp.dot(act, w_down, preferred_element_type=jnp.float32)
        norm_rows = jnp.dot(d_gate, w_gate.T, preferred_element_type=jnp.float32) + jnp.dot(
            d_up, w_up.T, preferred_element_type=jnp.float32
        )
        return (rows, act, d_gate, d_up, mlp_rows, norm_rows)

    normed2_all, act, d_gate, d_up, mlp_part, norm2_part = ring_gather(normed2, "mp", ffn_rows)
    norm2_part, normed2_all, act, d_gate, d_up = lax.optimization_barrier(
        (norm2_part, normed2_all, act, d_gate, d_up)
    )
    grad_gate = jnp.dot(normed2_all.T, d_gate, preferred_element_type=jnp.float32)
    grad_up = jnp.dot(normed2_all.T, d_up, preferred_element_type=jnp.float32)
    grad_down = jnp.dot(act.T, grad_rows_all, preferred_element_type=jnp.float32)
    d_norm2 = ring_scatter(norm2_part, "mp")
    gain2_part = jnp.sum(d_norm2 * resid * inverse2, axis=0)
    d_resid = out_grad.astype(jnp.float32) + norm_backward(resid, inverse2, norm2_gain, d_norm2)
    d_resid_low = d_resid.astype(jnp.bfloat16)
    grad_out = jnp.dot(mixed.T, d_resid_low, preferred_element_type=jnp.float32)
    d_mixed_rows = jnp.dot(d_resid_low, w_out_full.T, preferred_element_type=jnp.float32)
    d_mixed = to_heads(
        lax.all_to_all(d_mixed_rows.astype(jnp.bfloat16), "mp", 1, 0, tiled=True)
    ).astype(jnp.float32)
    mlp_part, d_mixed = lax.optimization_barrier((mlp_part, d_mixed))
    output = (resid + ring_scatter(mlp_part, "mp")).astype(jnp.bfloat16)
    gate_part = jnp.sum(d_mixed * (mem_out - dot_out), axis=(1, 2)) * gate_vec * (1.0 - gate_vec)
    d_dot = ((1.0 - gate) * d_mixed).astype(jnp.bfloat16)
    d_mem = (gate * d_mixed).reshape(seg_shape)
    dq_dot, dk_dot, dv_dot = attention_bwd(
        query_h, key_h, value_h, d_dot, log_sums, doc_index, score_scale
    )
    d_numer = read_mask[None, :, :, None] * d_mem / denom[..., None]
    d_denom = -jnp.sum(d_numer * numer, axis=-1) / denom * jnp.where(denom_raw > 1.0, 1.0, 0.0)
    d_sig_q = (
        jnp.einsum("hste,shde->hstd", d_numer, read_mem, precision=highest)
        + d_denom[..., None] * read_norm.transpose(1, 0, 2)[:, :, None]
    )
    d_read_mem = jnp.einsum("hstd,hste->shde", sig_q, d_numer, precision=highest)
    d_read_norm = jnp.einsum("hst,hstd->shd", d_denom, sig_q, precision=highest)
    back_mem = cont_flag[:, None, None, None] * d_read_mem
    back_norm = cont_flag[:, None, None] * d_read_norm
    back_summary, _ = lax.scan(
        fold_states, start_state, (keep_flag[:, None], back_mem, back_norm), reverse=True
    )
    grad_in, grad_norm_in = prefix(back_summary, "dp")

    def carry_back(state, item):
        flag, mem_read, norm_read = item
        grad_memory, grad_norm = state
        return (
            (flag * grad_memory + mem_read, flag * grad_norm + norm_read),
            (grad_memory, grad_norm),
        )

    _, (d_carried, d_carried_norm) = lax.scan(
        carry_back, (grad_in, grad_norm_in), (keep_flag, back_mem, back_norm), reverse=True
    )
    write4 = write_mask[None, :, :, None]
    d_sig_k = write4 * (
        jnp.einsum("hste,shde->hstd", value_f, d_carried, precision=highest)
        + d_carried_norm.transpose(1, 0, 2)[:, :, None]
    )
    d_val_mem = write4 * jnp.einsum("hstd,shde->hste", sig_k, d_carried, precision=highest)
    d_query = from_heads(
        dq_dot + (d_sig_q * feature_slope(query_f)).reshape(dq_dot.shape)
    ).astype(jnp.bfloat16)
    d_key = from_heads(
        dk_dot + (d_sig_k * feature_slope(key_f)).reshape(dk_dot.shape)
    ).astype(jnp.bfloat16)
    d_value = from_heads(dv_dot + d_val_mem.reshape(dv_dot.shape)).astype(jnp.bfloat16)
    grad_query = jnp.dot(normed1_all.T, d_query, preferred_element_type=jnp.float32)
    grad_key = jnp.dot(normed1_all.T, d_key, preferred_element_type=jnp.float32)
    grad_value = jnp.dot(normed1_all.T, d_value, preferred_element_type=jnp.float32)
    total_term = jnp.dot(d_query, w_query.T, preferred_element_type=jnp.float32)
    total_term = total_term + jnp.dot(d_key, w_key.T, preferred_element_type=jnp.float32)
    d_norm1 = ring_scatter(
        total_term + jnp.dot(d_value, w_value.T, preferred_element_type=jnp.float32), "mp"
    )
    gain1_part = jnp.sum(d_norm1 * x_rows * inverse1, axis=0)
    input_grad = d_resid + norm_backward(x_rows, inverse1, norm1_gain, d_norm1)
    gate_full = lax.dynamic_update_slice_in_dim(
        jnp.zeros((heads_here * mp_size,), jnp.float32),
        gate_part,
        lax.axis_index("mp") * heads_here,
        0,
    )
    gain1_sum, gain2_sum, gate_sum = lax.psum(
        lax.psum((gain1_part, gain2_part, gate_full), "mp"), "dp"
    )

    def over_dp(grad, dim):
        return lax.psum_scatter(
            grad.astype(jnp.bfloat16), "dp", scatter_dimension=dim, tiled=True
        ).astype(jnp.float32)

    out_sum = lax.psum_scatter(
        over_dp(grad_out, 1).astype(jnp.bfloat16), "mp", scatter_dimension=0, tiled=True
    ).astype(jnp.float32)
    query_sum, key_sum, value_sum, gate_w_sum, up_sum, down_sum = (
        over_dp(grad_query, 0),
        over_dp(grad_key, 0),
        over_dp(grad_value, 0),
        over_dp(grad_gate, 0),
        over_dp(grad_up, 0),
        over_dp(grad_down, 1),
    )
    return (
        output,
        input_grad,
        gain1_sum,
        query_sum,
        key_sum,
        value_sum,
        out_sum,
        gate_sum,
        gain2_sum,
        gate_w_sum,
        up_sum,
        down_sum,
    )


def solution(mesh):
    return jax.shard_map(
        local,
        mesh=mesh,
        in_specs=(
            P(("dp", "mp"), None),
            P(),
            P(None, "mp"),
            P(None, "mp"),
            P(None, "mp"),
            P("mp", None),
            P("mp"),
            P(),
            P(None, "mp"),
            P(None, "mp"),
            P("mp", None),
            P(),
            P(("dp", "mp"), None),
        ),
        out_specs=(
            P(("dp", "mp"), None),
            P(("dp", "mp"), None),
            P(),
            P("dp", "mp"),
            P("dp", "mp"),
            P("dp", "mp"),
            P("mp", "dp"),
            P(),
            P(),
            P("dp", "mp"),
            P("dp", "mp"),
            P("mp", "dp"),
        ),
        check_vma=False,
    )
```

```python
import functools
import math

import jax
import jax.numpy as jnp
from jax import lax
from jax.experimental import pallas as pl
from jax.experimental.pallas import tpu as pltpu
from jax.sharding import PartitionSpec as P


SEG = 2048


eps_norm = 1e-05
highest = lax.Precision.HIGHEST


def gather_states(state, axis, kind):
    flag, memory, norm = state
    heads, size = norm.shape
    packed = jnp.concatenate(
        [memory.reshape(heads * size, size), norm, jnp.broadcast_to(flag.reshape(1, 1), (1, size))],
        axis=0,
    )
    everything = lax.all_gather(packed.astype(kind), axis).astype(jnp.float32)
    return (
        everything[:, heads * size + heads, 0],
        everything[:, : heads * size].reshape((-1, heads, size, size)),
        everything[:, heads * size : heads * size + heads],
    )


def combine_selected(weights, states):
    _, memory, norm = states
    return (
        jnp.sum(weights[:, None, None, None] * memory, axis=0),
        jnp.sum(weights[:, None, None] * norm, axis=0),
    )


def carried_in(value, axis):
    size, place = (lax.axis_size(axis), lax.axis_index(axis))
    states = gather_states(value, axis, jnp.float32)
    flags = states[0]
    k = jnp.arange(size)[:, None]
    j = jnp.arange(size)[None, :]
    factors = jnp.where((j > k) & (j < place), flags[None, :], 1.0)
    weights = jnp.where(jnp.arange(size) < place, jnp.prod(factors, axis=1), 0.0)
    return combine_selected(weights, states)


def prefix(value, axis):
    size, place = (lax.axis_size(axis), lax.axis_index(axis))
    states = gather_states(value, axis, jnp.bfloat16)
    flags = states[0]
    k = jnp.arange(size)[:, None]
    j = jnp.arange(size)[None, :]
    factors = jnp.where((j > place) & (j < k), flags[None, :], 1.0)
    weights = jnp.where(jnp.arange(size) > place, jnp.prod(factors, axis=1), 0.0)
    return combine_selected(weights, states)


def ring_pairs(n, step):
    return [(j, (j + step) % n) for j in range(n)]


def ring_gather(rows, axis, compute):
    n, place = lax.axis_size(axis), lax.axis_index(axis)
    count = rows.shape[0]
    half = count // 2
    own = compute(rows)
    outs = [
        lax.dynamic_update_slice_in_dim(
            jnp.zeros((n * count,) + part.shape[1:], part.dtype), part, place * count, 0
        )
        for part in own
    ]
    ahead, behind = rows[:half], rows[half:]
    for step in range(1, n):
        ahead = lax.ppermute(ahead, axis, ring_pairs(n, 1))
        behind = lax.ppermute(behind, axis, ring_pairs(n, -1))
        for got, start in (
            (compute(ahead), ((place - step) % n) * count),
            (compute(behind), ((place + step) % n) * count + half),
        ):
            outs = [
                lax.dynamic_update_slice_in_dim(out, part, start, 0)
                for out, part in zip(outs, got)
            ]
    return outs


def ring_scatter(partial, axis, kind=jnp.bfloat16):
    n, place = lax.axis_size(axis), lax.axis_index(axis)
    count = partial.shape[0] // n
    half = count // 2

    def chunk(owner, start):
        return lax.dynamic_slice_in_dim(partial, owner * count + start, half, 0).astype(jnp.float32)

    ahead = chunk((place - 1) % n, 0)
    behind = chunk((place + 1) % n, half)
    for step in range(1, n):
        ahead = lax.ppermute(ahead.astype(kind), axis, ring_pairs(n, 1))
        behind = lax.ppermute(behind.astype(kind), axis, ring_pairs(n, -1))
        ahead = ahead.astype(jnp.float32) + chunk((place - 1 - step) % n, 0)
        behind = behind.astype(jnp.float32) + chunk((place + 1 + step) % n, half)
    return jnp.concatenate([ahead, behind], axis=0)


def inverse_rms(values):
    return lax.rsqrt(jnp.mean(values * values, axis=-1, keepdims=True) + eps_norm)


def norm_backward(values, inverse, gain, upstream):
    scaled = upstream * gain
    inner = jnp.mean(values * scaled, axis=-1, keepdims=True)
    return inverse * scaled - values * inverse * inverse * inverse * inner


def feature(values):
    return jnp.where(values > 0, values + 1.0, jnp.exp(jnp.minimum(values, 0.0)))


def feature_slope(values):
    return jnp.where(values > 0, 1.0, jnp.exp(jnp.minimum(values, 0.0)))


def link_states(earlier, later):
    return (
        earlier[0] * later[0],
        later[0] * earlier[1] + later[1],
        later[0] * earlier[2] + later[2],
    )


def fold_states(state, item):
    return (link_states(state, item), None)


def document_ids(doc_lengths, first, count):
    bounds = jnp.cumsum(doc_lengths)
    position = first + jnp.arange(count, dtype=jnp.int32)
    before = jnp.sum((bounds[None, :] <= position[:, None]).astype(jnp.int32), axis=1)
    return jnp.where(position < bounds[-1], before, doc_lengths.shape[0] + position)


NEG = -1e30
BQ = 256


def _mask(qi, docq, dock, seg):
    row = (qi * BQ) % seg + lax.broadcasted_iota(jnp.int32, (BQ, seg), 0)
    col = lax.broadcasted_iota(jnp.int32, (BQ, seg), 1)
    return (col <= row) & (docq == dock)


def _fwd_kernel(scale, seg, q_ref, k_ref, v_ref, docq_ref, dock_ref, o_ref, lse_ref):
    qi = pl.program_id(1)
    q = q_ref[0]
    k = k_ref[0]
    v = v_ref[0]
    s = lax.dot_general(q, k, (((1,), (1,)), ((), ())), preferred_element_type=jnp.float32)
    allowed = _mask(qi, docq_ref[...], dock_ref[...], seg)
    s = jnp.where(allowed, s * scale, NEG)
    m = jnp.max(s, axis=1, keepdims=True)
    e = jnp.exp(s - m)
    l = jnp.sum(e, axis=1, keepdims=True)
    p = (e / l).astype(jnp.bfloat16)
    o_ref[0] = jnp.dot(p, v, preferred_element_type=jnp.float32)
    lse_ref[0] = m + jnp.log(l)


def _bwd_kernel(scale, seg, q_ref, k_ref, v_ref, do_ref, lse_ref, docq_ref, dock_ref,
                dq_ref, dk_ref, dv_ref):
    qi = pl.program_id(1)

    @pl.when((qi * BQ) % seg == 0)
    def _():
        dk_ref[...] = jnp.zeros_like(dk_ref)
        dv_ref[...] = jnp.zeros_like(dv_ref)

    q = q_ref[0]
    k = k_ref[0]
    v = v_ref[0]
    do = do_ref[0]
    s = lax.dot_general(q, k, (((1,), (1,)), ((), ())), preferred_element_type=jnp.float32)
    allowed = _mask(qi, docq_ref[...], dock_ref[...], seg)
    s = jnp.where(allowed, s * scale, NEG)
    p = jnp.exp(s - lse_ref[0])
    dp = lax.dot_general(do, v, (((1,), (1,)), ((), ())), preferred_element_type=jnp.float32)
    delta = jnp.sum(p * dp, axis=1, keepdims=True)
    ds = (p * (dp - delta) * scale).astype(jnp.bfloat16)
    dq_ref[0] = jnp.dot(ds, k, preferred_element_type=jnp.float32)
    dk_ref[0] += lax.dot_general(ds, q, (((0,), (0,)), ((), ())), preferred_element_type=jnp.float32)
    dv_ref[0] += lax.dot_general(p.astype(jnp.bfloat16), do, (((0,), (0,)), ((), ())),
                                 preferred_element_type=jnp.float32)


def attention_fwd(q, k, v, doc, scale):
    H, T, d = q.shape
    seg = min(SEG, T)
    nq = T // BQ
    docq = doc.reshape(T, 1)
    dock = doc.reshape(1, T)
    qspec = pl.BlockSpec((1, BQ, d), lambda h, i: (h, i, 0))
    kspec = pl.BlockSpec((1, seg, d), lambda h, i: (h, i * BQ // seg, 0))
    flops = 4 * H * T * seg * d
    return pl.pallas_call(
        functools.partial(_fwd_kernel, scale, seg),
        grid=(H, nq),
        in_specs=[qspec, kspec, kspec,
                  pl.BlockSpec((BQ, 1), lambda h, i: (i, 0)),
                  pl.BlockSpec((1, seg), lambda h, i: (0, i * BQ // seg))],
        out_specs=[pl.BlockSpec((1, BQ, d), lambda h, i: (h, i, 0)),
                   pl.BlockSpec((1, BQ, 1), lambda h, i: (h, i, 0))],
        out_shape=[jax.ShapeDtypeStruct((H, T, d), jnp.float32),
                   jax.ShapeDtypeStruct((H, T, 1), jnp.float32)],
        compiler_params=pltpu.CompilerParams(dimension_semantics=("arbitrary", "arbitrary")),
        cost_estimate=pl.CostEstimate(flops=flops, transcendentals=H * T * seg,
                                      bytes_accessed=H * T * d * 10),
    )(q, k, v, docq, dock)


def attention_bwd(q, k, v, do, lse, doc, scale):
    H, T, d = q.shape
    seg = min(SEG, T)
    nq = T // BQ
    docq = doc.reshape(T, 1)
    dock = doc.reshape(1, T)
    qspec = pl.BlockSpec((1, BQ, d), lambda h, i: (h, i, 0))
    kspec = pl.BlockSpec((1, seg, d), lambda h, i: (h, i * BQ // seg, 0))
    flops = 10 * H * T * seg * d
    return pl.pallas_call(
        functools.partial(_bwd_kernel, scale, seg),
        grid=(H, nq),
        in_specs=[qspec, kspec, kspec, qspec,
                  pl.BlockSpec((1, BQ, 1), lambda h, i: (h, i, 0)),
                  pl.BlockSpec((BQ, 1), lambda h, i: (i, 0)),
                  pl.BlockSpec((1, seg), lambda h, i: (0, i * BQ // seg))],
        out_specs=[qspec, kspec, kspec],
        out_shape=[jax.ShapeDtypeStruct((H, T, d), jnp.float32)] * 3,
        compiler_params=pltpu.CompilerParams(dimension_semantics=("arbitrary", "arbitrary")),
        cost_estimate=pl.CostEstimate(flops=flops, transcendentals=H * T * seg,
                                      bytes_accessed=H * T * d * 24),
    )(q, k, v, do, lse, docq, dock)


def local(
    tokens,
    norm1_gain,
    w_query,
    w_key,
    w_value,
    w_out,
    gate_logit,
    norm2_gain,
    w_gate,
    w_up,
    w_down,
    doc_lengths,
    out_grad,
):
    heads_here = gate_logit.shape[0]
    head_size = w_query.shape[1] // heads_here
    local_rows = tokens.shape[0]
    mp_size = lax.axis_size("mp")
    dp_size = lax.axis_size("dp")
    group_rows = local_rows * mp_size
    seg_count = group_rows // SEG
    score_scale = 1.0 / math.sqrt(head_size)
    group_first = lax.axis_index("dp") * group_rows
    shifted_ids = document_ids(doc_lengths, group_first - 1, group_rows + 1)
    doc_index = shifted_ids[1:]
    before_doc = jnp.where(group_first > 0, shifted_ids[0], -1)
    seg_docs = doc_index.reshape(seg_count, SEG)
    seg_first = seg_docs[:, 0]
    seg_last = seg_docs[:, -1]
    prev_last = jnp.concatenate([before_doc[None], seg_last[:-1]])
    cont_flag = jnp.where(seg_first == prev_last, 1.0, 0.0).astype(jnp.float32)
    keep_flag = jnp.where(seg_last == prev_last, 1.0, 0.0).astype(jnp.float32)
    read_mask = jnp.where(seg_docs == seg_first[:, None], 1.0, 0.0).astype(jnp.float32)
    write_mask = jnp.where(seg_docs == seg_last[:, None], 1.0, 0.0).astype(jnp.float32)
    width = w_out.shape[1]

    def over_dp(grad, dim):
        return lax.psum_scatter(
            grad.astype(jnp.bfloat16), "dp", scatter_dimension=dim, tiled=True
        ).astype(jnp.float32)

    def to_heads(rows):
        return rows.reshape(group_rows, heads_here, head_size).transpose(1, 0, 2)

    def from_heads(heads):
        return heads.transpose(1, 0, 2).reshape(group_rows, heads_here * head_size)

    seg_shape = (heads_here, seg_count, SEG, head_size)
    piece = width // dp_size
    w_out_piece = lax.dynamic_slice_in_dim(w_out, lax.axis_index("dp") * piece, piece, axis=1)
    w_out_full = lax.all_gather(
        lax.all_gather(w_out_piece, "mp", axis=0, tiled=True), "dp", axis=1, tiled=True
    )
    x_rows = tokens.astype(jnp.float32)
    inverse1 = inverse_rms(x_rows)
    normed1 = (x_rows * inverse1 * norm1_gain).astype(jnp.bfloat16)

    def project_qkv(rows):
        return (rows,) + tuple(
            jnp.dot(rows, weight, preferred_element_type=jnp.float32).astype(jnp.bfloat16)
            for weight in (w_query, w_key, w_value)
        )

    normed1_all, query_rows, key_rows, value_rows = ring_gather(normed1, "mp", project_qkv)
    query_h, key_h, value_h = (to_heads(a) for a in (query_rows, key_rows, value_rows))
    grad_rows, query_h = lax.optimization_barrier((out_grad, query_h))
    dot_out, log_sums = attention_fwd(query_h, key_h, value_h, doc_index, score_scale)
    query_f = query_h.astype(jnp.float32).reshape(seg_shape)
    key_f = key_h.astype(jnp.float32).reshape(seg_shape)
    value_f = value_h.astype(jnp.float32).reshape(seg_shape)
    sig_q = feature(query_f)
    sig_k = feature(key_f)
    updates = jnp.einsum("st,hstd,hste->shde", write_mask, sig_k, value_f, precision=highest)
    norm_updates = jnp.einsum("st,hstd->shd", write_mask, sig_k, precision=highest)
    start_state = (
        jnp.ones((1,), jnp.float32),
        jnp.zeros(updates.shape[1:], jnp.float32),
        jnp.zeros(norm_updates.shape[1:], jnp.float32),
    )
    summary, _ = lax.scan(fold_states, start_state, (keep_flag[:, None], updates, norm_updates))
    memory_in, norm_in = carried_in(summary, "dp")

    def carry_forward(state, item):
        flag, read_flag, update, norm_update = item
        memory, norm_sum = state
        return (
            (flag * memory + update, flag * norm_sum + norm_update),
            (read_flag * memory, read_flag * norm_sum),
        )

    _, (read_mem, read_norm) = lax.scan(
        carry_forward, (memory_in, norm_in), (keep_flag, cont_flag, updates, norm_updates)
    )
    numer = jnp.einsum("hstd,shde->hste", sig_q, read_mem, precision=highest)
    denom_raw = jnp.einsum("hstd,shd->hst", sig_q, read_norm, precision=highest)
    denom = jnp.maximum(denom_raw, 1.0)
    mem_out = (read_mask[None, :, :, None] * numer / denom[..., None]).reshape(dot_out.shape)
    gate_vec = jax.nn.sigmoid(gate_logit)
    gate = gate_vec[:, None, None]
    mixed_cols = from_heads(gate * mem_out + (1.0 - gate) * dot_out).astype(jnp.bfloat16)
    mixed = lax.all_to_all(mixed_cols, "mp", 0, 1, tiled=True)
    attn_sum = jnp.dot(mixed, w_out_full, preferred_element_type=jnp.float32)
    resid = x_rows + attn_sum
    inverse2 = inverse_rms(resid)
    normed2 = (resid * inverse2 * norm2_gain).astype(jnp.bfloat16)

    def project_ffn(rows):
        return (rows,) + tuple(
            jnp.dot(rows, weight, preferred_element_type=jnp.float32).astype(jnp.bfloat16)
            for weight in (w_gate, w_up)
        )

    normed2_all, gate_pre, up_pre = ring_gather(normed2, "mp", project_ffn)
    gate_f = gate_pre.astype(jnp.float32)
    up_f = up_pre.astype(jnp.float32)
    sig_gate = jax.nn.sigmoid(gate_f)
    act = (gate_f * sig_gate * up_f).astype(jnp.bfloat16)
    mlp_part = jnp.dot(act, w_down, preferred_element_type=jnp.float32)
    (grad_rows_all,) = ring_gather(grad_rows, "mp", lambda rows: (rows,))
    d_act = jnp.dot(grad_rows_all, w_down.T, preferred_element_type=jnp.float32)
    d_gate = (d_act * up_f * sig_gate * (1.0 + gate_f * (1.0 - sig_gate))).astype(jnp.bfloat16)
    d_up = (d_act * gate_f * sig_gate).astype(jnp.bfloat16)
    norm2_part = jnp.dot(d_gate, w_gate.T, preferred_element_type=jnp.float32) + jnp.dot(
        d_up, w_up.T, preferred_element_type=jnp.float32
    )
    norm2_part, normed2_all, act, d_gate, d_up = lax.optimization_barrier(
        (norm2_part, normed2_all, act, d_gate, d_up)
    )
    grad_gate = jnp.dot(normed2_all.T, d_gate, preferred_element_type=jnp.float32)
    grad_up = jnp.dot(normed2_all.T, d_up, preferred_element_type=jnp.float32)
    grad_down = jnp.dot(act.T, grad_rows_all, preferred_element_type=jnp.float32)
    d_norm2 = ring_scatter(norm2_part, "mp")
    gate_w_sum = over_dp(grad_gate, 0)
    up_sum = over_dp(grad_up, 0)
    down_sum = over_dp(grad_down, 1)
    gain2_part = jnp.sum(d_norm2 * resid * inverse2, axis=0)
    d_resid = out_grad.astype(jnp.float32) + norm_backward(resid, inverse2, norm2_gain, d_norm2)
    d_resid_low = d_resid.astype(jnp.bfloat16)
    grad_out = jnp.dot(mixed.T, d_resid_low, preferred_element_type=jnp.float32)
    out_sum = lax.psum_scatter(
        over_dp(grad_out, 1).astype(jnp.bfloat16), "mp", scatter_dimension=0, tiled=True
    ).astype(jnp.float32)
    d_mixed_rows = jnp.dot(d_resid_low, w_out_full.T, preferred_element_type=jnp.float32)
    d_mixed = to_heads(
        lax.all_to_all(d_mixed_rows.astype(jnp.bfloat16), "mp", 1, 0, tiled=True)
    ).astype(jnp.float32)
    mlp_part, d_mixed, gate_w_sum, up_sum = lax.optimization_barrier(
        (mlp_part, d_mixed, gate_w_sum, up_sum)
    )
    output = (resid + ring_scatter(mlp_part, "mp")).astype(jnp.bfloat16)
    gate_part = jnp.sum(d_mixed * (mem_out - dot_out), axis=(1, 2)) * gate_vec * (1.0 - gate_vec)
    d_dot = ((1.0 - gate) * d_mixed).astype(jnp.bfloat16)
    d_mem = (gate * d_mixed).reshape(seg_shape)
    dq_dot, dk_dot, dv_dot = attention_bwd(
        query_h, key_h, value_h, d_dot, log_sums, doc_index, score_scale
    )
    dq_dot, down_sum, out_sum = lax.optimization_barrier((dq_dot, down_sum, out_sum))
    d_numer = read_mask[None, :, :, None] * d_mem / denom[..., None]
    d_denom = -jnp.sum(d_numer * numer, axis=-1) / denom * jnp.where(denom_raw > 1.0, 1.0, 0.0)
    d_sig_q = (
        jnp.einsum("hste,shde->hstd", d_numer, read_mem, precision=highest)
        + d_denom[..., None] * read_norm.transpose(1, 0, 2)[:, :, None]
    )
    d_read_mem = jnp.einsum("hstd,hste->shde", sig_q, d_numer, precision=highest)
    d_read_norm = jnp.einsum("hst,hstd->shd", d_denom, sig_q, precision=highest)
    back_mem = cont_flag[:, None, None, None] * d_read_mem
    back_norm = cont_flag[:, None, None] * d_read_norm
    back_summary, _ = lax.scan(
        fold_states, start_state, (keep_flag[:, None], back_mem, back_norm), reverse=True
    )
    grad_in, grad_norm_in = prefix(back_summary, "dp")

    def carry_back(state, item):
        flag, mem_read, norm_read = item
        grad_memory, grad_norm = state
        return (
            (flag * grad_memory + mem_read, flag * grad_norm + norm_read),
            (grad_memory, grad_norm),
        )

    _, (d_carried, d_carried_norm) = lax.scan(
        carry_back, (grad_in, grad_norm_in), (keep_flag, back_mem, back_norm), reverse=True
    )
    write4 = write_mask[None, :, :, None]
    d_sig_k = write4 * (
        jnp.einsum("hste,shde->hstd", value_f, d_carried, precision=highest)
        + d_carried_norm.transpose(1, 0, 2)[:, :, None]
    )
    d_val_mem = write4 * jnp.einsum("hstd,shde->hste", sig_k, d_carried, precision=highest)
    d_query = from_heads(
        dq_dot + (d_sig_q * feature_slope(query_f)).reshape(dq_dot.shape)
    ).astype(jnp.bfloat16)
    d_key = from_heads(
        dk_dot + (d_sig_k * feature_slope(key_f)).reshape(dk_dot.shape)
    ).astype(jnp.bfloat16)
    d_value = from_heads(dv_dot + d_val_mem.reshape(dv_dot.shape)).astype(jnp.bfloat16)
    grad_query = jnp.dot(normed1_all.T, d_query, preferred_element_type=jnp.float32)
    grad_key = jnp.dot(normed1_all.T, d_key, preferred_element_type=jnp.float32)
    grad_value = jnp.dot(normed1_all.T, d_value, preferred_element_type=jnp.float32)
    total_term = jnp.dot(d_query, w_query.T, preferred_element_type=jnp.float32)
    total_term = total_term + jnp.dot(d_key, w_key.T, preferred_element_type=jnp.float32)
    d_norm1 = ring_scatter(
        total_term + jnp.dot(d_value, w_value.T, preferred_element_type=jnp.float32), "mp"
    )
    gain1_part = jnp.sum(d_norm1 * x_rows * inverse1, axis=0)
    input_grad = d_resid + norm_backward(x_rows, inverse1, norm1_gain, d_norm1)
    gate_full = lax.dynamic_update_slice_in_dim(
        jnp.zeros((heads_here * mp_size,), jnp.float32),
        gate_part,
        lax.axis_index("mp") * heads_here,
        0,
    )
    gain1_sum, gain2_sum, gate_sum = lax.psum(
        lax.psum((gain1_part, gain2_part, gate_full), "mp"), "dp"
    )

    qkv_sum = over_dp(jnp.concatenate([grad_query, grad_key, grad_value], axis=1), 0)
    query_sum, key_sum, value_sum = jnp.split(qkv_sum, 3, axis=1)
    return (
        output,
        input_grad,
        gain1_sum,
        query_sum,
        key_sum,
        value_sum,
        out_sum,
        gate_sum,
        gain2_sum,
        gate_w_sum,
        up_sum,
        down_sum,
    )


def solution(mesh):
    return jax.shard_map(
        local,
        mesh=mesh,
        in_specs=(
            P(("dp", "mp"), None),
            P(),
            P(None, "mp"),
            P(None, "mp"),
            P(None, "mp"),
            P("mp", None),
            P("mp"),
            P(),
            P(None, "mp"),
            P(None, "mp"),
            P("mp", None),
            P(),
            P(("dp", "mp"), None),
        ),
        out_specs=(
            P(("dp", "mp"), None),
            P(("dp", "mp"), None),
            P(),
            P("dp", "mp"),
            P("dp", "mp"),
            P("dp", "mp"),
            P("mp", "dp"),
            P(),
            P(),
            P("dp", "mp"),
            P("dp", "mp"),
            P("mp", "dp"),
        ),
        check_vma=False,
    )
```

```python
import functools
import math

import jax
import jax.numpy as jnp
from jax import lax
from jax.experimental import pallas as pl
from jax.experimental.pallas import tpu as pltpu
from jax.sharding import PartitionSpec as P


SEG = 2048


eps_norm = 1e-05
highest = lax.Precision.HIGHEST


def gather_states(state, axis, kind):
    flag, memory, norm = state
    heads, size = norm.shape
    packed = jnp.concatenate(
        [memory.reshape(heads * size, size), norm, jnp.broadcast_to(flag.reshape(1, 1), (1, size))],
        axis=0,
    )
    everything = lax.all_gather(packed.astype(kind), axis).astype(jnp.float32)
    return (
        everything[:, heads * size + heads, 0],
        everything[:, : heads * size].reshape((-1, heads, size, size)),
        everything[:, heads * size : heads * size + heads],
    )


def combine_selected(weights, states):
    _, memory, norm = states
    return (
        jnp.sum(weights[:, None, None, None] * memory, axis=0),
        jnp.sum(weights[:, None, None] * norm, axis=0),
    )


def carried_in(value, axis):
    size, place = (lax.axis_size(axis), lax.axis_index(axis))
    states = gather_states(value, axis, jnp.float32)
    flags = states[0]
    k = jnp.arange(size)[:, None]
    j = jnp.arange(size)[None, :]
    factors = jnp.where((j > k) & (j < place), flags[None, :], 1.0)
    weights = jnp.where(jnp.arange(size) < place, jnp.prod(factors, axis=1), 0.0)
    return combine_selected(weights, states)


def prefix(value, axis):
    size, place = (lax.axis_size(axis), lax.axis_index(axis))
    states = gather_states(value, axis, jnp.bfloat16)
    flags = states[0]
    k = jnp.arange(size)[:, None]
    j = jnp.arange(size)[None, :]
    factors = jnp.where((j > place) & (j < k), flags[None, :], 1.0)
    weights = jnp.where(jnp.arange(size) > place, jnp.prod(factors, axis=1), 0.0)
    return combine_selected(weights, states)


def tree_sum(value, axis):
    n = lax.axis_size(axis)
    step = 1
    while step < n:
        value = value + lax.ppermute(value, axis, [(j, j ^ step) for j in range(n)])
        step *= 2
    return value


def ring_pairs(n, step):
    return [(j, (j + step) % n) for j in range(n)]


def ring_gather(rows, axis, compute):
    n, place = lax.axis_size(axis), lax.axis_index(axis)
    count = rows.shape[0]
    half = count // 2
    own = compute(rows)
    outs = [
        lax.dynamic_update_slice_in_dim(
            jnp.zeros((n * count,) + part.shape[1:], part.dtype), part, place * count, 0
        )
        for part in own
    ]
    ahead, behind = rows[:half], rows[half:]
    for step in range(1, n):
        ahead = lax.ppermute(ahead, axis, ring_pairs(n, 1))
        behind = lax.ppermute(behind, axis, ring_pairs(n, -1))
        for got, start in (
            (compute(ahead), ((place - step) % n) * count),
            (compute(behind), ((place + step) % n) * count + half),
        ):
            outs = [
                lax.dynamic_update_slice_in_dim(out, part, start, 0)
                for out, part in zip(outs, got)
            ]
    return outs


def ring_scatter(partial, axis, kind=jnp.bfloat16):
    n, place = lax.axis_size(axis), lax.axis_index(axis)
    count = partial.shape[0] // n
    half = count // 2

    def chunk(owner, start):
        return lax.dynamic_slice_in_dim(partial, owner * count + start, half, 0).astype(jnp.float32)

    ahead = chunk((place - 1) % n, 0)
    behind = chunk((place + 1) % n, half)
    for step in range(1, n):
        ahead = lax.ppermute(ahead.astype(kind), axis, ring_pairs(n, 1))
        behind = lax.ppermute(behind.astype(kind), axis, ring_pairs(n, -1))
        ahead = ahead.astype(jnp.float32) + chunk((place - 1 - step) % n, 0)
        behind = behind.astype(jnp.float32) + chunk((place + 1 + step) % n, half)
    return jnp.concatenate([ahead, behind], axis=0)


def inverse_rms(values):
    return lax.rsqrt(jnp.mean(values * values, axis=-1, keepdims=True) + eps_norm)


def norm_backward(values, inverse, gain, upstream):
    scaled = upstream * gain
    inner = jnp.mean(values * scaled, axis=-1, keepdims=True)
    return inverse * scaled - values * inverse * inverse * inverse * inner


def feature(values):
    return jnp.where(values > 0, values + 1.0, jnp.exp(jnp.minimum(values, 0.0)))


def feature_slope(values):
    return jnp.where(values > 0, 1.0, jnp.exp(jnp.minimum(values, 0.0)))


def link_states(earlier, later):
    return (
        earlier[0] * later[0],
        later[0] * earlier[1] + later[1],
        later[0] * earlier[2] + later[2],
    )


def fold_states(state, item):
    return (link_states(state, item), None)


def document_ids(doc_lengths, first, count):
    bounds = jnp.cumsum(doc_lengths)
    position = first + jnp.arange(count, dtype=jnp.int32)
    before = jnp.sum((bounds[None, :] <= position[:, None]).astype(jnp.int32), axis=1)
    return jnp.where(position < bounds[-1], before, doc_lengths.shape[0] + position)


NEG = -1e30
BQ = 256


def _mask(qi, docq, dock, seg):
    row = (qi * BQ) % seg + lax.broadcasted_iota(jnp.int32, (BQ, seg), 0)
    col = lax.broadcasted_iota(jnp.int32, (BQ, seg), 1)
    return (col <= row) & (docq == dock)


def _fwd_kernel(scale, seg, q_ref, k_ref, v_ref, docq_ref, dock_ref, o_ref, lse_ref):
    qi = pl.program_id(1)
    q = q_ref[0]
    k = k_ref[0]
    v = v_ref[0]
    s = lax.dot_general(q, k, (((1,), (1,)), ((), ())), preferred_element_type=jnp.float32)
    allowed = _mask(qi, docq_ref[...], dock_ref[...], seg)
    s = jnp.where(allowed, s * scale, NEG)
    m = jnp.max(s, axis=1, keepdims=True)
    e = jnp.exp(s - m)
    l = jnp.sum(e, axis=1, keepdims=True)
    p = (e / l).astype(jnp.bfloat16)
    o_ref[0] = jnp.dot(p, v, preferred_element_type=jnp.float32)
    lse_ref[0] = m + jnp.log(l)


def _bwd_kernel(scale, seg, q_ref, k_ref, v_ref, do_ref, lse_ref, docq_ref, dock_ref,
                dq_ref, dk_ref, dv_ref):
    qi = pl.program_id(1)

    @pl.when((qi * BQ) % seg == 0)
    def _():
        dk_ref[...] = jnp.zeros_like(dk_ref)
        dv_ref[...] = jnp.zeros_like(dv_ref)

    q = q_ref[0]
    k = k_ref[0]
    v = v_ref[0]
    do = do_ref[0]
    s = lax.dot_general(q, k, (((1,), (1,)), ((), ())), preferred_element_type=jnp.float32)
    allowed = _mask(qi, docq_ref[...], dock_ref[...], seg)
    s = jnp.where(allowed, s * scale, NEG)
    p = jnp.exp(s - lse_ref[0])
    dp = lax.dot_general(do, v, (((1,), (1,)), ((), ())), preferred_element_type=jnp.float32)
    delta = jnp.sum(p * dp, axis=1, keepdims=True)
    ds = (p * (dp - delta) * scale).astype(jnp.bfloat16)
    dq_ref[0] = jnp.dot(ds, k, preferred_element_type=jnp.float32)
    dk_ref[0] += lax.dot_general(ds, q, (((0,), (0,)), ((), ())), preferred_element_type=jnp.float32)
    dv_ref[0] += lax.dot_general(p.astype(jnp.bfloat16), do, (((0,), (0,)), ((), ())),
                                 preferred_element_type=jnp.float32)


def attention_fwd(q, k, v, doc, scale):
    H, T, d = q.shape
    seg = min(SEG, T)
    nq = T // BQ
    docq = doc.reshape(T, 1)
    dock = doc.reshape(1, T)
    qspec = pl.BlockSpec((1, BQ, d), lambda h, i: (h, i, 0))
    kspec = pl.BlockSpec((1, seg, d), lambda h, i: (h, i * BQ // seg, 0))
    flops = 4 * H * T * seg * d
    return pl.pallas_call(
        functools.partial(_fwd_kernel, scale, seg),
        grid=(H, nq),
        in_specs=[qspec, kspec, kspec,
                  pl.BlockSpec((BQ, 1), lambda h, i: (i, 0)),
                  pl.BlockSpec((1, seg), lambda h, i: (0, i * BQ // seg))],
        out_specs=[pl.BlockSpec((1, BQ, d), lambda h, i: (h, i, 0)),
                   pl.BlockSpec((1, BQ, 1), lambda h, i: (h, i, 0))],
        out_shape=[jax.ShapeDtypeStruct((H, T, d), jnp.float32),
                   jax.ShapeDtypeStruct((H, T, 1), jnp.float32)],
        compiler_params=pltpu.CompilerParams(dimension_semantics=("arbitrary", "arbitrary")),
        cost_estimate=pl.CostEstimate(flops=flops, transcendentals=H * T * seg,
                                      bytes_accessed=H * T * d * 10),
    )(q, k, v, docq, dock)


def attention_bwd(q, k, v, do, lse, doc, scale):
    H, T, d = q.shape
    seg = min(SEG, T)
    nq = T // BQ
    docq = doc.reshape(T, 1)
    dock = doc.reshape(1, T)
    qspec = pl.BlockSpec((1, BQ, d), lambda h, i: (h, i, 0))
    kspec = pl.BlockSpec((1, seg, d), lambda h, i: (h, i * BQ // seg, 0))
    flops = 10 * H * T * seg * d
    return pl.pallas_call(
        functools.partial(_bwd_kernel, scale, seg),
        grid=(H, nq),
        in_specs=[qspec, kspec, kspec, qspec,
                  pl.BlockSpec((1, BQ, 1), lambda h, i: (h, i, 0)),
                  pl.BlockSpec((BQ, 1), lambda h, i: (i, 0)),
                  pl.BlockSpec((1, seg), lambda h, i: (0, i * BQ // seg))],
        out_specs=[qspec, kspec, kspec],
        out_shape=[jax.ShapeDtypeStruct((H, T, d), jnp.float32)] * 3,
        compiler_params=pltpu.CompilerParams(dimension_semantics=("arbitrary", "arbitrary")),
        cost_estimate=pl.CostEstimate(flops=flops, transcendentals=H * T * seg,
                                      bytes_accessed=H * T * d * 24),
    )(q, k, v, do, lse, docq, dock)


def local(
    tokens,
    norm1_gain,
    w_query,
    w_key,
    w_value,
    w_out,
    gate_logit,
    norm2_gain,
    w_gate,
    w_up,
    w_down,
    doc_lengths,
    out_grad,
):
    heads_here = gate_logit.shape[0]
    head_size = w_query.shape[1] // heads_here
    local_rows = tokens.shape[0]
    mp_size = lax.axis_size("mp")
    dp_size = lax.axis_size("dp")
    group_rows = local_rows * mp_size
    seg_count = group_rows // SEG
    score_scale = 1.0 / math.sqrt(head_size)
    group_first = lax.axis_index("dp") * group_rows
    shifted_ids = document_ids(doc_lengths, group_first - 1, group_rows + 1)
    doc_index = shifted_ids[1:]
    before_doc = jnp.where(group_first > 0, shifted_ids[0], -1)
    seg_docs = doc_index.reshape(seg_count, SEG)
    seg_first = seg_docs[:, 0]
    seg_last = seg_docs[:, -1]
    prev_last = jnp.concatenate([before_doc[None], seg_last[:-1]])
    cont_flag = jnp.where(seg_first == prev_last, 1.0, 0.0).astype(jnp.float32)
    keep_flag = jnp.where(seg_last == prev_last, 1.0, 0.0).astype(jnp.float32)
    read_mask = jnp.where(seg_docs == seg_first[:, None], 1.0, 0.0).astype(jnp.float32)
    write_mask = jnp.where(seg_docs == seg_last[:, None], 1.0, 0.0).astype(jnp.float32)
    width = w_out.shape[1]

    def over_dp(grad, dim):
        return lax.psum_scatter(
            grad.astype(jnp.bfloat16), "dp", scatter_dimension=dim, tiled=True
        ).astype(jnp.float32)

    def to_heads(rows):
        return rows.reshape(group_rows, heads_here, head_size).transpose(1, 0, 2)

    def from_heads(heads):
        return heads.transpose(1, 0, 2).reshape(group_rows, heads_here * head_size)

    seg_shape = (heads_here, seg_count, SEG, head_size)
    piece = width // dp_size
    w_out_piece = lax.dynamic_slice_in_dim(w_out, lax.axis_index("dp") * piece, piece, axis=1)
    w_out_full = lax.all_gather(
        lax.all_gather(w_out_piece, "mp", axis=0, tiled=True), "dp", axis=1, tiled=True
    )
    x_rows = tokens.astype(jnp.float32)
    inverse1 = inverse_rms(x_rows)
    normed1 = (x_rows * inverse1 * norm1_gain).astype(jnp.bfloat16)

    def project_qkv(rows):
        return (rows,) + tuple(
            jnp.dot(rows, weight, preferred_element_type=jnp.float32).astype(jnp.bfloat16)
            for weight in (w_query, w_key, w_value)
        )

    normed1_all, query_rows, key_rows, value_rows = ring_gather(normed1, "mp", project_qkv)
    query_h, key_h, value_h = (to_heads(a) for a in (query_rows, key_rows, value_rows))
    grad_rows, query_h = lax.optimization_barrier((out_grad, query_h))
    dot_out, log_sums = attention_fwd(query_h, key_h, value_h, doc_index, score_scale)
    query_f = query_h.astype(jnp.float32).reshape(seg_shape)
    key_f = key_h.astype(jnp.float32).reshape(seg_shape)
    value_f = value_h.astype(jnp.float32).reshape(seg_shape)
    sig_q = feature(query_f)
    sig_k = feature(key_f)
    updates = jnp.einsum("st,hstd,hste->shde", write_mask, sig_k, value_f, precision=highest)
    norm_updates = jnp.einsum("st,hstd->shd", write_mask, sig_k, precision=highest)
    start_state = (
        jnp.ones((1,), jnp.float32),
        jnp.zeros(updates.shape[1:], jnp.float32),
        jnp.zeros(norm_updates.shape[1:], jnp.float32),
    )
    summary, _ = lax.scan(fold_states, start_state, (keep_flag[:, None], updates, norm_updates))
    memory_in, norm_in = carried_in(summary, "dp")

    def carry_forward(state, item):
        flag, read_flag, update, norm_update = item
        memory, norm_sum = state
        return (
            (flag * memory + update, flag * norm_sum + norm_update),
            (read_flag * memory, read_flag * norm_sum),
        )

    _, (read_mem, read_norm) = lax.scan(
        carry_forward, (memory_in, norm_in), (keep_flag, cont_flag, updates, norm_updates)
    )
    numer = jnp.einsum("hstd,shde->hste", sig_q, read_mem, precision=highest)
    denom_raw = jnp.einsum("hstd,shd->hst", sig_q, read_norm, precision=highest)
    denom = jnp.maximum(denom_raw, 1.0)
    mem_out = (read_mask[None, :, :, None] * numer / denom[..., None]).reshape(dot_out.shape)
    gate_vec = jax.nn.sigmoid(gate_logit)
    gate = gate_vec[:, None, None]
    mixed_cols = from_heads(gate * mem_out + (1.0 - gate) * dot_out).astype(jnp.bfloat16)
    mixed = lax.all_to_all(mixed_cols, "mp", 0, 1, tiled=True)
    attn_sum = jnp.dot(mixed, w_out_full, preferred_element_type=jnp.float32)
    resid = x_rows + attn_sum
    inverse2 = inverse_rms(resid)
    normed2 = (resid * inverse2 * norm2_gain).astype(jnp.bfloat16)

    def project_ffn(rows):
        return (rows,) + tuple(
            jnp.dot(rows, weight, preferred_element_type=jnp.float32).astype(jnp.bfloat16)
            for weight in (w_gate, w_up)
        )

    normed2_all, gate_pre, up_pre = ring_gather(normed2, "mp", project_ffn)
    gate_f = gate_pre.astype(jnp.float32)
    up_f = up_pre.astype(jnp.float32)
    sig_gate = jax.nn.sigmoid(gate_f)
    act = (gate_f * sig_gate * up_f).astype(jnp.bfloat16)
    mlp_part = jnp.dot(act, w_down, preferred_element_type=jnp.float32)
    (grad_rows_all,) = ring_gather(grad_rows, "mp", lambda rows: (rows,))
    d_act = lax.optimization_barrier(
        jnp.dot(grad_rows_all, w_down.T, preferred_element_type=jnp.float32)
    )
    d_gate = (d_act * up_f * sig_gate * (1.0 + gate_f * (1.0 - sig_gate))).astype(jnp.bfloat16)
    d_up = (d_act * gate_f * sig_gate).astype(jnp.bfloat16)
    norm2_part = jnp.dot(d_gate, w_gate.T, preferred_element_type=jnp.float32) + jnp.dot(
        d_up, w_up.T, preferred_element_type=jnp.float32
    )
    norm2_part, normed2_all, act, d_gate, d_up = lax.optimization_barrier(
        (norm2_part, normed2_all, act, d_gate, d_up)
    )
    grad_gate = jnp.dot(normed2_all.T, d_gate, preferred_element_type=jnp.float32)
    grad_up = jnp.dot(normed2_all.T, d_up, preferred_element_type=jnp.float32)
    grad_down = jnp.dot(act.T, grad_rows_all, preferred_element_type=jnp.float32)
    d_norm2 = ring_scatter(norm2_part, "mp")
    gate_w_sum = over_dp(grad_gate, 0)
    up_sum = over_dp(grad_up, 0)
    down_sum = over_dp(grad_down, 1)
    gain2_part = jnp.sum(d_norm2 * resid * inverse2, axis=0)
    d_resid = out_grad.astype(jnp.float32) + norm_backward(resid, inverse2, norm2_gain, d_norm2)
    d_resid_low = d_resid.astype(jnp.bfloat16)
    grad_out = jnp.dot(mixed.T, d_resid_low, preferred_element_type=jnp.float32)
    out_sum = lax.psum_scatter(
        over_dp(grad_out, 1).astype(jnp.bfloat16), "mp", scatter_dimension=0, tiled=True
    ).astype(jnp.float32)
    d_mixed_rows = jnp.dot(d_resid_low, w_out_full.T, preferred_element_type=jnp.float32)
    d_mixed = to_heads(
        lax.all_to_all(d_mixed_rows.astype(jnp.bfloat16), "mp", 1, 0, tiled=True)
    ).astype(jnp.float32)
    mlp_part, d_mixed, gate_w_sum, up_sum = lax.optimization_barrier(
        (mlp_part, d_mixed, gate_w_sum, up_sum)
    )
    output = (resid + ring_scatter(mlp_part, "mp")).astype(jnp.bfloat16)
    gate_part = jnp.sum(d_mixed * (mem_out - dot_out), axis=(1, 2)) * gate_vec * (1.0 - gate_vec)
    d_dot = ((1.0 - gate) * d_mixed).astype(jnp.bfloat16)
    d_mem = (gate * d_mixed).reshape(seg_shape)
    dq_dot, dk_dot, dv_dot = attention_bwd(
        query_h, key_h, value_h, d_dot, log_sums, doc_index, score_scale
    )
    dq_dot, down_sum, out_sum = lax.optimization_barrier((dq_dot, down_sum, out_sum))
    d_numer = read_mask[None, :, :, None] * d_mem / denom[..., None]
    d_denom = -jnp.sum(d_numer * numer, axis=-1) / denom * jnp.where(denom_raw > 1.0, 1.0, 0.0)
    d_sig_q = (
        jnp.einsum("hste,shde->hstd", d_numer, read_mem, precision=highest)
        + d_denom[..., None] * read_norm.transpose(1, 0, 2)[:, :, None]
    )
    d_read_mem = jnp.einsum("hstd,hste->shde", sig_q, d_numer, precision=highest)
    d_read_norm = jnp.einsum("hst,hstd->shd", d_denom, sig_q, precision=highest)
    back_mem = cont_flag[:, None, None, None] * d_read_mem
    back_norm = cont_flag[:, None, None] * d_read_norm
    back_summary, _ = lax.scan(
        fold_states, start_state, (keep_flag[:, None], back_mem, back_norm), reverse=True
    )
    grad_in, grad_norm_in = prefix(back_summary, "dp")

    def carry_back(state, item):
        flag, mem_read, norm_read = item
        grad_memory, grad_norm = state
        return (
            (flag * grad_memory + mem_read, flag * grad_norm + norm_read),
            (grad_memory, grad_norm),
        )

    _, (d_carried, d_carried_norm) = lax.scan(
        carry_back, (grad_in, grad_norm_in), (keep_flag, back_mem, back_norm), reverse=True
    )
    write4 = write_mask[None, :, :, None]
    d_sig_k = write4 * (
        jnp.einsum("hste,shde->hstd", value_f, d_carried, precision=highest)
        + d_carried_norm.transpose(1, 0, 2)[:, :, None]
    )
    d_val_mem = write4 * jnp.einsum("hstd,shde->hste", sig_k, d_carried, precision=highest)
    d_query = from_heads(
        dq_dot + (d_sig_q * feature_slope(query_f)).reshape(dq_dot.shape)
    ).astype(jnp.bfloat16)
    d_key = from_heads(
        dk_dot + (d_sig_k * feature_slope(key_f)).reshape(dk_dot.shape)
    ).astype(jnp.bfloat16)
    d_value = from_heads(dv_dot + d_val_mem.reshape(dv_dot.shape)).astype(jnp.bfloat16)
    grad_query = jnp.dot(normed1_all.T, d_query, preferred_element_type=jnp.float32)
    grad_key = jnp.dot(normed1_all.T, d_key, preferred_element_type=jnp.float32)
    grad_value = jnp.dot(normed1_all.T, d_value, preferred_element_type=jnp.float32)
    total_term = jnp.dot(d_query, w_query.T, preferred_element_type=jnp.float32)
    total_term = total_term + jnp.dot(d_key, w_key.T, preferred_element_type=jnp.float32)
    d_norm1 = ring_scatter(
        total_term + jnp.dot(d_value, w_value.T, preferred_element_type=jnp.float32), "mp"
    )
    gain1_part = jnp.sum(d_norm1 * x_rows * inverse1, axis=0)
    input_grad = d_resid + norm_backward(x_rows, inverse1, norm1_gain, d_norm1)
    gate_full = lax.dynamic_update_slice_in_dim(
        jnp.zeros((heads_here * mp_size,), jnp.float32),
        gate_part,
        lax.axis_index("mp") * heads_here,
        0,
    )
    gains = tree_sum(tree_sum(jnp.concatenate([gain1_part, gain2_part, gate_full]), "mp"), "dp")
    gain1_sum, gain2_sum, gate_sum = jnp.split(
        gains, [gain1_part.shape[0], gain1_part.shape[0] + gain2_part.shape[0]]
    )
    qkv_sum = over_dp(jnp.concatenate([grad_query, grad_key, grad_value], axis=1), 0)
    query_sum, key_sum, value_sum = jnp.split(qkv_sum, 3, axis=1)
    return (
        output,
        input_grad,
        gain1_sum,
        query_sum,
        key_sum,
        value_sum,
        out_sum,
        gate_sum,
        gain2_sum,
        gate_w_sum,
        up_sum,
        down_sum,
    )


def solution(mesh):
    return jax.shard_map(
        local,
        mesh=mesh,
        in_specs=(
            P(("dp", "mp"), None),
            P(),
            P(None, "mp"),
            P(None, "mp"),
            P(None, "mp"),
            P("mp", None),
            P("mp"),
            P(),
            P(None, "mp"),
            P(None, "mp"),
            P("mp", None),
            P(),
            P(("dp", "mp"), None),
        ),
        out_specs=(
            P(("dp", "mp"), None),
            P(("dp", "mp"), None),
            P(),
            P("dp", "mp"),
            P("dp", "mp"),
            P("dp", "mp"),
            P("mp", "dp"),
            P(),
            P(),
            P("dp", "mp"),
            P("dp", "mp"),
            P("mp", "dp"),
        ),
        check_vma=False,
    )
```

```python
import functools
import math

import jax
import jax.numpy as jnp
from jax import lax
from jax.experimental import pallas as pl
from jax.experimental.pallas import tpu as pltpu
from jax.sharding import PartitionSpec as P


SEG = 2048


eps_norm = 1e-05
highest = lax.Precision.HIGHEST


def gather_states(state, axis, kind):
    flag, memory, norm = state
    heads, size = norm.shape
    packed = jnp.concatenate(
        [memory.reshape(heads * size, size), norm, jnp.broadcast_to(flag.reshape(1, 1), (1, size))],
        axis=0,
    )
    everything = lax.all_gather(packed.astype(kind), axis).astype(jnp.float32)
    return (
        everything[:, heads * size + heads, 0],
        everything[:, : heads * size].reshape((-1, heads, size, size)),
        everything[:, heads * size : heads * size + heads],
    )


def combine_selected(weights, states):
    _, memory, norm = states
    return (
        jnp.sum(weights[:, None, None, None] * memory, axis=0),
        jnp.sum(weights[:, None, None] * norm, axis=0),
    )


def carried_in(value, axis):
    size, place = (lax.axis_size(axis), lax.axis_index(axis))
    states = gather_states(value, axis, jnp.float32)
    flags = states[0]
    k = jnp.arange(size)[:, None]
    j = jnp.arange(size)[None, :]
    factors = jnp.where((j > k) & (j < place), flags[None, :], 1.0)
    weights = jnp.where(jnp.arange(size) < place, jnp.prod(factors, axis=1), 0.0)
    return combine_selected(weights, states)


def prefix(value, axis):
    size, place = (lax.axis_size(axis), lax.axis_index(axis))
    states = gather_states(value, axis, jnp.bfloat16)
    flags = states[0]
    k = jnp.arange(size)[:, None]
    j = jnp.arange(size)[None, :]
    factors = jnp.where((j > place) & (j < k), flags[None, :], 1.0)
    weights = jnp.where(jnp.arange(size) > place, jnp.prod(factors, axis=1), 0.0)
    return combine_selected(weights, states)


def tree_sum(value, axis):
    n = lax.axis_size(axis)
    step = 1
    while step < n:
        value = value + lax.ppermute(value, axis, [(j, j ^ step) for j in range(n)])
        step *= 2
    return value


def ring_pairs(n, step):
    return [(j, (j + step) % n) for j in range(n)]


def ring_gather(rows, axis, compute):
    n, place = lax.axis_size(axis), lax.axis_index(axis)
    count = rows.shape[0]
    half = count // 2
    own = compute(rows)
    outs = [
        lax.dynamic_update_slice_in_dim(
            jnp.zeros((n * count,) + part.shape[1:], part.dtype), part, place * count, 0
        )
        for part in own
    ]
    ahead, behind = rows[:half], rows[half:]
    for step in range(1, n):
        ahead = lax.ppermute(ahead, axis, ring_pairs(n, 1))
        behind = lax.ppermute(behind, axis, ring_pairs(n, -1))
        for got, start in (
            (compute(ahead), ((place - step) % n) * count),
            (compute(behind), ((place + step) % n) * count + half),
        ):
            outs = [
                lax.dynamic_update_slice_in_dim(out, part, start, 0)
                for out, part in zip(outs, got)
            ]
    return outs


def ring_scatter(partial, axis, kind=jnp.bfloat16):
    n, place = lax.axis_size(axis), lax.axis_index(axis)
    count = partial.count // n
    half = count // 2

    def chunk(owner, start):
        return partial(owner * count + start, half).astype(jnp.float32)

    ahead = chunk((place - 1) % n, 0)
    behind = chunk((place + 1) % n, half)
    for step in range(1, n):
        ahead = lax.ppermute(ahead.astype(kind), axis, ring_pairs(n, 1))
        behind = lax.ppermute(behind.astype(kind), axis, ring_pairs(n, -1))
        ahead = ahead.astype(jnp.float32) + chunk((place - 1 - step) % n, 0)
        behind = behind.astype(jnp.float32) + chunk((place + 1 + step) % n, half)
    return jnp.concatenate([ahead, behind], axis=0)


class Rows:
    def __init__(self, terms):
        self.terms = terms
        self.count = terms[0][0].shape[0]

    def __call__(self, first, count):
        total = None
        for lhs, rhs in self.terms:
            part = jnp.dot(
                lax.dynamic_slice_in_dim(lhs, first, count, 0), rhs, preferred_element_type=jnp.float32
            )
            total = part if total is None else total + part
        return total


class Given:
    def __init__(self, value):
        self.value = value
        self.count = value.shape[0]

    def __call__(self, first, count):
        return lax.dynamic_slice_in_dim(self.value, first, count, 0)


def inverse_rms(values):
    return lax.rsqrt(jnp.mean(values * values, axis=-1, keepdims=True) + eps_norm)


def norm_backward(values, inverse, gain, upstream):
    scaled = upstream * gain
    inner = jnp.mean(values * scaled, axis=-1, keepdims=True)
    return inverse * scaled - values * inverse * inverse * inverse * inner


def feature(values):
    return jnp.where(values > 0, values + 1.0, jnp.exp(jnp.minimum(values, 0.0)))


def feature_slope(values):
    return jnp.where(values > 0, 1.0, jnp.exp(jnp.minimum(values, 0.0)))


def link_states(earlier, later):
    return (
        earlier[0] * later[0],
        later[0] * earlier[1] + later[1],
        later[0] * earlier[2] + later[2],
    )


def fold_states(state, item):
    return (link_states(state, item), None)


def document_ids(doc_lengths, first, count):
    bounds = jnp.cumsum(doc_lengths)
    position = first + jnp.arange(count, dtype=jnp.int32)
    before = jnp.sum((bounds[None, :] <= position[:, None]).astype(jnp.int32), axis=1)
    return jnp.where(position < bounds[-1], before, doc_lengths.shape[0] + position)


NEG = -1e30
BQ = 256


def _mask(qi, docq, dock, seg):
    row = (qi * BQ) % seg + lax.broadcasted_iota(jnp.int32, (BQ, seg), 0)
    col = lax.broadcasted_iota(jnp.int32, (BQ, seg), 1)
    return (col <= row) & (docq == dock)


def _fwd_kernel(scale, seg, q_ref, k_ref, v_ref, docq_ref, dock_ref, o_ref, lse_ref):
    qi = pl.program_id(1)
    q = q_ref[0]
    k = k_ref[0]
    v = v_ref[0]
    s = lax.dot_general(q, k, (((1,), (1,)), ((), ())), preferred_element_type=jnp.float32)
    allowed = _mask(qi, docq_ref[...], dock_ref[...], seg)
    s = jnp.where(allowed, s * scale, NEG)
    m = jnp.max(s, axis=1, keepdims=True)
    e = jnp.exp(s - m)
    l = jnp.sum(e, axis=1, keepdims=True)
    p = (e / l).astype(jnp.bfloat16)
    o_ref[0] = jnp.dot(p, v, preferred_element_type=jnp.float32)
    lse_ref[0] = m + jnp.log(l)


def _bwd_kernel(scale, seg, q_ref, k_ref, v_ref, do_ref, lse_ref, docq_ref, dock_ref,
                dq_ref, dk_ref, dv_ref):
    qi = pl.program_id(1)

    @pl.when((qi * BQ) % seg == 0)
    def _():
        dk_ref[...] = jnp.zeros_like(dk_ref)
        dv_ref[...] = jnp.zeros_like(dv_ref)

    q = q_ref[0]
    k = k_ref[0]
    v = v_ref[0]
    do = do_ref[0]
    s = lax.dot_general(q, k, (((1,), (1,)), ((), ())), preferred_element_type=jnp.float32)
    allowed = _mask(qi, docq_ref[...], dock_ref[...], seg)
    s = jnp.where(allowed, s * scale, NEG)
    p = jnp.exp(s - lse_ref[0])
    dp = lax.dot_general(do, v, (((1,), (1,)), ((), ())), preferred_element_type=jnp.float32)
    delta = jnp.sum(p * dp, axis=1, keepdims=True)
    ds = (p * (dp - delta) * scale).astype(jnp.bfloat16)
    dq_ref[0] = jnp.dot(ds, k, preferred_element_type=jnp.float32)
    dk_ref[0] += lax.dot_general(ds, q, (((0,), (0,)), ((), ())), preferred_element_type=jnp.float32)
    dv_ref[0] += lax.dot_general(p.astype(jnp.bfloat16), do, (((0,), (0,)), ((), ())),
                                 preferred_element_type=jnp.float32)


def attention_fwd(q, k, v, doc, scale):
    H, T, d = q.shape
    seg = min(SEG, T)
    nq = T // BQ
    docq = doc.reshape(T, 1)
    dock = doc.reshape(1, T)
    qspec = pl.BlockSpec((1, BQ, d), lambda h, i: (h, i, 0))
    kspec = pl.BlockSpec((1, seg, d), lambda h, i: (h, i * BQ // seg, 0))
    flops = 4 * H * T * seg * d
    return pl.pallas_call(
        functools.partial(_fwd_kernel, scale, seg),
        grid=(H, nq),
        in_specs=[qspec, kspec, kspec,
                  pl.BlockSpec((BQ, 1), lambda h, i: (i, 0)),
                  pl.BlockSpec((1, seg), lambda h, i: (0, i * BQ // seg))],
        out_specs=[pl.BlockSpec((1, BQ, d), lambda h, i: (h, i, 0)),
                   pl.BlockSpec((1, BQ, 1), lambda h, i: (h, i, 0))],
        out_shape=[jax.ShapeDtypeStruct((H, T, d), jnp.float32),
                   jax.ShapeDtypeStruct((H, T, 1), jnp.float32)],
        compiler_params=pltpu.CompilerParams(dimension_semantics=("arbitrary", "arbitrary")),
        cost_estimate=pl.CostEstimate(flops=flops, transcendentals=H * T * seg,
                                      bytes_accessed=H * T * d * 10),
    )(q, k, v, docq, dock)


def attention_bwd(q, k, v, do, lse, doc, scale):
    H, T, d = q.shape
    seg = min(SEG, T)
    nq = T // BQ
    docq = doc.reshape(T, 1)
    dock = doc.reshape(1, T)
    qspec = pl.BlockSpec((1, BQ, d), lambda h, i: (h, i, 0))
    kspec = pl.BlockSpec((1, seg, d), lambda h, i: (h, i * BQ // seg, 0))
    flops = 10 * H * T * seg * d
    return pl.pallas_call(
        functools.partial(_bwd_kernel, scale, seg),
        grid=(H, nq),
        in_specs=[qspec, kspec, kspec, qspec,
                  pl.BlockSpec((1, BQ, 1), lambda h, i: (h, i, 0)),
                  pl.BlockSpec((BQ, 1), lambda h, i: (i, 0)),
                  pl.BlockSpec((1, seg), lambda h, i: (0, i * BQ // seg))],
        out_specs=[qspec, kspec, kspec],
        out_shape=[jax.ShapeDtypeStruct((H, T, d), jnp.float32)] * 3,
        compiler_params=pltpu.CompilerParams(dimension_semantics=("arbitrary", "arbitrary")),
        cost_estimate=pl.CostEstimate(flops=flops, transcendentals=H * T * seg,
                                      bytes_accessed=H * T * d * 24),
    )(q, k, v, do, lse, docq, dock)


def local(
    tokens,
    norm1_gain,
    w_query,
    w_key,
    w_value,
    w_out,
    gate_logit,
    norm2_gain,
    w_gate,
    w_up,
    w_down,
    doc_lengths,
    out_grad,
):
    heads_here = gate_logit.shape[0]
    head_size = w_query.shape[1] // heads_here
    local_rows = tokens.shape[0]
    mp_size = lax.axis_size("mp")
    dp_size = lax.axis_size("dp")
    group_rows = local_rows * mp_size
    seg_count = group_rows // SEG
    score_scale = 1.0 / math.sqrt(head_size)
    group_first = lax.axis_index("dp") * group_rows
    shifted_ids = document_ids(doc_lengths, group_first - 1, group_rows + 1)
    doc_index = shifted_ids[1:]
    before_doc = jnp.where(group_first > 0, shifted_ids[0], -1)
    seg_docs = doc_index.reshape(seg_count, SEG)
    seg_first = seg_docs[:, 0]
    seg_last = seg_docs[:, -1]
    prev_last = jnp.concatenate([before_doc[None], seg_last[:-1]])
    cont_flag = jnp.where(seg_first == prev_last, 1.0, 0.0).astype(jnp.float32)
    keep_flag = jnp.where(seg_last == prev_last, 1.0, 0.0).astype(jnp.float32)
    read_mask = jnp.where(seg_docs == seg_first[:, None], 1.0, 0.0).astype(jnp.float32)
    write_mask = jnp.where(seg_docs == seg_last[:, None], 1.0, 0.0).astype(jnp.float32)
    width = w_out.shape[1]

    def over_dp(grad, dim):
        return lax.psum_scatter(
            grad.astype(jnp.bfloat16), "dp", scatter_dimension=dim, tiled=True
        ).astype(jnp.float32)

    def to_heads(rows):
        return rows.reshape(group_rows, heads_here, head_size).transpose(1, 0, 2)

    def from_heads(heads):
        return heads.transpose(1, 0, 2).reshape(group_rows, heads_here * head_size)

    seg_shape = (heads_here, seg_count, SEG, head_size)
    piece = width // dp_size
    w_out_piece = lax.dynamic_slice_in_dim(w_out, lax.axis_index("dp") * piece, piece, axis=1)
    w_out_full = lax.all_gather(
        lax.all_gather(w_out_piece, "mp", axis=0, tiled=True), "dp", axis=1, tiled=True
    )
    x_rows = tokens.astype(jnp.float32)
    inverse1 = inverse_rms(x_rows)
    normed1 = (x_rows * inverse1 * norm1_gain).astype(jnp.bfloat16)

    def project_qkv(rows):
        return (rows,) + tuple(
            jnp.dot(rows, weight, preferred_element_type=jnp.float32).astype(jnp.bfloat16)
            for weight in (w_query, w_key, w_value)
        )

    normed1_all, query_rows, key_rows, value_rows = ring_gather(normed1, "mp", project_qkv)
    query_h, key_h, value_h = (to_heads(a) for a in (query_rows, key_rows, value_rows))
    grad_rows, query_h = lax.optimization_barrier((out_grad, query_h))
    dot_out, log_sums = attention_fwd(query_h, key_h, value_h, doc_index, score_scale)
    query_f = query_h.astype(jnp.float32).reshape(seg_shape)
    key_f = key_h.astype(jnp.float32).reshape(seg_shape)
    value_f = value_h.astype(jnp.float32).reshape(seg_shape)
    sig_q = feature(query_f)
    sig_k = feature(key_f)
    updates = jnp.einsum("st,hstd,hste->shde", write_mask, sig_k, value_f, precision=highest)
    norm_updates = jnp.einsum("st,hstd->shd", write_mask, sig_k, precision=highest)
    start_state = (
        jnp.ones((1,), jnp.float32),
        jnp.zeros(updates.shape[1:], jnp.float32),
        jnp.zeros(norm_updates.shape[1:], jnp.float32),
    )
    summary, _ = lax.scan(fold_states, start_state, (keep_flag[:, None], updates, norm_updates))
    memory_in, norm_in = carried_in(summary, "dp")

    def carry_forward(state, item):
        flag, read_flag, update, norm_update = item
        memory, norm_sum = state
        return (
            (flag * memory + update, flag * norm_sum + norm_update),
            (read_flag * memory, read_flag * norm_sum),
        )

    _, (read_mem, read_norm) = lax.scan(
        carry_forward, (memory_in, norm_in), (keep_flag, cont_flag, updates, norm_updates)
    )
    numer = jnp.einsum("hstd,shde->hste", sig_q, read_mem, precision=highest)
    denom_raw = jnp.einsum("hstd,shd->hst", sig_q, read_norm, precision=highest)
    denom = jnp.maximum(denom_raw, 1.0)
    mem_out = (read_mask[None, :, :, None] * numer / denom[..., None]).reshape(dot_out.shape)
    gate_vec = jax.nn.sigmoid(gate_logit)
    gate = gate_vec[:, None, None]
    mixed_cols = from_heads(gate * mem_out + (1.0 - gate) * dot_out).astype(jnp.bfloat16)
    mixed = lax.all_to_all(mixed_cols, "mp", 0, 1, tiled=True)
    attn_sum = jnp.dot(mixed, w_out_full, preferred_element_type=jnp.float32)
    resid = x_rows + attn_sum
    inverse2 = inverse_rms(resid)
    normed2 = (resid * inverse2 * norm2_gain).astype(jnp.bfloat16)

    def project_ffn(rows):
        return (rows,) + tuple(
            jnp.dot(rows, weight, preferred_element_type=jnp.float32).astype(jnp.bfloat16)
            for weight in (w_gate, w_up)
        )

    normed2_all, gate_pre, up_pre = ring_gather(normed2, "mp", project_ffn)
    gate_f = gate_pre.astype(jnp.float32)
    up_f = up_pre.astype(jnp.float32)
    sig_gate = jax.nn.sigmoid(gate_f)
    act = (gate_f * sig_gate * up_f).astype(jnp.bfloat16)
    mlp_part = jnp.dot(act, w_down, preferred_element_type=jnp.float32)
    (grad_rows_all,) = ring_gather(grad_rows, "mp", lambda rows: (rows,))
    d_act = lax.optimization_barrier(
        jnp.dot(grad_rows_all, w_down.T, preferred_element_type=jnp.float32)
    )
    d_gate = (d_act * up_f * sig_gate * (1.0 + gate_f * (1.0 - sig_gate))).astype(jnp.bfloat16)
    d_up = (d_act * gate_f * sig_gate).astype(jnp.bfloat16)
    normed2_all, act, d_gate, d_up = lax.optimization_barrier((normed2_all, act, d_gate, d_up))
    grad_gate = jnp.dot(normed2_all.T, d_gate, preferred_element_type=jnp.float32)
    grad_up = jnp.dot(normed2_all.T, d_up, preferred_element_type=jnp.float32)
    grad_down = jnp.dot(act.T, grad_rows_all, preferred_element_type=jnp.float32)
    d_norm2 = ring_scatter(Rows(((d_gate, w_gate.T), (d_up, w_up.T))), "mp")
    gate_w_sum = over_dp(grad_gate, 0)
    up_sum = over_dp(grad_up, 0)
    down_sum = over_dp(grad_down, 1)
    gain2_part = jnp.sum(d_norm2 * resid * inverse2, axis=0)
    d_resid = out_grad.astype(jnp.float32) + norm_backward(resid, inverse2, norm2_gain, d_norm2)
    d_resid_low = d_resid.astype(jnp.bfloat16)
    grad_out = jnp.dot(mixed.T, d_resid_low, preferred_element_type=jnp.float32)
    out_sum = lax.psum_scatter(
        over_dp(grad_out, 1).astype(jnp.bfloat16), "mp", scatter_dimension=0, tiled=True
    ).astype(jnp.float32)
    d_mixed_rows = jnp.dot(d_resid_low, w_out_full.T, preferred_element_type=jnp.float32)
    d_mixed = to_heads(
        lax.all_to_all(d_mixed_rows.astype(jnp.bfloat16), "mp", 1, 0, tiled=True)
    ).astype(jnp.float32)
    mlp_part, d_mixed, gate_w_sum, up_sum = lax.optimization_barrier(
        (mlp_part, d_mixed, gate_w_sum, up_sum)
    )
    output = (resid + ring_scatter(Given(mlp_part), "mp")).astype(jnp.bfloat16)
    gate_part = jnp.sum(d_mixed * (mem_out - dot_out), axis=(1, 2)) * gate_vec * (1.0 - gate_vec)
    d_dot = ((1.0 - gate) * d_mixed).astype(jnp.bfloat16)
    d_mem = (gate * d_mixed).reshape(seg_shape)
    dq_dot, dk_dot, dv_dot = attention_bwd(
        query_h, key_h, value_h, d_dot, log_sums, doc_index, score_scale
    )
    dq_dot, down_sum, out_sum = lax.optimization_barrier((dq_dot, down_sum, out_sum))
    d_numer = read_mask[None, :, :, None] * d_mem / denom[..., None]
    d_denom = -jnp.sum(d_numer * numer, axis=-1) / denom * jnp.where(denom_raw > 1.0, 1.0, 0.0)
    d_sig_q = (
        jnp.einsum("hste,shde->hstd", d_numer, read_mem, precision=highest)
        + d_denom[..., None] * read_norm.transpose(1, 0, 2)[:, :, None]
    )
    d_read_mem = jnp.einsum("hstd,hste->shde", sig_q, d_numer, precision=highest)
    d_read_norm = jnp.einsum("hst,hstd->shd", d_denom, sig_q, precision=highest)
    back_mem = cont_flag[:, None, None, None] * d_read_mem
    back_norm = cont_flag[:, None, None] * d_read_norm
    back_summary, _ = lax.scan(
        fold_states, start_state, (keep_flag[:, None], back_mem, back_norm), reverse=True
    )
    grad_in, grad_norm_in = prefix(back_summary, "dp")

    def carry_back(state, item):
        flag, mem_read, norm_read = item
        grad_memory, grad_norm = state
        return (
            (flag * grad_memory + mem_read, flag * grad_norm + norm_read),
            (grad_memory, grad_norm),
        )

    _, (d_carried, d_carried_norm) = lax.scan(
        carry_back, (grad_in, grad_norm_in), (keep_flag, back_mem, back_norm), reverse=True
    )
    write4 = write_mask[None, :, :, None]
    d_sig_k = write4 * (
        jnp.einsum("hste,shde->hstd", value_f, d_carried, precision=highest)
        + d_carried_norm.transpose(1, 0, 2)[:, :, None]
    )
    d_val_mem = write4 * jnp.einsum("hstd,shde->hste", sig_k, d_carried, precision=highest)
    d_query = from_heads(
        dq_dot + (d_sig_q * feature_slope(query_f)).reshape(dq_dot.shape)
    ).astype(jnp.bfloat16)
    d_key = from_heads(
        dk_dot + (d_sig_k * feature_slope(key_f)).reshape(dk_dot.shape)
    ).astype(jnp.bfloat16)
    d_value = from_heads(dv_dot + d_val_mem.reshape(dv_dot.shape)).astype(jnp.bfloat16)
    grad_query = jnp.dot(normed1_all.T, d_query, preferred_element_type=jnp.float32)
    grad_key = jnp.dot(normed1_all.T, d_key, preferred_element_type=jnp.float32)
    grad_value = jnp.dot(normed1_all.T, d_value, preferred_element_type=jnp.float32)
    qkv_grads = jnp.concatenate([grad_query, grad_key, grad_value], axis=1).astype(jnp.bfloat16)
    qkv_sum = over_dp(qkv_grads, 0)
    d_norm1 = ring_scatter(
        Rows(((d_query, w_query.T), (d_key, w_key.T), (d_value, w_value.T))), "mp"
    )
    gain1_part = jnp.sum(d_norm1 * x_rows * inverse1, axis=0)
    input_grad = d_resid + norm_backward(x_rows, inverse1, norm1_gain, d_norm1)
    gate_full = lax.dynamic_update_slice_in_dim(
        jnp.zeros((heads_here * mp_size,), jnp.float32),
        gate_part,
        lax.axis_index("mp") * heads_here,
        0,
    )
    gains = tree_sum(tree_sum(jnp.concatenate([gain1_part, gain2_part, gate_full]), "mp"), "dp")
    gain1_sum, gain2_sum, gate_sum = jnp.split(
        gains, [gain1_part.shape[0], gain1_part.shape[0] + gain2_part.shape[0]]
    )
    query_sum, key_sum, value_sum = jnp.split(qkv_sum, 3, axis=1)
    return (
        output,
        input_grad,
        gain1_sum,
        query_sum,
        key_sum,
        value_sum,
        out_sum,
        gate_sum,
        gain2_sum,
        gate_w_sum,
        up_sum,
        down_sum,
    )


def solution(mesh):
    return jax.shard_map(
        local,
        mesh=mesh,
        in_specs=(
            P(("dp", "mp"), None),
            P(),
            P(None, "mp"),
            P(None, "mp"),
            P(None, "mp"),
            P("mp", None),
            P("mp"),
            P(),
            P(None, "mp"),
            P(None, "mp"),
            P("mp", None),
            P(),
            P(("dp", "mp"), None),
        ),
        out_specs=(
            P(("dp", "mp"), None),
            P(("dp", "mp"), None),
            P(),
            P("dp", "mp"),
            P("dp", "mp"),
            P("dp", "mp"),
            P("mp", "dp"),
            P(),
            P(),
            P("dp", "mp"),
            P("dp", "mp"),
            P("mp", "dp"),
        ),
        check_vma=False,
    )
```

```python
import functools
import math

import jax
import jax.numpy as jnp
from jax import lax
from jax.experimental import pallas as pl
from jax.experimental.pallas import tpu as pltpu
from jax.sharding import PartitionSpec as P


SEG = 2048


eps_norm = 1e-05
highest = lax.Precision.HIGHEST


def gather_states(state, axis, kind):
    flag, memory, norm = state
    heads, size = norm.shape
    packed = jnp.concatenate(
        [memory.reshape(heads * size, size), norm, jnp.broadcast_to(flag.reshape(1, 1), (1, size))],
        axis=0,
    )
    everything = lax.all_gather(packed.astype(kind), axis).astype(jnp.float32)
    return (
        everything[:, heads * size + heads, 0],
        everything[:, : heads * size].reshape((-1, heads, size, size)),
        everything[:, heads * size : heads * size + heads],
    )


def combine_selected(weights, states):
    _, memory, norm = states
    return (
        jnp.sum(weights[:, None, None, None] * memory, axis=0),
        jnp.sum(weights[:, None, None] * norm, axis=0),
    )


def carried_in(value, axis):
    size, place = (lax.axis_size(axis), lax.axis_index(axis))
    states = gather_states(value, axis, jnp.float32)
    flags = states[0]
    k = jnp.arange(size)[:, None]
    j = jnp.arange(size)[None, :]
    factors = jnp.where((j > k) & (j < place), flags[None, :], 1.0)
    weights = jnp.where(jnp.arange(size) < place, jnp.prod(factors, axis=1), 0.0)
    return combine_selected(weights, states)


def prefix(value, axis):
    size, place = (lax.axis_size(axis), lax.axis_index(axis))
    states = gather_states(value, axis, jnp.bfloat16)
    flags = states[0]
    k = jnp.arange(size)[:, None]
    j = jnp.arange(size)[None, :]
    factors = jnp.where((j > place) & (j < k), flags[None, :], 1.0)
    weights = jnp.where(jnp.arange(size) > place, jnp.prod(factors, axis=1), 0.0)
    return combine_selected(weights, states)


def tree_sum(value, axis):
    n = lax.axis_size(axis)
    step = 1
    while step < n:
        value = value + lax.ppermute(value, axis, [(j, j ^ step) for j in range(n)])
        step *= 2
    return value


def ring_pairs(n, step):
    return [(j, (j + step) % n) for j in range(n)]


def ring_gather(rows, axis, compute):
    n, place = lax.axis_size(axis), lax.axis_index(axis)
    count = rows.shape[0]
    half = count // 2
    own = compute(rows)
    outs = [
        lax.dynamic_update_slice_in_dim(
            jnp.zeros((n * count,) + part.shape[1:], part.dtype), part, place * count, 0
        )
        for part in own
    ]
    ahead, behind = rows[:half], rows[half:]
    for step in range(1, n):
        ahead = lax.ppermute(ahead, axis, ring_pairs(n, 1))
        behind = lax.ppermute(behind, axis, ring_pairs(n, -1))
        for got, start in (
            (compute(ahead), ((place - step) % n) * count),
            (compute(behind), ((place + step) % n) * count + half),
        ):
            outs = [
                lax.dynamic_update_slice_in_dim(out, part, start, 0)
                for out, part in zip(outs, got)
            ]
    return outs


def ring_scatter(partial, axis, kind=jnp.bfloat16):
    n, place = lax.axis_size(axis), lax.axis_index(axis)
    count = partial.count // n
    half = count // 2

    def chunk(owner, start):
        return partial(owner * count + start, half).astype(jnp.float32)

    ahead = chunk((place - 1) % n, 0)
    behind = chunk((place + 1) % n, half)
    for step in range(1, n):
        ahead = lax.ppermute(ahead.astype(kind), axis, ring_pairs(n, 1))
        behind = lax.ppermute(behind.astype(kind), axis, ring_pairs(n, -1))
        ahead = ahead.astype(jnp.float32) + chunk((place - 1 - step) % n, 0)
        behind = behind.astype(jnp.float32) + chunk((place + 1 + step) % n, half)
    return jnp.concatenate([ahead, behind], axis=0)


class Rows:
    def __init__(self, terms):
        self.terms = terms
        self.count = terms[0][0].shape[0]

    def __call__(self, first, count):
        total = None
        for lhs, rhs in self.terms:
            part = jnp.dot(
                lax.dynamic_slice_in_dim(lhs, first, count, 0), rhs, preferred_element_type=jnp.float32
            )
            total = part if total is None else total + part
        return total


class Given:
    def __init__(self, value):
        self.value = value
        self.count = value.shape[0]

    def __call__(self, first, count):
        return lax.dynamic_slice_in_dim(self.value, first, count, 0)


def inverse_rms(values):
    return lax.rsqrt(jnp.mean(values * values, axis=-1, keepdims=True) + eps_norm)


def norm_backward(values, inverse, gain, upstream):
    scaled = upstream * gain
    inner = jnp.mean(values * scaled, axis=-1, keepdims=True)
    return inverse * scaled - values * inverse * inverse * inverse * inner


def feature(values):
    return jnp.where(values > 0, values + 1.0, jnp.exp(jnp.minimum(values, 0.0)))


def feature_slope(values):
    return jnp.where(values > 0, 1.0, jnp.exp(jnp.minimum(values, 0.0)))


def link_states(earlier, later):
    return (
        earlier[0] * later[0],
        later[0] * earlier[1] + later[1],
        later[0] * earlier[2] + later[2],
    )


def fold_states(state, item):
    return (link_states(state, item), None)


def document_ids(doc_lengths, first, count):
    bounds = jnp.cumsum(doc_lengths)
    position = first + jnp.arange(count, dtype=jnp.int32)
    before = jnp.sum((bounds[None, :] <= position[:, None]).astype(jnp.int32), axis=1)
    return jnp.where(position < bounds[-1], before, doc_lengths.shape[0] + position)


NEG = -1e30
BQ = 256


def _mask(qi, docq, dock, seg, width):
    row = (qi * BQ) % seg + lax.broadcasted_iota(jnp.int32, (BQ, width), 0)
    col = lax.broadcasted_iota(jnp.int32, (BQ, width), 1)
    return (col <= row) & (docq == dock)


LEVEL = 256


def _levels(qi, seg, body):
    local = (qi * BQ) % seg
    need = local + BQ
    for lvl in range(seg // LEVEL):
        width = (lvl + 1) * LEVEL
        low = lvl * LEVEL

        @pl.when((need > low) & (need <= width))
        def _():
            body(width)


def _fwd_kernel(scale, seg, q_ref, k_ref, v_ref, docq_ref, dock_ref, o_ref, lse_ref):
    qi = pl.program_id(1)

    def body(width):
        q = q_ref[0]
        k = k_ref[0, :width]
        v = v_ref[0, :width]
        s = lax.dot_general(q, k, (((1,), (1,)), ((), ())), preferred_element_type=jnp.float32)
        allowed = _mask(qi, docq_ref[...], dock_ref[:, :width], seg, width)
        s = jnp.where(allowed, s * scale, NEG)
        m = jnp.max(s, axis=1, keepdims=True)
        e = jnp.exp(s - m)
        l = jnp.sum(e, axis=1, keepdims=True)
        p = (e / l).astype(jnp.bfloat16)
        o_ref[0] = jnp.dot(p, v, preferred_element_type=jnp.float32)
        lse_ref[0] = m + jnp.log(l)

    _levels(qi, seg, body)


def _bwd_kernel(scale, seg, q_ref, k_ref, v_ref, do_ref, lse_ref, docq_ref, dock_ref,
                dq_ref, dk_ref, dv_ref):
    qi = pl.program_id(1)

    @pl.when((qi * BQ) % seg == 0)
    def _():
        dk_ref[...] = jnp.zeros_like(dk_ref)
        dv_ref[...] = jnp.zeros_like(dv_ref)

    def body(width):
        q = q_ref[0]
        k = k_ref[0, :width]
        v = v_ref[0, :width]
        do = do_ref[0]
        s = lax.dot_general(q, k, (((1,), (1,)), ((), ())), preferred_element_type=jnp.float32)
        allowed = _mask(qi, docq_ref[...], dock_ref[:, :width], seg, width)
        s = jnp.where(allowed, s * scale, NEG)
        p = jnp.exp(s - lse_ref[0])
        dp = lax.dot_general(do, v, (((1,), (1,)), ((), ())), preferred_element_type=jnp.float32)
        delta = jnp.sum(p * dp, axis=1, keepdims=True)
        ds = (p * (dp - delta) * scale).astype(jnp.bfloat16)
        dq_ref[0] = jnp.dot(ds, k, preferred_element_type=jnp.float32)
        dk_ref[0, :width] += lax.dot_general(ds, q, (((0,), (0,)), ((), ())),
                                             preferred_element_type=jnp.float32)
        dv_ref[0, :width] += lax.dot_general(p.astype(jnp.bfloat16), do, (((0,), (0,)), ((), ())),
                                             preferred_element_type=jnp.float32)

    _levels(qi, seg, body)


def attention_fwd(q, k, v, doc, scale):
    H, T, d = q.shape
    seg = min(SEG, T)
    nq = T // BQ
    docq = doc.reshape(T, 1)
    dock = doc.reshape(1, T)
    qspec = pl.BlockSpec((1, BQ, d), lambda h, i: (h, i, 0))
    kspec = pl.BlockSpec((1, seg, d), lambda h, i: (h, i * BQ // seg, 0))
    flops = 4 * H * T * seg * d
    return pl.pallas_call(
        functools.partial(_fwd_kernel, scale, seg),
        grid=(H, nq),
        in_specs=[qspec, kspec, kspec,
                  pl.BlockSpec((BQ, 1), lambda h, i: (i, 0)),
                  pl.BlockSpec((1, seg), lambda h, i: (0, i * BQ // seg))],
        out_specs=[pl.BlockSpec((1, BQ, d), lambda h, i: (h, i, 0)),
                   pl.BlockSpec((1, BQ, 1), lambda h, i: (h, i, 0))],
        out_shape=[jax.ShapeDtypeStruct((H, T, d), jnp.float32),
                   jax.ShapeDtypeStruct((H, T, 1), jnp.float32)],
        compiler_params=pltpu.CompilerParams(dimension_semantics=("arbitrary", "arbitrary")),
        cost_estimate=pl.CostEstimate(flops=flops, transcendentals=H * T * seg,
                                      bytes_accessed=H * T * d * 10),
    )(q, k, v, docq, dock)


def attention_bwd(q, k, v, do, lse, doc, scale):
    H, T, d = q.shape
    seg = min(SEG, T)
    nq = T // BQ
    docq = doc.reshape(T, 1)
    dock = doc.reshape(1, T)
    qspec = pl.BlockSpec((1, BQ, d), lambda h, i: (h, i, 0))
    kspec = pl.BlockSpec((1, seg, d), lambda h, i: (h, i * BQ // seg, 0))
    flops = 10 * H * T * seg * d
    return pl.pallas_call(
        functools.partial(_bwd_kernel, scale, seg),
        grid=(H, nq),
        in_specs=[qspec, kspec, kspec, qspec,
                  pl.BlockSpec((1, BQ, 1), lambda h, i: (h, i, 0)),
                  pl.BlockSpec((BQ, 1), lambda h, i: (i, 0)),
                  pl.BlockSpec((1, seg), lambda h, i: (0, i * BQ // seg))],
        out_specs=[qspec, kspec, kspec],
        out_shape=[jax.ShapeDtypeStruct((H, T, d), jnp.float32)] * 3,
        compiler_params=pltpu.CompilerParams(dimension_semantics=("arbitrary", "arbitrary")),
        cost_estimate=pl.CostEstimate(flops=flops, transcendentals=H * T * seg,
                                      bytes_accessed=H * T * d * 24),
    )(q, k, v, do, lse, docq, dock)


def local(
    tokens,
    norm1_gain,
    w_query,
    w_key,
    w_value,
    w_out,
    gate_logit,
    norm2_gain,
    w_gate,
    w_up,
    w_down,
    doc_lengths,
    out_grad,
):
    heads_here = gate_logit.shape[0]
    head_size = w_query.shape[1] // heads_here
    local_rows = tokens.shape[0]
    mp_size = lax.axis_size("mp")
    dp_size = lax.axis_size("dp")
    group_rows = local_rows * mp_size
    seg_count = group_rows // SEG
    score_scale = 1.0 / math.sqrt(head_size)
    group_first = lax.axis_index("dp") * group_rows
    shifted_ids = document_ids(doc_lengths, group_first - 1, group_rows + 1)
    doc_index = shifted_ids[1:]
    before_doc = jnp.where(group_first > 0, shifted_ids[0], -1)
    seg_docs = doc_index.reshape(seg_count, SEG)
    seg_first = seg_docs[:, 0]
    seg_last = seg_docs[:, -1]
    prev_last = jnp.concatenate([before_doc[None], seg_last[:-1]])
    cont_flag = jnp.where(seg_first == prev_last, 1.0, 0.0).astype(jnp.float32)
    keep_flag = jnp.where(seg_last == prev_last, 1.0, 0.0).astype(jnp.float32)
    read_mask = jnp.where(seg_docs == seg_first[:, None], 1.0, 0.0).astype(jnp.float32)
    write_mask = jnp.where(seg_docs == seg_last[:, None], 1.0, 0.0).astype(jnp.float32)
    width = w_out.shape[1]

    def over_dp(grad, dim):
        return lax.psum_scatter(
            grad.astype(jnp.bfloat16), "dp", scatter_dimension=dim, tiled=True
        ).astype(jnp.float32)

    def to_heads(rows):
        return rows.reshape(group_rows, heads_here, head_size).transpose(1, 0, 2)

    def from_heads(heads):
        return heads.transpose(1, 0, 2).reshape(group_rows, heads_here * head_size)

    seg_shape = (heads_here, seg_count, SEG, head_size)
    piece = width // dp_size
    w_out_piece = lax.dynamic_slice_in_dim(w_out, lax.axis_index("dp") * piece, piece, axis=1)
    x_rows = tokens.astype(jnp.float32)
    inverse1 = inverse_rms(x_rows)
    normed1 = (x_rows * inverse1 * norm1_gain).astype(jnp.bfloat16)

    def project_qkv(rows):
        return (rows,) + tuple(
            jnp.dot(rows, weight, preferred_element_type=jnp.float32).astype(jnp.bfloat16)
            for weight in (w_query, w_key, w_value)
        )

    normed1_all, query_rows, key_rows, value_rows = ring_gather(normed1, "mp", project_qkv)
    grad_rows, query_rows, w_out_piece = lax.optimization_barrier((out_grad, query_rows, w_out_piece))
    w_out_full = lax.all_gather(
        lax.all_gather(w_out_piece, "mp", axis=0, tiled=True), "dp", axis=1, tiled=True
    )
    query_h, key_h, value_h = (to_heads(a) for a in (query_rows, key_rows, value_rows))
    dot_out, log_sums = attention_fwd(query_h, key_h, value_h, doc_index, score_scale)
    query_f = query_h.astype(jnp.float32).reshape(seg_shape)
    key_f = key_h.astype(jnp.float32).reshape(seg_shape)
    value_f = value_h.astype(jnp.float32).reshape(seg_shape)
    sig_q = feature(query_f)
    sig_k = feature(key_f)
    updates = jnp.einsum("st,hstd,hste->shde", write_mask, sig_k, value_f, precision=highest)
    norm_updates = jnp.einsum("st,hstd->shd", write_mask, sig_k, precision=highest)
    start_state = (
        jnp.ones((1,), jnp.float32),
        jnp.zeros(updates.shape[1:], jnp.float32),
        jnp.zeros(norm_updates.shape[1:], jnp.float32),
    )
    summary, _ = lax.scan(fold_states, start_state, (keep_flag[:, None], updates, norm_updates))
    memory_in, norm_in = carried_in(summary, "dp")

    def carry_forward(state, item):
        flag, read_flag, update, norm_update = item
        memory, norm_sum = state
        return (
            (flag * memory + update, flag * norm_sum + norm_update),
            (read_flag * memory, read_flag * norm_sum),
        )

    _, (read_mem, read_norm) = lax.scan(
        carry_forward, (memory_in, norm_in), (keep_flag, cont_flag, updates, norm_updates)
    )
    numer = jnp.einsum("hstd,shde->hste", sig_q, read_mem, precision=highest)
    denom_raw = jnp.einsum("hstd,shd->hst", sig_q, read_norm, precision=highest)
    denom = jnp.maximum(denom_raw, 1.0)
    mem_out = (read_mask[None, :, :, None] * numer / denom[..., None]).reshape(dot_out.shape)
    gate_vec = jax.nn.sigmoid(gate_logit)
    gate = gate_vec[:, None, None]
    mixed_cols = from_heads(gate * mem_out + (1.0 - gate) * dot_out).astype(jnp.bfloat16)
    mixed = lax.all_to_all(mixed_cols, "mp", 0, 1, tiled=True)
    attn_sum = jnp.dot(mixed, w_out_full, preferred_element_type=jnp.float32)
    resid = x_rows + attn_sum
    inverse2 = inverse_rms(resid)
    normed2 = (resid * inverse2 * norm2_gain).astype(jnp.bfloat16)

    def project_ffn(rows):
        return (rows,) + tuple(
            jnp.dot(rows, weight, preferred_element_type=jnp.float32).astype(jnp.bfloat16)
            for weight in (w_gate, w_up)
        )

    normed2_all, gate_pre, up_pre = ring_gather(normed2, "mp", project_ffn)
    gate_f = gate_pre.astype(jnp.float32)
    up_f = up_pre.astype(jnp.float32)
    sig_gate = jax.nn.sigmoid(gate_f)
    act = (gate_f * sig_gate * up_f).astype(jnp.bfloat16)
    mlp_part = jnp.dot(act, w_down, preferred_element_type=jnp.float32)
    (grad_rows_all,) = ring_gather(grad_rows, "mp", lambda rows: (rows,))
    d_act = lax.optimization_barrier(
        jnp.dot(grad_rows_all, w_down.T, preferred_element_type=jnp.float32)
    )
    d_gate = (d_act * up_f * sig_gate * (1.0 + gate_f * (1.0 - sig_gate))).astype(jnp.bfloat16)
    d_up = (d_act * gate_f * sig_gate).astype(jnp.bfloat16)
    normed2_all, act, d_gate, d_up = lax.optimization_barrier((normed2_all, act, d_gate, d_up))
    grad_gate = jnp.dot(normed2_all.T, d_gate, preferred_element_type=jnp.float32)
    grad_up = jnp.dot(normed2_all.T, d_up, preferred_element_type=jnp.float32)
    grad_down = jnp.dot(act.T, grad_rows_all, preferred_element_type=jnp.float32)
    d_norm2 = ring_scatter(Rows(((d_gate, w_gate.T), (d_up, w_up.T))), "mp")
    gate_w_sum = over_dp(grad_gate, 0)
    up_sum = over_dp(grad_up, 0)
    down_sum = over_dp(grad_down, 1)
    gain2_part = jnp.sum(d_norm2 * resid * inverse2, axis=0)
    d_resid = out_grad.astype(jnp.float32) + norm_backward(resid, inverse2, norm2_gain, d_norm2)
    d_resid_low = d_resid.astype(jnp.bfloat16)
    grad_out = jnp.dot(mixed.T, d_resid_low, preferred_element_type=jnp.float32)
    out_sum = lax.psum_scatter(
        over_dp(grad_out, 1).astype(jnp.bfloat16), "mp", scatter_dimension=0, tiled=True
    ).astype(jnp.float32)
    d_mixed_rows = jnp.dot(d_resid_low, w_out_full.T, preferred_element_type=jnp.float32)
    d_mixed = to_heads(
        lax.all_to_all(d_mixed_rows.astype(jnp.bfloat16), "mp", 1, 0, tiled=True)
    ).astype(jnp.float32)
    mlp_part, d_mixed, gate_w_sum, up_sum = lax.optimization_barrier(
        (mlp_part, d_mixed, gate_w_sum, up_sum)
    )
    output = (resid + ring_scatter(Given(mlp_part), "mp")).astype(jnp.bfloat16)
    gate_part = jnp.sum(d_mixed * (mem_out - dot_out), axis=(1, 2)) * gate_vec * (1.0 - gate_vec)
    d_dot = ((1.0 - gate) * d_mixed).astype(jnp.bfloat16)
    d_mem = (gate * d_mixed).reshape(seg_shape)
    dq_dot, dk_dot, dv_dot = attention_bwd(
        query_h, key_h, value_h, d_dot, log_sums, doc_index, score_scale
    )
    dq_dot, down_sum, out_sum = lax.optimization_barrier((dq_dot, down_sum, out_sum))
    d_numer = read_mask[None, :, :, None] * d_mem / denom[..., None]
    d_denom = -jnp.sum(d_numer * numer, axis=-1) / denom * jnp.where(denom_raw > 1.0, 1.0, 0.0)
    d_sig_q = (
        jnp.einsum("hste,shde->hstd", d_numer, read_mem, precision=highest)
        + d_denom[..., None] * read_norm.transpose(1, 0, 2)[:, :, None]
    )
    d_read_mem = jnp.einsum("hstd,hste->shde", sig_q, d_numer, precision=highest)
    d_read_norm = jnp.einsum("hst,hstd->shd", d_denom, sig_q, precision=highest)
    back_mem = cont_flag[:, None, None, None] * d_read_mem
    back_norm = cont_flag[:, None, None] * d_read_norm
    back_summary, _ = lax.scan(
        fold_states, start_state, (keep_flag[:, None], back_mem, back_norm), reverse=True
    )
    grad_in, grad_norm_in = prefix(back_summary, "dp")

    def carry_back(state, item):
        flag, mem_read, norm_read = item
        grad_memory, grad_norm = state
        return (
            (flag * grad_memory + mem_read, flag * grad_norm + norm_read),
            (grad_memory, grad_norm),
        )

    _, (d_carried, d_carried_norm) = lax.scan(
        carry_back, (grad_in, grad_norm_in), (keep_flag, back_mem, back_norm), reverse=True
    )
    write4 = write_mask[None, :, :, None]
    d_sig_k = write4 * (
        jnp.einsum("hste,shde->hstd", value_f, d_carried, precision=highest)
        + d_carried_norm.transpose(1, 0, 2)[:, :, None]
    )
    d_val_mem = write4 * jnp.einsum("hstd,shde->hste", sig_k, d_carried, precision=highest)
    d_query = from_heads(
        dq_dot + (d_sig_q * feature_slope(query_f)).reshape(dq_dot.shape)
    ).astype(jnp.bfloat16)
    d_key = from_heads(
        dk_dot + (d_sig_k * feature_slope(key_f)).reshape(dk_dot.shape)
    ).astype(jnp.bfloat16)
    d_value = from_heads(dv_dot + d_val_mem.reshape(dv_dot.shape)).astype(jnp.bfloat16)
    grad_query = jnp.dot(normed1_all.T, d_query, preferred_element_type=jnp.float32)
    grad_key = jnp.dot(normed1_all.T, d_key, preferred_element_type=jnp.float32)
    grad_value = jnp.dot(normed1_all.T, d_value, preferred_element_type=jnp.float32)
    qkv_grads = jnp.concatenate([grad_query, grad_key, grad_value], axis=1).astype(jnp.bfloat16)
    qkv_sum = over_dp(qkv_grads, 0)
    d_norm1 = ring_scatter(
        Rows(((d_query, w_query.T), (d_key, w_key.T), (d_value, w_value.T))), "mp"
    )
    gain1_part = jnp.sum(d_norm1 * x_rows * inverse1, axis=0)
    input_grad = d_resid + norm_backward(x_rows, inverse1, norm1_gain, d_norm1)
    gate_full = lax.dynamic_update_slice_in_dim(
        jnp.zeros((heads_here * mp_size,), jnp.float32),
        gate_part,
        lax.axis_index("mp") * heads_here,
        0,
    )
    gains = tree_sum(tree_sum(jnp.concatenate([gain1_part, gain2_part, gate_full]), "mp"), "dp")
    gain1_sum, gain2_sum, gate_sum = jnp.split(
        gains, [gain1_part.shape[0], gain1_part.shape[0] + gain2_part.shape[0]]
    )
    query_sum, key_sum, value_sum = jnp.split(qkv_sum, 3, axis=1)
    return (
        output,
        input_grad,
        gain1_sum,
        query_sum,
        key_sum,
        value_sum,
        out_sum,
        gate_sum,
        gain2_sum,
        gate_w_sum,
        up_sum,
        down_sum,
    )


def solution(mesh):
    return jax.shard_map(
        local,
        mesh=mesh,
        in_specs=(
            P(("dp", "mp"), None),
            P(),
            P(None, "mp"),
            P(None, "mp"),
            P(None, "mp"),
            P("mp", None),
            P("mp"),
            P(),
            P(None, "mp"),
            P(None, "mp"),
            P("mp", None),
            P(),
            P(("dp", "mp"), None),
        ),
        out_specs=(
            P(("dp", "mp"), None),
            P(("dp", "mp"), None),
            P(),
            P("dp", "mp"),
            P("dp", "mp"),
            P("dp", "mp"),
            P("mp", "dp"),
            P(),
            P(),
            P("dp", "mp"),
            P("dp", "mp"),
            P("mp", "dp"),
        ),
        check_vma=False,
    )
```
